32 devices in a mesh: grp: 4 (over y, core), blk: 8 (over z, x).
Axes of the slice: x: 2, y: 2, z: 4, core: 2. Of those that a mesh axis runs over, the one named last changes fastest.
Arguments:
- fields: float32 [14, 512, 4096], P(None, 'grp', 'blk'), may hold values from -6 to 6
- react_rate: float32 [512, 4096], P('grp', 'blk'), may hold values from 0.05 to 0.8
- mix_matrix: float32 [14, 14], replicated, may hold values from -1.5 to 1.5
- activation: float32 [14], replicated, may hold values from 0.3 to 4
- inlet_ids: int32 [4, 4096], P(None, 'blk'), may hold values from 0 to 4095
- inlet_weights: float32 [4, 4096], P(None, 'blk'), may hold values from 0.1 to 0.45
- outlet_ids: int32 [4, 4096], P(None, 'blk'), may hold values from 0 to 4095
- outlet_weights: float32 [4, 4096], P(None, 'blk'), may hold values from 0.1 to 0.45
Outputs:
- advanced: float32 [14, 512, 4096], P(None, 'grp', 'blk')
The draws below stay inside these ranges and needn't reach their ends.
Inputs may be any that keep to these rules, and one draw needn't show every extreme that they name: Every inlet_ids entry names a row of the combustor exit plane. Every outlet_ids entry names a row of the turbine inlet plane.
All inputs are finite; a program needn't handle non-finite values.
Results may differ from the reference program's by a relative error of at most 0.00005.
Values sent between devices are 32-bit elements; how exact they have to be, the bound alone decides.
No kernel may reach another device: no remote copies, remote signals or barrier semaphores. Data moves between devices by JAX's collectives and lax.ppermute only.
A program may use at most 128 MiB of HBM per device.

```python
import math
import jax
import jax.numpy as jnp
from jax import lax

NF = 14
KS = 4
CX = 128
AXIAL = 512
AZ = 4096
N_GRP = 4


def touch_ends(array, rng, least, largest):
    dims = array.shape
    place = [jax.random.randint(jax.random.fold_in(rng, axis), (), 0, dims[axis]) for axis in range(len(dims))]
    array = array.at[tuple(place)].set(least)
    longest = dims.index(max(dims))
    place[longest] = (place[longest] + 1) % dims[longest]
    return array.at[tuple(place)].set(largest)


def block_levels(rng, extent, split, smallest, largest):
    def one(position, shards_of):
        steps = jax.random.uniform(jax.random.fold_in(jax.random.fold_in(rng, 6), position), (shards_of,), jnp.float32, smallest / len(split), largest / len(split))
        return jnp.repeat(jnp.exp(steps), extent[position] // shards_of).reshape((-1,) + (1,) * (len(extent) - position - 1))

    gain = one(*split[0])
    for cut in split[1:]:
        gain = gain * one(*cut)
    return gain


def normal_values(key, dims, scale, bound, cuts=(), held_as=jnp.bfloat16):
    level = block_levels(key, dims, cuts, -0.22, 0.18) if cuts else 1.0
    values = jax.random.normal(key, dims, jnp.float32) * scale * level
    return jnp.minimum(jnp.maximum(values, -bound), bound).astype(held_as)


def setup_inputs(seed: int = 0) -> dict:
    splits = jax.random.split(jax.random.key(seed), 9)
    return {
        "fields": normal_values(splits[0], (NF, AXIAL, AZ), 1.0, 6.0, ((1, 4), (2, 8)), jnp.float32),
        "react_rate": jnp.clip(jnp.exp(math.log(0.8) - 2.7725887 * jax.random.uniform(splits[1], (AXIAL, AZ), jnp.float32) ** block_levels(splits[1], (AXIAL, AZ), ((0, 4), (1, 8)), -0.2, 0.2)), 0.05, 0.8),
        "mix_matrix": normal_values(splits[2], (NF, NF), NF ** -0.5, 1.5, (), jnp.float32),
        "activation": jnp.clip(jnp.exp(jax.random.uniform(splits[3], (NF,), jnp.float32, math.log(0.3), math.log(4.0))), 0.3, 4.0),
        "inlet_ids": touch_ends(jax.random.randint(splits[4], (KS, AZ), 0, AZ), jax.random.fold_in(splits[4], 1), 0, AZ - 1).astype(jnp.int32),
        "inlet_weights": jnp.clip(0.1 + 0.35 * jax.random.uniform(splits[5], (KS, AZ), jnp.float32) ** block_levels(splits[5], (KS, AZ), ((1, 8),), -0.2, 0.2), 0.1, 0.45),
        "outlet_ids": touch_ends(jax.random.randint(splits[6], (KS, AZ), 0, AZ), jax.random.fold_in(splits[6], 1), 0, AZ - 1).astype(jnp.int32),
        "outlet_weights": jnp.clip(0.1 + 0.35 * jax.random.uniform(splits[7], (KS, AZ), jnp.float32) ** block_levels(splits[7], (KS, AZ), ((1, 8),), -0.2, 0.2), 0.1, 0.45),
    }


courant = 0.5
diffusion = 0.1
source_step = 0.5


def tendency(values, low_ghost, high_ghost, react_rate, mix_matrix, activation):
    backward = jnp.concatenate([low_ghost[:, None, :], values[:, :-1, :]], axis=1)
    forward = jnp.concatenate([values[:, 1:, :], high_ghost[:, None, :]], axis=1)
    cycle_left = jnp.roll(values, 1, axis=2)
    cycle_right = jnp.roll(values, -1, axis=2)
    heat = 1.0 + jax.nn.softplus(values[4])
    reaction = react_rate[None] * values * jnp.exp(-activation[:, None, None] / heat[None])
    source = jnp.einsum("fg,gxr->fxr", mix_matrix, reaction, precision=lax.Precision.HIGHEST)
    advect = -courant * (values - backward)
    spread = diffusion * (backward + forward + cycle_left + cycle_right - 4.0 * values)
    return advect + spread + source_step * source


def reference(fields, react_rate, mix_matrix, activation, inlet_ids, inlet_weights, outlet_ids, outlet_weights):
    boundary_row = (N_GRP - 1) * CX
    combustor = fields[:, :boundary_row, :]
    turbine = fields[:, boundary_row:, :]
    rate_comb = react_rate[:boundary_row]
    rate_turb = react_rate[boundary_row:]
    exit_layer = combustor[:, -1, :]
    inlet_values = jnp.sum(exit_layer[:, inlet_ids] * inlet_weights[None], axis=1)
    pressure_row = turbine[4, 0, :]
    back_pressure = jnp.sum(pressure_row[outlet_ids] * outlet_weights, axis=0)
    zero_layer = jnp.zeros((NF, AZ), jnp.float32)

    def comb_rate(values):
        high_ghost = values[:, -1, :].at[4].set(back_pressure)
        return tendency(values, zero_layer, high_ghost, rate_comb, mix_matrix, activation)

    def turb_rate(values):
        return tendency(values, inlet_values, values[:, -1, :], rate_turb, mix_matrix, activation)

    first_c = combustor + comb_rate(combustor)
    new_c = 0.5 * (combustor + first_c + comb_rate(first_c))
    first_t = turbine + turb_rate(turbine)
    new_t = 0.5 * (turbine + first_t + turb_rate(first_t))
    return jnp.concatenate([new_c, new_t], axis=1)
```

```python
import functools

import jax
import jax.numpy as jnp
from jax import lax
from jax.experimental import pallas as pl
from jax.experimental.pallas import tpu as pltpu
from jax.sharding import PartitionSpec as P

courant = 0.5
diffusion = 0.1
source_step = 0.5

SUB = 8
LANE = 128


def shift_from(axis, count, step, pairs_of):
    return [(i, (i + step) % count) for i in pairs_of]


def step_kernel(nf, rows, lanes, mix_s, act_s, ahi_s, f_hbm, rate_ref, lo1_ref, lo2_ref, hi1_ref,
                hi2_ref, lft_ref, rgt_ref, out_ref, edge_rows_ref, col0_ref, col1_ref, ext1, ext2, sem):
    n_i = rows // SUB
    n_j = lanes // LANE
    top = SUB + rows
    right = LANE + lanes

    copy = pltpu.make_async_copy(f_hbm, ext1.at[:, SUB:top, LANE:right], sem.at[0])
    copy.start()
    ext1[:, SUB - 1:SUB, LANE:right] = lo1_ref[...]
    ext2[:, SUB - 1:SUB, LANE:right] = lo2_ref[...]
    ext1[:, SUB:top, 0:LANE] = jnp.broadcast_to(lft_ref[...], (nf, rows, LANE))
    ext1[:, SUB:top, right:right + LANE] = jnp.broadcast_to(rgt_ref[...], (nf, rows, LANE))
    zeros = jnp.zeros((nf, rows, LANE), jnp.float32)
    ext2[:, SUB:top, 0:LANE] = zeros
    ext2[:, SUB:top, right:right + LANE] = zeros
    copy.wait()
    for f in range(nf):
        ext1[f, top:top + 1, LANE:right] = ahi_s[f] * ext1[f, top - 1:top, LANE:right] + hi1_ref[f]

    sub_id = lax.broadcasted_iota(jnp.int32, (SUB, LANE), 0)
    lane_id = lax.broadcasted_iota(jnp.int32, (SUB, LANE), 1)
    first_sub = sub_id == 0
    last_sub = sub_id == SUB - 1
    first_lane = lane_id == 0
    last_lane = lane_id == LANE - 1

    def tendency_tile(src, r, c, rate_t):
        v4 = src[4, pl.ds(r, SUB), pl.ds(c, LANE)]
        heat = 1.0 + (jnp.maximum(v4, 0.0) + jnp.log1p(jnp.exp(-jnp.abs(v4))))
        inv_heat = 1.0 / heat
        vals = []
        react = []
        for f in range(nf):
            v = src[f, pl.ds(r, SUB), pl.ds(c, LANE)]
            vals.append(v)
            react.append(rate_t * v * jnp.exp(-act_s[f] * inv_heat))
        tends = []
        for f in range(nf):
            v = vals[f]
            up = src[f, pl.ds(r - SUB, SUB), pl.ds(c, LANE)]
            down = src[f, pl.ds(r + SUB, SUB), pl.ds(c, LANE)]
            west = src[f, pl.ds(r, SUB), pl.ds(c - LANE, LANE)]
            east = src[f, pl.ds(r, SUB), pl.ds(c + LANE, LANE)]
            backward = jnp.where(first_sub, pltpu.roll(up, 1, 0), pltpu.roll(v, 1, 0))
            forward = jnp.where(last_sub, pltpu.roll(down, SUB - 1, 0), pltpu.roll(v, SUB - 1, 0))
            left = jnp.where(first_lane, pltpu.roll(west, 1, 1), pltpu.roll(v, 1, 1))
            rgt = jnp.where(last_lane, pltpu.roll(east, LANE - 1, 1), pltpu.roll(v, LANE - 1, 1))
            acc = mix_s[f, 0] * react[0]
            for g in range(1, nf):
                acc = acc + mix_s[f, g] * react[g]
            advect = -courant * (v - backward)
            spread = diffusion * (backward + forward + left + rgt - 4.0 * v)
            tends.append(advect + spread + source_step * acc)
        return vals, tends

    def tile_offsets(t):
        i = t // n_j
        j = t % n_j
        r0 = pl.multiple_of(i * SUB, SUB)
        c0 = pl.multiple_of(j * LANE, LANE)
        return r0, c0

    def stage_one(t, carry):
        r0, c0 = tile_offsets(t)
        rate_t = rate_ref[pl.ds(r0, SUB), pl.ds(c0, LANE)]
        vals, tends = tendency_tile(ext1, r0 + SUB, c0 + LANE, rate_t)
        for f in range(nf):
            ext2[f, pl.ds(r0 + SUB, SUB), pl.ds(c0 + LANE, LANE)] = vals[f] + tends[f]
        return carry

    lax.fori_loop(0, n_i * n_j, stage_one, 0)

    for f in range(nf):
        ext2[f, top:top + 1, LANE:right] = ahi_s[f] * ext2[f, top - 1:top, LANE:right] + hi2_ref[f]

    def stage_two(t, carry):
        r0, c0 = tile_offsets(t)
        rate_t = rate_ref[pl.ds(r0, SUB), pl.ds(c0, LANE)]
        vals, tends = tendency_tile(ext2, r0 + SUB, c0 + LANE, rate_t)
        for f in range(nf):
            base = ext1[f, pl.ds(r0 + SUB, SUB), pl.ds(c0 + LANE, LANE)]
            out_ref[f, pl.ds(r0, SUB), pl.ds(c0, LANE)] = 0.5 * (base + vals[f] + tends[f])
        return carry

    lax.fori_loop(0, n_i * n_j, stage_two, 0)

    edge_rows_ref[:, 0:1, :] = ext2[:, SUB:SUB + 1, LANE:right]
    edge_rows_ref[:, 1:2, :] = ext2[:, top - 1:top, LANE:right]
    col0_ref[...] = ext2[:, SUB:top, LANE:LANE + 1]
    col1_ref[...] = ext2[:, SUB:top, right - 1:right]


def fused_step(fields, rate, mix, act, ahi, lo1, lo2, hi1, hi2, lft, rgt):
    nf, rows, lanes = fields.shape
    vmem = pltpu.VMEM
    smem = pl.BlockSpec(memory_space=pltpu.SMEM)
    vspec = pl.BlockSpec(memory_space=vmem)
    cells = rows * lanes
    cost = pl.CostEstimate(
        flops=2 * cells * nf * (2 * nf + 24),
        transcendentals=2 * cells * (nf + 3),
        bytes_accessed=4 * cells * (2 * nf + 1),
    )
    return pl.pallas_call(
        functools.partial(step_kernel, nf, rows, lanes),
        out_shape=(
            jax.ShapeDtypeStruct((nf, rows, lanes), jnp.float32),
            jax.ShapeDtypeStruct((nf, 2, lanes), jnp.float32),
            jax.ShapeDtypeStruct((nf, rows, 1), jnp.float32),
            jax.ShapeDtypeStruct((nf, rows, 1), jnp.float32),
        ),
        in_specs=[smem, smem, smem, pl.BlockSpec(memory_space=pl.ANY)] + [vspec] * 7,
        out_specs=(vspec, vspec, vspec, vspec),
        scratch_shapes=[
            vmem((nf, rows + 2 * SUB, lanes + 2 * LANE), jnp.float32),
            vmem((nf, rows + 2 * SUB, lanes + 2 * LANE), jnp.float32),
            pltpu.SemaphoreType.DMA((1,)),
        ],
        compiler_params=pltpu.CompilerParams(vmem_limit_bytes=60 * 1024 * 1024),
        cost_estimate=cost,
    )(mix, act, ahi, fields, rate, lo1, lo2, hi1, hi2, lft, rgt)


def shards(
    fields, react_rate, mix_matrix, activation, inlet_ids, inlet_weights, outlet_ids, outlet_weights
):
    nf, rows, lanes = fields.shape
    n_grp = lax.axis_size("grp")
    n_blk = lax.axis_size("blk")
    g = lax.axis_index("grp")
    exit_grp = n_grp - 2
    turb_grp = n_grp - 1
    at_exit = g == exit_grp
    at_turb = g == turb_grp

    last_row = fields[:, -1, :]
    first_row = fields[:, 0, :]
    payload = jnp.concatenate([last_row, first_row[4:5]], axis=0)
    planes = lax.all_gather(payload, "blk", axis=0, tiled=False)
    table = jnp.transpose(planes, (0, 2, 1)).reshape(n_blk * lanes, nf + 1)
    ids = jnp.concatenate([inlet_ids, outlet_ids], axis=0)
    picked = jnp.take(table, ids, axis=0, mode="clip")
    ks = inlet_ids.shape[0]
    inlet = jnp.sum(picked[:ks, :, :nf] * inlet_weights[:, :, None], axis=0)
    back = jnp.sum(picked[ks:, :, nf] * outlet_weights, axis=0)
    swap = jnp.concatenate([jnp.transpose(inlet), back[None]], axis=0)
    swapped = lax.ppermute(swap, "grp", [(exit_grp, turb_grp), (turb_grp, exit_grp)])
    inlet_values = swapped[:nf]
    back_pressure = swapped[nf]

    halo_lo = lax.ppermute(last_row, "grp", [(i, i + 1) for i in range(n_grp - 2)])
    halo_hi = lax.ppermute(first_row, "grp", [(i + 1, i) for i in range(n_grp - 2)])
    lft = lax.ppermute(fields[:, :, -1:], "blk", [(i, (i + 1) % n_blk) for i in range(n_blk)])
    rgt = lax.ppermute(fields[:, :, :1], "blk", [((i + 1) % n_blk, i) for i in range(n_blk)])

    field_id = jnp.arange(nf)
    bp_term = jnp.where((field_id[:, None] == 4) & at_exit, back_pressure[None, :], 0.0)
    lo1 = jnp.where(at_turb, inlet_values, halo_lo)
    lo2 = jnp.where(at_turb, inlet_values, 0.0)
    hi1 = halo_hi + bp_term
    hi2 = bp_term
    ahi = jnp.where(at_turb, 1.0, jnp.where(at_exit & (field_id != 4), 1.0, 0.0)).astype(jnp.float32)

    out, edge_rows, col0, col1 = fused_step(
        fields, react_rate, mix_matrix, activation, ahi,
        lo1[:, None, :], lo2[:, None, :], hi1[:, None, :], hi2[:, None, :], lft, rgt,
    )

    g0 = lax.ppermute(edge_rows[:, 1, :], "grp", [(i, i + 1) for i in range(n_grp - 2)])
    g1 = lax.ppermute(edge_rows[:, 0, :], "grp", [(i + 1, i) for i in range(n_grp - 2)])
    gl = lax.ppermute(col1, "blk", [(i, (i + 1) % n_blk) for i in range(n_blk)])
    gr = lax.ppermute(col0, "blk", [((i + 1) % n_blk, i) for i in range(n_blk)])
    low_w = 0.5 * (courant + diffusion)
    side_w = 0.5 * diffusion
    row = lax.slice_in_dim(out, 0, 1, axis=1) + low_w * g0[:, None, :]
    out = lax.dynamic_update_slice(out, row, (0, 0, 0))
    row = lax.slice_in_dim(out, rows - 1, rows, axis=1) + side_w * g1[:, None, :]
    out = lax.dynamic_update_slice(out, row, (0, rows - 1, 0))
    col = lax.slice_in_dim(out, 0, 1, axis=2) + side_w * gl
    out = lax.dynamic_update_slice(out, col, (0, 0, 0))
    col = lax.slice_in_dim(out, lanes - 1, lanes, axis=2) + side_w * gr
    return lax.dynamic_update_slice(out, col, (0, 0, lanes - 1))


def solution(mesh):
    in_specs = (
        P(None, "grp", "blk"),
        P("grp", "blk"),
        P(),
        P(),
        P(None, "blk"),
        P(None, "blk"),
        P(None, "blk"),
        P(None, "blk"),
    )
    out_specs = P(None, "grp", "blk")
    return jax.shard_map(shards, mesh=mesh, in_specs=in_specs, out_specs=out_specs, check_vma=False)
```

```python
import functools

import jax
import jax.numpy as jnp
from jax import lax
from jax.experimental import pallas as pl
from jax.experimental.pallas import tpu as pltpu
from jax.sharding import PartitionSpec as P

courant = 0.5
diffusion = 0.1
source_step = 0.5

SUB = 8
LANE = 128


def shift_from(axis, count, step, pairs_of):
    return [(i, (i + step) % count) for i in pairs_of]


def step_kernel(nf, rows, lanes, mix_s, act_s, ahi_s, f_hbm, rate_ref, lo1_ref, lo2_ref, hi1_ref,
                hi2_ref, lft_ref, rgt_ref, out_ref, edge_rows_ref, col0_ref, col1_ref, ext1, ext2, sem):
    n_i = rows // SUB
    n_j = lanes // LANE
    top = SUB + rows
    right = LANE + lanes

    copy = pltpu.make_async_copy(f_hbm, ext1.at[:, SUB:top, LANE:right], sem.at[0])
    copy.start()
    ext1[:, SUB - 1:SUB, LANE:right] = lo1_ref[...]
    ext2[:, SUB - 1:SUB, LANE:right] = lo2_ref[...]
    ext1[:, SUB:top, 0:LANE] = jnp.broadcast_to(lft_ref[...], (nf, rows, LANE))
    ext1[:, SUB:top, right:right + LANE] = jnp.broadcast_to(rgt_ref[...], (nf, rows, LANE))
    zeros = jnp.zeros((nf, rows, LANE), jnp.float32)
    ext2[:, SUB:top, 0:LANE] = zeros
    ext2[:, SUB:top, right:right + LANE] = zeros
    copy.wait()
    for f in range(nf):
        ext1[f, top:top + 1, LANE:right] = ahi_s[f] * ext1[f, top - 1:top, LANE:right] + hi1_ref[f]

    sub_id = lax.broadcasted_iota(jnp.int32, (SUB, LANE), 0)
    lane_id = lax.broadcasted_iota(jnp.int32, (SUB, LANE), 1)
    first_sub = sub_id == 0
    last_sub = sub_id == SUB - 1
    first_lane = lane_id == 0
    last_lane = lane_id == LANE - 1

    def tendency_tile(src, r, c, rate_t):
        v4 = src[4, pl.ds(r, SUB), pl.ds(c, LANE)]
        heat = 1.0 + (jnp.maximum(v4, 0.0) + jnp.log1p(jnp.exp(-jnp.abs(v4))))
        inv_heat = 1.0 / heat
        vals = []
        react = []
        for f in range(nf):
            v = src[f, pl.ds(r, SUB), pl.ds(c, LANE)]
            vals.append(v)
            react.append(rate_t * v * jnp.exp(-act_s[f] * inv_heat))
        tends = []
        for f in range(nf):
            v = vals[f]
            up = src[f, pl.ds(r - SUB, SUB), pl.ds(c, LANE)]
            down = src[f, pl.ds(r + SUB, SUB), pl.ds(c, LANE)]
            west = src[f, pl.ds(r, SUB), pl.ds(c - LANE, LANE)]
            east = src[f, pl.ds(r, SUB), pl.ds(c + LANE, LANE)]
            backward = jnp.where(first_sub, pltpu.roll(up, 1, 0), pltpu.roll(v, 1, 0))
            forward = jnp.where(last_sub, pltpu.roll(down, SUB - 1, 0), pltpu.roll(v, SUB - 1, 0))
            left = jnp.where(first_lane, pltpu.roll(west, 1, 1), pltpu.roll(v, 1, 1))
            rgt = jnp.where(last_lane, pltpu.roll(east, LANE - 1, 1), pltpu.roll(v, LANE - 1, 1))
            acc = mix_s[f, 0] * react[0]
            for g in range(1, nf):
                acc = acc + mix_s[f, g] * react[g]
            advect = -courant * (v - backward)
            spread = diffusion * (backward + forward + left + rgt - 4.0 * v)
            tends.append(advect + spread + source_step * acc)
        return vals, tends

    def tile_offsets(t):
        i = t // n_j
        j = t % n_j
        r0 = pl.multiple_of(i * SUB, SUB)
        c0 = pl.multiple_of(j * LANE, LANE)
        return r0, c0

    def stage_one(t, carry):
        r0, c0 = tile_offsets(t)
        rate_t = rate_ref[pl.ds(r0, SUB), pl.ds(c0, LANE)]
        vals, tends = tendency_tile(ext1, r0 + SUB, c0 + LANE, rate_t)
        for f in range(nf):
            ext2[f, pl.ds(r0 + SUB, SUB), pl.ds(c0 + LANE, LANE)] = vals[f] + tends[f]
        return carry

    lax.fori_loop(0, n_i * n_j, stage_one, 0)

    for f in range(nf):
        ext2[f, top:top + 1, LANE:right] = ahi_s[f] * ext2[f, top - 1:top, LANE:right] + hi2_ref[f]

    def stage_two(t, carry):
        r0, c0 = tile_offsets(t)
        rate_t = rate_ref[pl.ds(r0, SUB), pl.ds(c0, LANE)]
        vals, tends = tendency_tile(ext2, r0 + SUB, c0 + LANE, rate_t)
        for f in range(nf):
            base = ext1[f, pl.ds(r0 + SUB, SUB), pl.ds(c0 + LANE, LANE)]
            out_ref[f, pl.ds(r0, SUB), pl.ds(c0, LANE)] = 0.5 * (base + vals[f] + tends[f])
        return carry

    lax.fori_loop(0, n_i * n_j, stage_two, 0)

    edge_rows_ref[:, 0:1, :] = ext2[:, SUB:SUB + 1, LANE:right]
    edge_rows_ref[:, 1:2, :] = ext2[:, top - 1:top, LANE:right]
    col0_ref[...] = ext2[:, SUB:top, LANE:LANE + 1]
    col1_ref[...] = ext2[:, SUB:top, right - 1:right]


def fused_step(fields, rate, mix, act, ahi, lo1, lo2, hi1, hi2, lft, rgt):
    nf, rows, lanes = fields.shape
    vmem = pltpu.VMEM
    smem = pl.BlockSpec(memory_space=pltpu.SMEM)
    vspec = pl.BlockSpec(memory_space=vmem)
    cells = rows * lanes
    cost = pl.CostEstimate(
        flops=2 * cells * nf * (2 * nf + 24),
        transcendentals=2 * cells * (nf + 3),
        bytes_accessed=4 * cells * (2 * nf + 1),
    )
    return pl.pallas_call(
        functools.partial(step_kernel, nf, rows, lanes),
        out_shape=(
            jax.ShapeDtypeStruct((nf, rows, lanes), jnp.float32),
            jax.ShapeDtypeStruct((nf, 2, lanes), jnp.float32),
            jax.ShapeDtypeStruct((nf, rows, 1), jnp.float32),
            jax.ShapeDtypeStruct((nf, rows, 1), jnp.float32),
        ),
        in_specs=[smem, smem, smem, pl.BlockSpec(memory_space=pl.ANY)] + [vspec] * 7,
        out_specs=(vspec, vspec, vspec, vspec),
        scratch_shapes=[
            vmem((nf, rows + 2 * SUB, lanes + 2 * LANE), jnp.float32),
            vmem((nf, rows + 2 * SUB, lanes + 2 * LANE), jnp.float32),
            pltpu.SemaphoreType.DMA((1,)),
        ],
        compiler_params=pltpu.CompilerParams(vmem_limit_bytes=60 * 1024 * 1024),
        cost_estimate=cost,
    )(mix, act, ahi, fields, rate, lo1, lo2, hi1, hi2, lft, rgt)


def interp_kernel(ks, ids_s, w_s, table_ref, o_ref):
    lanes = o_ref.shape[1]

    def body(p, carry):
        for half in range(2):
            acc = None
            for k in range(ks):
                row = half * ks + k
                q = ids_s[row, p]
                term = w_s[row, p] * table_ref[pl.ds(q, 1), :]
                acc = term if acc is None else acc + term
            o_ref[half, pl.ds(p, 1), :] = acc
        return carry

    lax.fori_loop(0, lanes, body, 0)


def interpolate(ids, weights, table):
    ks2, lanes = ids.shape
    smem = pl.BlockSpec(memory_space=pltpu.SMEM)
    vspec = pl.BlockSpec(memory_space=pltpu.VMEM)
    return pl.pallas_call(
        functools.partial(interp_kernel, ks2 // 2),
        out_shape=jax.ShapeDtypeStruct((2, lanes, table.shape[1]), jnp.float32),
        in_specs=[smem, smem, vspec],
        out_specs=vspec,
    )(ids, weights, table)


def fix_kernel(low_w, side_w, out_in, g0_ref, g1_ref, gl_ref, gr_ref, out_ref, rb, cb, sem):
    nf, rows, lanes = out_ref.shape
    row_win = (pl.ds(0, SUB), pl.ds(rows - SUB, SUB))
    col_win = (pl.ds(0, LANE), pl.ds(lanes - LANE, LANE))
    loads = [pltpu.make_async_copy(out_ref.at[:, row_win[s], :], rb.at[s], sem.at[s]) for s in range(2)]
    for c in loads:
        c.start()
    for c in loads:
        c.wait()
    sub_id = lax.broadcasted_iota(jnp.int32, (nf, SUB, lanes), 1)
    rb[0] = rb[0] + jnp.where(sub_id == 0, low_w * g0_ref[...], 0.0)
    rb[1] = rb[1] + jnp.where(sub_id == SUB - 1, side_w * g1_ref[...], 0.0)
    stores = [pltpu.make_async_copy(rb.at[s], out_ref.at[:, row_win[s], :], sem.at[s]) for s in range(2)]
    for c in stores:
        c.start()
    for c in stores:
        c.wait()
    loads = [pltpu.make_async_copy(out_ref.at[:, :, col_win[s]], cb.at[s], sem.at[s]) for s in range(2)]
    for c in loads:
        c.start()
    for c in loads:
        c.wait()
    lane_id = lax.broadcasted_iota(jnp.int32, (nf, rows, LANE), 2)
    cb[0] = cb[0] + jnp.where(lane_id == 0, side_w * gl_ref[...], 0.0)
    cb[1] = cb[1] + jnp.where(lane_id == LANE - 1, side_w * gr_ref[...], 0.0)
    stores = [pltpu.make_async_copy(cb.at[s], out_ref.at[:, :, col_win[s]], sem.at[s]) for s in range(2)]
    for c in stores:
        c.start()
    for c in stores:
        c.wait()


def fix_edges(out, g0, g1, gl, gr, low_w, side_w):
    nf, rows, lanes = out.shape
    vspec = pl.BlockSpec(memory_space=pltpu.VMEM)
    anyspec = pl.BlockSpec(memory_space=pl.ANY)
    return pl.pallas_call(
        functools.partial(fix_kernel, low_w, side_w),
        out_shape=jax.ShapeDtypeStruct(out.shape, jnp.float32),
        in_specs=[anyspec, vspec, vspec, vspec, vspec],
        out_specs=anyspec,
        scratch_shapes=[
            pltpu.VMEM((2, nf, SUB, lanes), jnp.float32),
            pltpu.VMEM((2, nf, rows, LANE), jnp.float32),
            pltpu.SemaphoreType.DMA((2,)),
        ],
        input_output_aliases={0: 0},
    )(out, g0, g1, gl, gr)


def shards(
    fields, react_rate, mix_matrix, activation, inlet_ids, inlet_weights, outlet_ids, outlet_weights
):
    nf, rows, lanes = fields.shape
    n_grp = lax.axis_size("grp")
    n_blk = lax.axis_size("blk")
    g = lax.axis_index("grp")
    exit_grp = n_grp - 2
    turb_grp = n_grp - 1
    at_exit = g == exit_grp
    at_turb = g == turb_grp

    last_row = fields[:, -1, :]
    first_row = fields[:, 0, :]
    b = lax.axis_index("blk")
    payload = jnp.concatenate([last_row, first_row[4:5]], axis=0)
    slots = jnp.zeros((n_blk, nf + 1, lanes), jnp.float32)
    slots = lax.dynamic_update_slice(slots, payload[None], (b, 0, 0))
    planes = lax.psum(slots, "blk")
    table = jnp.transpose(planes, (0, 2, 1)).reshape(n_blk * lanes, nf + 1)
    ids = jnp.concatenate([inlet_ids, outlet_ids], axis=0)
    wts = jnp.concatenate([inlet_weights, outlet_weights], axis=0)
    picked = interpolate(ids, wts, table)
    inlet = picked[0, :, :nf]
    back = picked[1, :, nf]
    swap = jnp.concatenate([jnp.transpose(inlet), back[None]], axis=0)
    swapped = lax.ppermute(swap, "grp", [(exit_grp, turb_grp), (turb_grp, exit_grp)])
    inlet_values = swapped[:nf]
    back_pressure = swapped[nf]

    halo_lo = lax.ppermute(last_row, "grp", [(i, i + 1) for i in range(n_grp - 2)])
    halo_hi = lax.ppermute(first_row, "grp", [(i + 1, i) for i in range(n_grp - 2)])
    lft = lax.ppermute(fields[:, :, -1:], "blk", [(i, (i + 1) % n_blk) for i in range(n_blk)])
    rgt = lax.ppermute(fields[:, :, :1], "blk", [((i + 1) % n_blk, i) for i in range(n_blk)])

    field_id = jnp.arange(nf)
    bp_term = jnp.where((field_id[:, None] == 4) & at_exit, back_pressure[None, :], 0.0)
    lo1 = jnp.where(at_turb, inlet_values, halo_lo)
    lo2 = jnp.where(at_turb, inlet_values, 0.0)
    hi1 = halo_hi + bp_term
    hi2 = bp_term
    ahi = jnp.where(at_turb, 1.0, jnp.where(at_exit & (field_id != 4), 1.0, 0.0)).astype(jnp.float32)

    out, edge_rows, col0, col1 = fused_step(
        fields, react_rate, mix_matrix, activation, ahi,
        lo1[:, None, :], lo2[:, None, :], hi1[:, None, :], hi2[:, None, :], lft, rgt,
    )

    g0 = lax.ppermute(edge_rows[:, 1, :], "grp", [(i, i + 1) for i in range(n_grp - 2)])
    g1 = lax.ppermute(edge_rows[:, 0, :], "grp", [(i + 1, i) for i in range(n_grp - 2)])
    gl = lax.ppermute(col1, "blk", [(i, (i + 1) % n_blk) for i in range(n_blk)])
    gr = lax.ppermute(col0, "blk", [((i + 1) % n_blk, i) for i in range(n_blk)])
    low_w = 0.5 * (courant + diffusion)
    side_w = 0.5 * diffusion
    return fix_edges(out, g0[:, None, :], g1[:, None, :], gl, gr, low_w, side_w)


def solution(mesh):
    in_specs = (
        P(None, "grp", "blk"),
        P("grp", "blk"),
        P(),
        P(),
        P(None, "blk"),
        P(None, "blk"),
        P(None, "blk"),
        P(None, "blk"),
    )
    out_specs = P(None, "grp", "blk")
    return jax.shard_map(shards, mesh=mesh, in_specs=in_specs, out_specs=out_specs, check_vma=False)
```

```python
import functools

import jax
import jax.numpy as jnp
from jax import lax
from jax.experimental import pallas as pl
from jax.experimental.pallas import tpu as pltpu
from jax.sharding import PartitionSpec as P

courant = 0.5
diffusion = 0.1
source_step = 0.5

SUB = 8
LANE = 128


def step_kernel(nf, rows, lanes, mix_s, act_s, ahi_s, f_hbm, rate_ref, lo1_ref, lo2_ref, hi1_ref,
                hi2_ref, lft_ref, rgt_ref, out_ref, edge_rows_ref, col0_ref, col1_ref, ext1, ext2, sem):
    n_i = rows // SUB
    n_j = lanes // LANE
    top = SUB + rows
    right = LANE + lanes

    copy = pltpu.make_async_copy(f_hbm, ext1.at[:, SUB:top, LANE:right], sem.at[0])
    copy.start()
    ext1[:, SUB - 1:SUB, LANE:right] = lo1_ref[...]
    ext2[:, SUB - 1:SUB, LANE:right] = lo2_ref[...]
    ext1[:, SUB:top, 0:LANE] = jnp.broadcast_to(lft_ref[...], (nf, rows, LANE))
    ext1[:, SUB:top, right:right + LANE] = jnp.broadcast_to(rgt_ref[...], (nf, rows, LANE))
    zeros = jnp.zeros((nf, rows, LANE), jnp.float32)
    ext2[:, SUB:top, 0:LANE] = zeros
    ext2[:, SUB:top, right:right + LANE] = zeros
    copy.wait()
    for f in range(nf):
        ext1[f, top:top + 1, LANE:right] = ahi_s[f] * ext1[f, top - 1:top, LANE:right] + hi1_ref[f]

    sub_id = lax.broadcasted_iota(jnp.int32, (SUB, LANE), 0)
    lane_id = lax.broadcasted_iota(jnp.int32, (SUB, LANE), 1)
    first_sub = sub_id == 0
    last_sub = sub_id == SUB - 1
    first_lane = lane_id == 0
    last_lane = lane_id == LANE - 1

    def tendency_tile(src, r, c, rate_t):
        v4 = src[4, pl.ds(r, SUB), pl.ds(c, LANE)]
        heat = 1.0 + (jnp.maximum(v4, 0.0) + jnp.log1p(jnp.exp(-jnp.abs(v4))))
        inv_heat = 1.0 / heat
        vals = []
        react = []
        for f in range(nf):
            v = src[f, pl.ds(r, SUB), pl.ds(c, LANE)]
            vals.append(v)
            react.append(rate_t * v * jnp.exp(-act_s[f] * inv_heat))
        tends = []
        for f in range(nf):
            v = vals[f]
            up = src[f, pl.ds(r - SUB, SUB), pl.ds(c, LANE)]
            down = src[f, pl.ds(r + SUB, SUB), pl.ds(c, LANE)]
            west = src[f, pl.ds(r, SUB), pl.ds(c - LANE, LANE)]
            east = src[f, pl.ds(r, SUB), pl.ds(c + LANE, LANE)]
            backward = jnp.where(first_sub, pltpu.roll(up, 1, 0), pltpu.roll(v, 1, 0))
            forward = jnp.where(last_sub, pltpu.roll(down, SUB - 1, 0), pltpu.roll(v, SUB - 1, 0))
            left = jnp.where(first_lane, pltpu.roll(west, 1, 1), pltpu.roll(v, 1, 1))
            rgt = jnp.where(last_lane, pltpu.roll(east, LANE - 1, 1), pltpu.roll(v, LANE - 1, 1))
            acc = mix_s[f, 0] * react[0]
            for g in range(1, nf):
                acc = acc + mix_s[f, g] * react[g]
            advect = -courant * (v - backward)
            spread = diffusion * (backward + forward + left + rgt - 4.0 * v)
            tends.append(advect + spread + source_step * acc)
        return vals, tends

    def tile_offsets(t):
        i = t // n_j
        j = t % n_j
        r0 = pl.multiple_of(i * SUB, SUB)
        c0 = pl.multiple_of(j * LANE, LANE)
        return r0, c0

    def stage_one(t, carry):
        r0, c0 = tile_offsets(t)
        rate_t = rate_ref[pl.ds(r0, SUB), pl.ds(c0, LANE)]
        vals, tends = tendency_tile(ext1, r0 + SUB, c0 + LANE, rate_t)
        for f in range(nf):
            ext2[f, pl.ds(r0 + SUB, SUB), pl.ds(c0 + LANE, LANE)] = vals[f] + tends[f]
        return carry

    lax.fori_loop(0, n_i * n_j, stage_one, 0)

    for f in range(nf):
        ext2[f, top:top + 1, LANE:right] = ahi_s[f] * ext2[f, top - 1:top, LANE:right] + hi2_ref[f]

    def stage_two(t, carry):
        r0, c0 = tile_offsets(t)
        rate_t = rate_ref[pl.ds(r0, SUB), pl.ds(c0, LANE)]
        vals, tends = tendency_tile(ext2, r0 + SUB, c0 + LANE, rate_t)
        for f in range(nf):
            base = ext1[f, pl.ds(r0 + SUB, SUB), pl.ds(c0 + LANE, LANE)]
            out_ref[f, pl.ds(r0, SUB), pl.ds(c0, LANE)] = 0.5 * (base + vals[f] + tends[f])
        return carry

    lax.fori_loop(0, n_i * n_j, stage_two, 0)

    edge_rows_ref[:, 0:1, :] = ext2[:, SUB:SUB + 1, LANE:right]
    edge_rows_ref[:, 1:2, :] = ext2[:, top - 1:top, LANE:right]
    col0_ref[...] = ext2[:, SUB:top, LANE:LANE + 1]
    col1_ref[...] = ext2[:, SUB:top, right - 1:right]


def fused_step(fields, rate, mix, act, ahi, lo1, lo2, hi1, hi2, lft, rgt):
    nf, rows, lanes = fields.shape
    vmem = pltpu.VMEM
    smem = pl.BlockSpec(memory_space=pltpu.SMEM)
    vspec = pl.BlockSpec(memory_space=vmem)
    cells = rows * lanes
    cost = pl.CostEstimate(
        flops=2 * cells * nf * (2 * nf + 24),
        transcendentals=2 * cells * (nf + 3),
        bytes_accessed=4 * cells * (2 * nf + 1),
    )
    return pl.pallas_call(
        functools.partial(step_kernel, nf, rows, lanes),
        out_shape=(
            jax.ShapeDtypeStruct((nf, rows, lanes), jnp.float32),
            jax.ShapeDtypeStruct((nf, 2, lanes), jnp.float32),
            jax.ShapeDtypeStruct((nf, rows, 1), jnp.float32),
            jax.ShapeDtypeStruct((nf, rows, 1), jnp.float32),
        ),
        in_specs=[smem, smem, smem, pl.BlockSpec(memory_space=pl.ANY)] + [vspec] * 7,
        out_specs=(vspec, vspec, vspec, vspec),
        scratch_shapes=[
            vmem((nf, rows + 2 * SUB, lanes + 2 * LANE), jnp.float32),
            vmem((nf, rows + 2 * SUB, lanes + 2 * LANE), jnp.float32),
            pltpu.SemaphoreType.DMA((1,)),
        ],
        compiler_params=pltpu.CompilerParams(vmem_limit_bytes=60 * 1024 * 1024),
        cost_estimate=cost,
    )(mix, act, ahi, fields, rate, lo1, lo2, hi1, hi2, lft, rgt)


def interp_kernel(ks, ids_s, w_s, table_ref, o_ref):
    lanes = o_ref.shape[1]

    def body(p, carry):
        for half in range(2):
            acc = None
            for k in range(ks):
                row = half * ks + k
                q = ids_s[row, p]
                term = w_s[row, p] * table_ref[pl.ds(q, 1), :]
                acc = term if acc is None else acc + term
            o_ref[half, pl.ds(p, 1), :] = acc
        return carry

    lax.fori_loop(0, lanes, body, 0, unroll=8)


def interpolate(ids, weights, table):
    ks2, lanes = ids.shape
    smem = pl.BlockSpec(memory_space=pltpu.SMEM)
    vspec = pl.BlockSpec(memory_space=pltpu.VMEM)
    return pl.pallas_call(
        functools.partial(interp_kernel, ks2 // 2),
        out_shape=jax.ShapeDtypeStruct((2, lanes, table.shape[1]), jnp.float32),
        in_specs=[smem, smem, vspec],
        out_specs=vspec,
    )(ids, weights, table)


def fix_kernel(low_w, side_w, out_in, g0_ref, g1_ref, gl_ref, gr_ref, out_ref, rb, cb, sem):
    nf, rows, lanes = out_ref.shape
    row_win = (pl.ds(0, SUB), pl.ds(rows - SUB, SUB))
    col_win = (pl.ds(0, LANE), pl.ds(lanes - LANE, LANE))
    loads = [pltpu.make_async_copy(out_ref.at[:, row_win[s], :], rb.at[s], sem.at[s]) for s in range(2)]
    for c in loads:
        c.start()
    for c in loads:
        c.wait()
    sub_id = lax.broadcasted_iota(jnp.int32, (nf, SUB, lanes), 1)
    rb[0] = rb[0] + jnp.where(sub_id == 0, low_w * g0_ref[...], 0.0)
    rb[1] = rb[1] + jnp.where(sub_id == SUB - 1, side_w * g1_ref[...], 0.0)
    stores = [pltpu.make_async_copy(rb.at[s], out_ref.at[:, row_win[s], :], sem.at[s]) for s in range(2)]
    for c in stores:
        c.start()
    for c in stores:
        c.wait()
    loads = [pltpu.make_async_copy(out_ref.at[:, :, col_win[s]], cb.at[s], sem.at[s]) for s in range(2)]
    for c in loads:
        c.start()
    for c in loads:
        c.wait()
    lane_id = lax.broadcasted_iota(jnp.int32, (nf, rows, LANE), 2)
    cb[0] = cb[0] + jnp.where(lane_id == 0, side_w * gl_ref[...], 0.0)
    cb[1] = cb[1] + jnp.where(lane_id == LANE - 1, side_w * gr_ref[...], 0.0)
    stores = [pltpu.make_async_copy(cb.at[s], out_ref.at[:, :, col_win[s]], sem.at[s]) for s in range(2)]
    for c in stores:
        c.start()
    for c in stores:
        c.wait()


def fix_edges(out, g0, g1, gl, gr, low_w, side_w):
    nf, rows, lanes = out.shape
    vspec = pl.BlockSpec(memory_space=pltpu.VMEM)
    anyspec = pl.BlockSpec(memory_space=pl.ANY)
    return pl.pallas_call(
        functools.partial(fix_kernel, low_w, side_w),
        out_shape=jax.ShapeDtypeStruct(out.shape, jnp.float32),
        in_specs=[anyspec, vspec, vspec, vspec, vspec],
        out_specs=anyspec,
        scratch_shapes=[
            pltpu.VMEM((2, nf, SUB, lanes), jnp.float32),
            pltpu.VMEM((2, nf, rows, LANE), jnp.float32),
            pltpu.SemaphoreType.DMA((2,)),
        ],
        input_output_aliases={0: 0},
    )(out, g0, g1, gl, gr)


def shards(
    fields, react_rate, mix_matrix, activation, inlet_ids, inlet_weights, outlet_ids, outlet_weights
):
    nf, rows, lanes = fields.shape
    n_grp = lax.axis_size("grp")
    n_blk = lax.axis_size("blk")
    g = lax.axis_index("grp")
    exit_grp = n_grp - 2
    turb_grp = n_grp - 1
    at_exit = g == exit_grp
    at_turb = g == turb_grp

    last_row = fields[:, -1, :]
    first_row = fields[:, 0, :]
    b = lax.axis_index("blk")
    payload = jnp.concatenate([last_row, first_row[4:5]], axis=0)
    planes = payload[None]
    span = 1
    while span < n_blk:
        partner = [(i, i ^ span) for i in range(n_blk)]
        planes = jnp.concatenate([planes, lax.ppermute(planes, "blk", partner)], axis=0)
        span *= 2
    table = jnp.transpose(planes, (0, 2, 1)).reshape(n_blk * lanes, nf + 1)
    ids = jnp.concatenate([inlet_ids, outlet_ids], axis=0)
    ids = (jnp.bitwise_xor(ids // lanes, b) * lanes) + ids % lanes
    wts = jnp.concatenate([inlet_weights, outlet_weights], axis=0)
    picked = interpolate(ids, wts, table)
    inlet = picked[0, :, :nf]
    back = picked[1, :, nf]
    swap = jnp.concatenate([jnp.transpose(inlet), back[None]], axis=0)
    swapped = lax.ppermute(swap, "grp", [(exit_grp, turb_grp), (turb_grp, exit_grp)])
    inlet_values = swapped[:nf]
    back_pressure = swapped[nf]

    halo_lo = lax.ppermute(last_row, "grp", [(i, i + 1) for i in range(n_grp - 2)])
    halo_hi = lax.ppermute(first_row, "grp", [(i + 1, i) for i in range(n_grp - 2)])
    lft = lax.ppermute(fields[:, :, -1:], "blk", [(i, (i + 1) % n_blk) for i in range(n_blk)])
    rgt = lax.ppermute(fields[:, :, :1], "blk", [((i + 1) % n_blk, i) for i in range(n_blk)])

    field_id = jnp.arange(nf)
    bp_term = jnp.where((field_id[:, None] == 4) & at_exit, back_pressure[None, :], 0.0)
    lo1 = jnp.where(at_turb, inlet_values, halo_lo)
    lo2 = jnp.where(at_turb, inlet_values, 0.0)
    hi1 = halo_hi + bp_term
    hi2 = bp_term
    ahi = jnp.where(at_turb, 1.0, jnp.where(at_exit & (field_id != 4), 1.0, 0.0)).astype(jnp.float32)

    out, edge_rows, col0, col1 = fused_step(
        fields, react_rate, mix_matrix, activation, ahi,
        lo1[:, None, :], lo2[:, None, :], hi1[:, None, :], hi2[:, None, :], lft, rgt,
    )

    g0 = lax.ppermute(edge_rows[:, 1, :], "grp", [(i, i + 1) for i in range(n_grp - 2)])
    g1 = lax.ppermute(edge_rows[:, 0, :], "grp", [(i + 1, i) for i in range(n_grp - 2)])
    gl = lax.ppermute(col1, "blk", [(i, (i + 1) % n_blk) for i in range(n_blk)])
    gr = lax.ppermute(col0, "blk", [((i + 1) % n_blk, i) for i in range(n_blk)])
    low_w = 0.5 * (courant + diffusion)
    side_w = 0.5 * diffusion
    return fix_edges(out, g0[:, None, :], g1[:, None, :], gl, gr, low_w, side_w)


def solution(mesh):
    in_specs = (
        P(None, "grp", "blk"),
        P("grp", "blk"),
        P(),
        P(),
        P(None, "blk"),
        P(None, "blk"),
        P(None, "blk"),
        P(None, "blk"),
    )
    out_specs = P(None, "grp", "blk")
    return jax.shard_map(shards, mesh=mesh, in_specs=in_specs, out_specs=out_specs, check_vma=False)
```

```python
import functools

import jax
import jax.numpy as jnp
from jax import lax
from jax.experimental import pallas as pl
from jax.experimental.pallas import tpu as pltpu
from jax.sharding import PartitionSpec as P

courant = 0.5
diffusion = 0.1
source_step = 0.5

SUB = 8
LANE = 128


def tile_t(row):
    n = row.shape[1]
    return jnp.transpose(jnp.broadcast_to(row, (n, n)))


def step_kernel(nf, rows, lanes, mix_s, act_s, flag_s, f_hbm, rate_ref, hlo_ref, hhi_ref, sw_ref,
                lft_ref, rgt_ref, out_ref, elo_ref, ehi_ref, clo_ref, chi_ref, ext1, ext2, sem):
    n_i = rows // SUB
    n_j = lanes // LANE
    top = SUB + rows
    right = LANE + lanes
    at_exit = flag_s[0] > 0.5
    at_turb = flag_s[1] > 0.5
    at_end = flag_s[0] + flag_s[1] > 0.5

    copy = pltpu.make_async_copy(f_hbm, ext1.at[:, SUB:top, LANE:right], sem.at[0])
    copy.start()
    zeros = jnp.zeros((rows, LANE), jnp.float32)
    for f in range(nf):
        inlet = sw_ref[f:f + 1, :]
        ext1[f, SUB - 1:SUB, LANE:right] = jnp.where(at_turb, inlet, hlo_ref[f:f + 1, :])
        ext2[f, SUB - 1:SUB, LANE:right] = jnp.where(at_turb, inlet, 0.0)
        ext1[f, SUB:top, 0:LANE] = tile_t(lft_ref[f:f + 1, :])
        ext1[f, SUB:top, right:right + LANE] = tile_t(rgt_ref[f:f + 1, :])
        ext2[f, SUB:top, 0:LANE] = zeros
        ext2[f, SUB:top, right:right + LANE] = zeros
    copy.wait()

    def high_ghost(ext, halo_of):
        for f in range(nf):
            own = ext[f, top - 1:top, LANE:right]
            halo = halo_of(f)
            if f == 4:
                row = jnp.where(at_turb, own, jnp.where(at_exit, sw_ref[nf:nf + 1, :], halo))
            else:
                row = jnp.where(at_end, own, halo)
            ext[f, top:top + 1, LANE:right] = row

    high_ghost(ext1, lambda f: hhi_ref[f:f + 1, :])

    sub_id = lax.broadcasted_iota(jnp.int32, (SUB, LANE), 0)
    lane_id = lax.broadcasted_iota(jnp.int32, (SUB, LANE), 1)
    first_sub = sub_id == 0
    last_sub = sub_id == SUB - 1
    first_lane = lane_id == 0
    last_lane = lane_id == LANE - 1

    def tendency_tile(src, r0, c0, rate_t):
        r = pl.multiple_of(r0 + SUB, SUB)
        c = pl.multiple_of(c0 + LANE, LANE)
        r_up = pl.multiple_of(r0, SUB)
        r_dn = pl.multiple_of(r0 + 2 * SUB, SUB)
        c_w = pl.multiple_of(c0, LANE)
        c_e = pl.multiple_of(c0 + 2 * LANE, LANE)
        v4 = src[4, pl.ds(r, SUB), pl.ds(c, LANE)]
        heat = 1.0 + (jnp.maximum(v4, 0.0) + jnp.log1p(jnp.exp(-jnp.abs(v4))))
        inv_heat = 1.0 / heat
        vals = []
        react = []
        for f in range(nf):
            v = src[f, pl.ds(r, SUB), pl.ds(c, LANE)]
            vals.append(v)
            react.append(rate_t * v * jnp.exp(-act_s[f] * inv_heat))
        tends = []
        for f in range(nf):
            v = vals[f]
            up = src[f, pl.ds(r_up, SUB), pl.ds(c, LANE)]
            down = src[f, pl.ds(r_dn, SUB), pl.ds(c, LANE)]
            west = src[f, pl.ds(r, SUB), pl.ds(c_w, LANE)]
            east = src[f, pl.ds(r, SUB), pl.ds(c_e, LANE)]
            backward = jnp.where(first_sub, pltpu.roll(up, 1, 0), pltpu.roll(v, 1, 0))
            forward = jnp.where(last_sub, pltpu.roll(down, SUB - 1, 0), pltpu.roll(v, SUB - 1, 0))
            left = jnp.where(first_lane, pltpu.roll(west, 1, 1), pltpu.roll(v, 1, 1))
            rgt = jnp.where(last_lane, pltpu.roll(east, LANE - 1, 1), pltpu.roll(v, LANE - 1, 1))
            acc = mix_s[f, 0] * react[0]
            for g in range(1, nf):
                acc = acc + mix_s[f, g] * react[g]
            advect = -courant * (v - backward)
            spread = diffusion * (backward + forward + left + rgt - 4.0 * v)
            tends.append(advect + spread + source_step * acc)
        return vals, tends

    def tile_offsets(t):
        i = t // n_j
        j = t % n_j
        r0 = pl.multiple_of(i * SUB, SUB)
        c0 = pl.multiple_of(j * LANE, LANE)
        return r0, c0

    def stage_one(t, carry):
        r0, c0 = tile_offsets(t)
        rate_t = rate_ref[pl.ds(r0, SUB), pl.ds(c0, LANE)]
        vals, tends = tendency_tile(ext1, r0, c0, rate_t)
        r = pl.multiple_of(r0 + SUB, SUB)
        c = pl.multiple_of(c0 + LANE, LANE)
        for f in range(nf):
            ext2[f, pl.ds(r, SUB), pl.ds(c, LANE)] = vals[f] + tends[f]
        return carry

    lax.fori_loop(0, n_i * n_j, stage_one, 0)

    high_ghost(ext2, lambda f: jnp.zeros((1, lanes), jnp.float32))

    def stage_two(t, carry):
        r0, c0 = tile_offsets(t)
        rate_t = rate_ref[pl.ds(r0, SUB), pl.ds(c0, LANE)]
        vals, tends = tendency_tile(ext2, r0, c0, rate_t)
        r = pl.multiple_of(r0 + SUB, SUB)
        c = pl.multiple_of(c0 + LANE, LANE)
        for f in range(nf):
            base = ext1[f, pl.ds(r, SUB), pl.ds(c, LANE)]
            out_ref[f, pl.ds(r0, SUB), pl.ds(c0, LANE)] = 0.5 * (base + vals[f] + tends[f])
        return carry

    lax.fori_loop(0, n_i * n_j, stage_two, 0)

    for f in range(nf):
        elo_ref[f:f + 1, :] = ext2[f, SUB:SUB + 1, LANE:right]
        ehi_ref[f:f + 1, :] = ext2[f, top - 1:top, LANE:right]
        west = jnp.transpose(ext2[f, SUB:top, LANE:2 * LANE])
        east = jnp.transpose(ext2[f, SUB:top, right - LANE:right])
        clo_ref[f:f + 1, :] = west[0:1, :]
        chi_ref[f:f + 1, :] = east[LANE - 1:LANE, :]


def fused_step(fields, rate, mix, act, flags, halo_lo, halo_hi, swapped, lft, rgt):
    nf, rows, lanes = fields.shape
    vmem = pltpu.VMEM
    smem = pl.BlockSpec(memory_space=pltpu.SMEM)
    vspec = pl.BlockSpec(memory_space=vmem)
    cells = rows * lanes
    cost = pl.CostEstimate(
        flops=2 * cells * nf * (2 * nf + 24),
        transcendentals=2 * cells * (nf + 3),
        bytes_accessed=4 * cells * (2 * nf + 1),
    )
    return pl.pallas_call(
        functools.partial(step_kernel, nf, rows, lanes),
        out_shape=(
            jax.ShapeDtypeStruct((nf, rows, lanes), jnp.float32),
            jax.ShapeDtypeStruct((nf, lanes), jnp.float32),
            jax.ShapeDtypeStruct((nf, lanes), jnp.float32),
            jax.ShapeDtypeStruct((nf, rows), jnp.float32),
            jax.ShapeDtypeStruct((nf, rows), jnp.float32),
        ),
        in_specs=[smem, smem, smem, pl.BlockSpec(memory_space=pl.ANY)] + [vspec] * 6,
        out_specs=(vspec,) * 5,
        scratch_shapes=[
            vmem((nf, rows + 2 * SUB, lanes + 2 * LANE), jnp.float32),
            vmem((nf, rows + 2 * SUB, lanes + 2 * LANE), jnp.float32),
            pltpu.SemaphoreType.DMA((1,)),
        ],
        compiler_params=pltpu.CompilerParams(vmem_limit_bytes=60 * 1024 * 1024),
        cost_estimate=cost,
    )(mix, act, flags, fields, rate, halo_lo, halo_hi, swapped, lft, rgt)


def interp_kernel(ks, flag_s, ids_s, w_s, table_ref, o_ref, acc):
    lanes = o_ref.shape[1]
    half = jnp.where(flag_s[0] > 0.5, 0, ks)
    acc[...] = jnp.zeros(acc.shape, jnp.float32)
    width = table_ref.shape[1]

    @pl.when(flag_s[0] + flag_s[1] > 0.5)
    def _():
        def body(p, carry):
            total = None
            for k in range(ks):
                q = ids_s[half + k, p]
                term = w_s[half + k, p] * table_ref[pl.ds(q, 1), :]
                total = term if total is None else total + term
            acc[pl.ds(p, 1), 0:width] = total
            return carry

        lax.fori_loop(0, lanes, body, 0, unroll=8)

    o_ref[...] = jnp.transpose(acc[...])[0:o_ref.shape[0], :]


def interpolate(flags, ids, weights, table):
    ks2, lanes = ids.shape
    smem = pl.BlockSpec(memory_space=pltpu.SMEM)
    vspec = pl.BlockSpec(memory_space=pltpu.VMEM)
    return pl.pallas_call(
        functools.partial(interp_kernel, ks2 // 2),
        out_shape=jax.ShapeDtypeStruct((table.shape[1], lanes), jnp.float32),
        in_specs=[smem, smem, smem, vspec],
        out_specs=vspec,
        scratch_shapes=[pltpu.VMEM((lanes, LANE), jnp.float32)],
    )(flags, ids, weights, table)


def fix_kernel(low_w, side_w, out_in, g0_ref, g1_ref, gl_ref, gr_ref, out_ref, rb, cb, sem):
    nf, rows, lanes = out_ref.shape
    row_win = (pl.ds(0, SUB), pl.ds(rows - SUB, SUB))
    col_win = (pl.ds(0, LANE), pl.ds(lanes - LANE, LANE))
    loads = [pltpu.make_async_copy(out_ref.at[:, row_win[s], :], rb.at[s], sem.at[s]) for s in range(2)]
    for c in loads:
        c.start()
    for c in loads:
        c.wait()
    for f in range(nf):
        rb[0, f, 0:1, :] = rb[0, f, 0:1, :] + low_w * g0_ref[f:f + 1, :]
        rb[1, f, SUB - 1:SUB, :] = rb[1, f, SUB - 1:SUB, :] + side_w * g1_ref[f:f + 1, :]
    stores = [pltpu.make_async_copy(rb.at[s], out_ref.at[:, row_win[s], :], sem.at[s]) for s in range(2)]
    for c in stores:
        c.start()
    for c in stores:
        c.wait()
    loads = [pltpu.make_async_copy(out_ref.at[:, :, col_win[s]], cb.at[s], sem.at[s]) for s in range(2)]
    for c in loads:
        c.start()
    for c in loads:
        c.wait()
    lane_id = lax.broadcasted_iota(jnp.int32, (rows, LANE), 1)
    for f in range(nf):
        cb[0, f] = cb[0, f] + jnp.where(lane_id == 0, side_w * tile_t(gl_ref[f:f + 1, :]), 0.0)
        cb[1, f] = cb[1, f] + jnp.where(lane_id == LANE - 1, side_w * tile_t(gr_ref[f:f + 1, :]), 0.0)
    stores = [pltpu.make_async_copy(cb.at[s], out_ref.at[:, :, col_win[s]], sem.at[s]) for s in range(2)]
    for c in stores:
        c.start()
    for c in stores:
        c.wait()


def fix_edges(out, g0, g1, gl, gr, low_w, side_w):
    nf, rows, lanes = out.shape
    vspec = pl.BlockSpec(memory_space=pltpu.VMEM)
    anyspec = pl.BlockSpec(memory_space=pl.ANY)
    return pl.pallas_call(
        functools.partial(fix_kernel, low_w, side_w),
        out_shape=jax.ShapeDtypeStruct(out.shape, jnp.float32),
        in_specs=[anyspec, vspec, vspec, vspec, vspec],
        out_specs=anyspec,
        scratch_shapes=[
            pltpu.VMEM((2, nf, SUB, lanes), jnp.float32),
            pltpu.VMEM((2, nf, rows, LANE), jnp.float32),
            pltpu.SemaphoreType.DMA((2,)),
        ],
        input_output_aliases={0: 0},
    )(out, g0, g1, gl, gr)


def shards(
    fields, react_rate, mix_matrix, activation, inlet_ids, inlet_weights, outlet_ids, outlet_weights
):
    nf, rows, lanes = fields.shape
    n_grp = lax.axis_size("grp")
    n_blk = lax.axis_size("blk")
    g = lax.axis_index("grp")
    b = lax.axis_index("blk")
    exit_grp = n_grp - 2
    turb_grp = n_grp - 1
    flags = jnp.stack([g == exit_grp, g == turb_grp]).astype(jnp.float32)

    last_row = fields[:, -1, :]
    first_row = fields[:, 0, :]
    payload = jnp.concatenate([last_row, first_row[4:5]], axis=0)
    planes = payload[None]
    span = 1
    while span < n_blk:
        partner = [(i, i ^ span) for i in range(n_blk)]
        planes = jnp.concatenate([planes, lax.ppermute(planes, "blk", partner)], axis=0)
        span *= 2
    table = jnp.transpose(planes, (0, 2, 1)).reshape(n_blk * lanes, nf + 1)
    ids = jnp.concatenate([inlet_ids, outlet_ids], axis=0)
    ids = (jnp.bitwise_xor(ids // lanes, b) * lanes) + ids % lanes
    wts = jnp.concatenate([inlet_weights, outlet_weights], axis=0)
    swap = interpolate(flags, ids, wts, table)
    swapped = lax.ppermute(swap, "grp", [(exit_grp, turb_grp), (turb_grp, exit_grp)])

    halo_lo = lax.ppermute(last_row, "grp", [(i, i + 1) for i in range(n_grp - 2)])
    halo_hi = lax.ppermute(first_row, "grp", [(i + 1, i) for i in range(n_grp - 2)])
    lft = lax.ppermute(fields[:, :, lanes - 1], "blk", [(i, (i + 1) % n_blk) for i in range(n_blk)])
    rgt = lax.ppermute(fields[:, :, 0], "blk", [((i + 1) % n_blk, i) for i in range(n_blk)])

    out, elo, ehi, clo, chi = fused_step(
        fields, react_rate, mix_matrix, activation, flags, halo_lo, halo_hi, swapped, lft, rgt
    )

    g0 = lax.ppermute(ehi, "grp", [(i, i + 1) for i in range(n_grp - 2)])
    g1 = lax.ppermute(elo, "grp", [(i + 1, i) for i in range(n_grp - 2)])
    gl = lax.ppermute(chi, "blk", [(i, (i + 1) % n_blk) for i in range(n_blk)])
    gr = lax.ppermute(clo, "blk", [((i + 1) % n_blk, i) for i in range(n_blk)])
    low_w = 0.5 * (courant + diffusion)
    side_w = 0.5 * diffusion
    return fix_edges(out, g0, g1, gl, gr, low_w, side_w)


def solution(mesh):
    in_specs = (
        P(None, "grp", "blk"),
        P("grp", "blk"),
        P(),
        P(),
        P(None, "blk"),
        P(None, "blk"),
        P(None, "blk"),
        P(None, "blk"),
    )
    out_specs = P(None, "grp", "blk")
    return jax.shard_map(shards, mesh=mesh, in_specs=in_specs, out_specs=out_specs, check_vma=False)
```

```python
import functools

import jax
import jax.numpy as jnp
from jax import lax
from jax.experimental import pallas as pl
from jax.experimental.pallas import tpu as pltpu
from jax.sharding import PartitionSpec as P

courant = 0.5
diffusion = 0.1
source_step = 0.5

SUB = 8
LANE = 128


def tile_t(row):
    n = row.shape[1]
    return jnp.transpose(jnp.broadcast_to(row, (n, n)))


def step_kernel(nf, rows, lanes, mix_s, act_s, flag_s, f_hbm, rate_ref, hlo_ref, hhi_ref, sw_ref,
                lft_ref, rgt_ref, out_ref, elo_ref, ehi_ref, clo_ref, chi_ref, ext1, ext2, coef, sem):
    n_i = rows // SUB
    n_j = lanes // LANE
    top = SUB + rows
    right = LANE + lanes
    at_exit = flag_s[0] > 0.5
    at_turb = flag_s[1] > 0.5
    at_end = flag_s[0] + flag_s[1] > 0.5

    copy = pltpu.make_async_copy(f_hbm, ext1.at[:, SUB:top, LANE:right], sem.at[0])
    copy.start()
    zeros = jnp.zeros((rows, LANE), jnp.float32)
    for f in range(nf):
        inlet = sw_ref[f:f + 1, :]
        ext1[f, SUB - 1:SUB, LANE:right] = jnp.where(at_turb, inlet, hlo_ref[f:f + 1, :])
        ext2[f, SUB - 1:SUB, LANE:right] = jnp.where(at_turb, inlet, 0.0)
        ext1[f, SUB:top, 0:LANE] = tile_t(lft_ref[f:f + 1, :])
        ext1[f, SUB:top, right:right + LANE] = tile_t(rgt_ref[f:f + 1, :])
        ext2[f, SUB:top, 0:LANE] = zeros
        ext2[f, SUB:top, right:right + LANE] = zeros
    for f in range(nf):
        for g in range(nf):
            coef[f * nf + g] = jnp.full((SUB, LANE), mix_s[f, g], jnp.float32)
        coef[nf * nf + f] = jnp.full((SUB, LANE), -act_s[f], jnp.float32)
    copy.wait()

    def high_ghost(ext, halo_of):
        for f in range(nf):
            own = ext[f, top - 1:top, LANE:right]
            halo = halo_of(f)
            if f == 4:
                row = jnp.where(at_turb, own, jnp.where(at_exit, sw_ref[nf:nf + 1, :], halo))
            else:
                row = jnp.where(at_end, own, halo)
            ext[f, top:top + 1, LANE:right] = row

    high_ghost(ext1, lambda f: hhi_ref[f:f + 1, :])

    sub_id = lax.broadcasted_iota(jnp.int32, (SUB, LANE), 0)
    lane_id = lax.broadcasted_iota(jnp.int32, (SUB, LANE), 1)
    first_sub = sub_id == 0
    last_sub = sub_id == SUB - 1
    first_lane = lane_id == 0
    last_lane = lane_id == LANE - 1

    def tendency_tiles(src, r0, c0s, rate_ts):
        r = pl.multiple_of(r0 + SUB, SUB)
        r_up = pl.multiple_of(r0, SUB)
        r_dn = pl.multiple_of(r0 + 2 * SUB, SUB)
        cs = [pl.multiple_of(c0 + LANE, LANE) for c0 in c0s]
        reacts = []
        for c, rate_t in zip(cs, rate_ts):
            v4 = src[4, pl.ds(r, SUB), pl.ds(c, LANE)]
            heat = 1.0 + (jnp.maximum(v4, 0.0) + jnp.log1p(jnp.exp(-jnp.abs(v4))))
            inv_heat = 1.0 / heat
            reacts.append([
                rate_t * src[f, pl.ds(r, SUB), pl.ds(c, LANE)] * jnp.exp(coef[nf * nf + f] * inv_heat)
                for f in range(nf)
            ])
        tends = [[] for _ in cs]
        for f in range(nf):
            accs = [None] * len(cs)
            for g in range(nf):
                m = coef[f * nf + g]
                for h in range(len(cs)):
                    term = m * reacts[h][g]
                    accs[h] = term if accs[h] is None else accs[h] + term
            for h, c in enumerate(cs):
                c_w = pl.multiple_of(c - LANE, LANE)
                c_e = pl.multiple_of(c + LANE, LANE)
                v = src[f, pl.ds(r, SUB), pl.ds(c, LANE)]
                up = src[f, pl.ds(r_up, SUB), pl.ds(c, LANE)]
                down = src[f, pl.ds(r_dn, SUB), pl.ds(c, LANE)]
                west = src[f, pl.ds(r, SUB), pl.ds(c_w, LANE)]
                east = src[f, pl.ds(r, SUB), pl.ds(c_e, LANE)]
                backward = jnp.where(first_sub, pltpu.roll(up, 1, 0), pltpu.roll(v, 1, 0))
                forward = jnp.where(last_sub, pltpu.roll(down, SUB - 1, 0), pltpu.roll(v, SUB - 1, 0))
                left = jnp.where(first_lane, pltpu.roll(west, 1, 1), pltpu.roll(v, 1, 1))
                rgt = jnp.where(last_lane, pltpu.roll(east, LANE - 1, 1), pltpu.roll(v, LANE - 1, 1))
                advect = -courant * (v - backward)
                spread = diffusion * (backward + forward + left + rgt - 4.0 * v)
                tends[h].append((v, advect + spread + source_step * accs[h]))
        return tends

    pair = 2 if n_j % 2 == 0 else 1
    n_jp = n_j // pair

    def tile_offsets(t):
        i = t // n_jp
        jp = t % n_jp
        r0 = pl.multiple_of(i * SUB, SUB)
        c0s = [pl.multiple_of((jp * pair + h) * LANE, LANE) for h in range(pair)]
        return r0, c0s

    def stage_one(t, carry):
        r0, c0s = tile_offsets(t)
        rate_ts = [rate_ref[pl.ds(r0, SUB), pl.ds(c0, LANE)] for c0 in c0s]
        tends = tendency_tiles(ext1, r0, c0s, rate_ts)
        r = pl.multiple_of(r0 + SUB, SUB)
        for c0, tend in zip(c0s, tends):
            c = pl.multiple_of(c0 + LANE, LANE)
            for f in range(nf):
                v, tf = tend[f]
                ext2[f, pl.ds(r, SUB), pl.ds(c, LANE)] = v + tf
        return carry

    lax.fori_loop(0, n_i * n_jp, stage_one, 0)

    high_ghost(ext2, lambda f: jnp.zeros((1, lanes), jnp.float32))

    def stage_two(t, carry):
        r0, c0s = tile_offsets(t)
        rate_ts = [rate_ref[pl.ds(r0, SUB), pl.ds(c0, LANE)] for c0 in c0s]
        tends = tendency_tiles(ext2, r0, c0s, rate_ts)
        r = pl.multiple_of(r0 + SUB, SUB)
        for c0, tend in zip(c0s, tends):
            c = pl.multiple_of(c0 + LANE, LANE)
            for f in range(nf):
                v, tf = tend[f]
                base = ext1[f, pl.ds(r, SUB), pl.ds(c, LANE)]
                out_ref[f, pl.ds(r0, SUB), pl.ds(c0, LANE)] = 0.5 * (base + v + tf)
        return carry

    lax.fori_loop(0, n_i * n_jp, stage_two, 0)

    for f in range(nf):
        elo_ref[f:f + 1, :] = ext2[f, SUB:SUB + 1, LANE:right]
        ehi_ref[f:f + 1, :] = ext2[f, top - 1:top, LANE:right]
        west = jnp.transpose(ext2[f, SUB:top, LANE:2 * LANE])
        east = jnp.transpose(ext2[f, SUB:top, right - LANE:right])
        clo_ref[f:f + 1, :] = west[0:1, :]
        chi_ref[f:f + 1, :] = east[LANE - 1:LANE, :]


def fused_step(fields, rate, mix, act, flags, halo_lo, halo_hi, swapped, lft, rgt):
    nf, rows, lanes = fields.shape
    vmem = pltpu.VMEM
    smem = pl.BlockSpec(memory_space=pltpu.SMEM)
    vspec = pl.BlockSpec(memory_space=vmem)
    cells = rows * lanes
    cost = pl.CostEstimate(
        flops=2 * cells * nf * (2 * nf + 24),
        transcendentals=2 * cells * (nf + 3),
        bytes_accessed=4 * cells * (2 * nf + 1),
    )
    return pl.pallas_call(
        functools.partial(step_kernel, nf, rows, lanes),
        out_shape=(
            jax.ShapeDtypeStruct((nf, rows, lanes), jnp.float32),
            jax.ShapeDtypeStruct((nf, lanes), jnp.float32),
            jax.ShapeDtypeStruct((nf, lanes), jnp.float32),
            jax.ShapeDtypeStruct((nf, rows), jnp.float32),
            jax.ShapeDtypeStruct((nf, rows), jnp.float32),
        ),
        in_specs=[smem, smem, smem, pl.BlockSpec(memory_space=pl.ANY)] + [vspec] * 6,
        out_specs=(vspec,) * 5,
        scratch_shapes=[
            vmem((nf, rows + 2 * SUB, lanes + 2 * LANE), jnp.float32),
            vmem((nf, rows + 2 * SUB, lanes + 2 * LANE), jnp.float32),
            vmem((nf * nf + nf, SUB, LANE), jnp.float32),
            pltpu.SemaphoreType.DMA((1,)),
        ],
        compiler_params=pltpu.CompilerParams(vmem_limit_bytes=60 * 1024 * 1024),
        cost_estimate=cost,
    )(mix, act, flags, fields, rate, halo_lo, halo_hi, swapped, lft, rgt)


def interp_kernel(ks, flag_s, ids_s, w_s, table_ref, o_ref, acc):
    lanes = o_ref.shape[1]
    half = jnp.where(flag_s[0] > 0.5, 0, ks)
    acc[...] = jnp.zeros(acc.shape, jnp.float32)
    width = table_ref.shape[1]

    @pl.when(flag_s[0] + flag_s[1] > 0.5)
    def _():
        def body(p, carry):
            total = None
            for k in range(ks):
                q = ids_s[half + k, p]
                term = w_s[half + k, p] * table_ref[pl.ds(q, 1), :]
                total = term if total is None else total + term
            acc[pl.ds(p, 1), 0:width] = total
            return carry

        lax.fori_loop(0, lanes, body, 0, unroll=8)

    o_ref[...] = jnp.transpose(acc[...])[0:o_ref.shape[0], :]


def interpolate(flags, ids, weights, table):
    ks2, lanes = ids.shape
    smem = pl.BlockSpec(memory_space=pltpu.SMEM)
    vspec = pl.BlockSpec(memory_space=pltpu.VMEM)
    return pl.pallas_call(
        functools.partial(interp_kernel, ks2 // 2),
        out_shape=jax.ShapeDtypeStruct((table.shape[1], lanes), jnp.float32),
        in_specs=[smem, smem, smem, vspec],
        out_specs=vspec,
        scratch_shapes=[pltpu.VMEM((lanes, LANE), jnp.float32)],
    )(flags, ids, weights, table)


def fix_kernel(low_w, side_w, out_in, g0_ref, g1_ref, gl_ref, gr_ref, out_ref, rb, cb, sem):
    nf, rows, lanes = out_ref.shape
    row_win = (pl.ds(0, SUB), pl.ds(rows - SUB, SUB))
    col_win = (pl.ds(0, LANE), pl.ds(lanes - LANE, LANE))
    loads = [pltpu.make_async_copy(out_ref.at[:, row_win[s], :], rb.at[s], sem.at[s]) for s in range(2)]
    for c in loads:
        c.start()
    for c in loads:
        c.wait()
    for f in range(nf):
        rb[0, f, 0:1, :] = rb[0, f, 0:1, :] + low_w * g0_ref[f:f + 1, :]
        rb[1, f, SUB - 1:SUB, :] = rb[1, f, SUB - 1:SUB, :] + side_w * g1_ref[f:f + 1, :]
    stores = [pltpu.make_async_copy(rb.at[s], out_ref.at[:, row_win[s], :], sem.at[s]) for s in range(2)]
    for c in stores:
        c.start()
    for c in stores:
        c.wait()
    loads = [pltpu.make_async_copy(out_ref.at[:, :, col_win[s]], cb.at[s], sem.at[s]) for s in range(2)]
    for c in loads:
        c.start()
    for c in loads:
        c.wait()
    lane_id = lax.broadcasted_iota(jnp.int32, (rows, LANE), 1)
    for f in range(nf):
        cb[0, f] = cb[0, f] + jnp.where(lane_id == 0, side_w * tile_t(gl_ref[f:f + 1, :]), 0.0)
        cb[1, f] = cb[1, f] + jnp.where(lane_id == LANE - 1, side_w * tile_t(gr_ref[f:f + 1, :]), 0.0)
    stores = [pltpu.make_async_copy(cb.at[s], out_ref.at[:, :, col_win[s]], sem.at[s]) for s in range(2)]
    for c in stores:
        c.start()
    for c in stores:
        c.wait()


def fix_edges(out, g0, g1, gl, gr, low_w, side_w):
    nf, rows, lanes = out.shape
    vspec = pl.BlockSpec(memory_space=pltpu.VMEM)
    anyspec = pl.BlockSpec(memory_space=pl.ANY)
    return pl.pallas_call(
        functools.partial(fix_kernel, low_w, side_w),
        out_shape=jax.ShapeDtypeStruct(out.shape, jnp.float32),
        in_specs=[anyspec, vspec, vspec, vspec, vspec],
        out_specs=anyspec,
        scratch_shapes=[
            pltpu.VMEM((2, nf, SUB, lanes), jnp.float32),
            pltpu.VMEM((2, nf, rows, LANE), jnp.float32),
            pltpu.SemaphoreType.DMA((2,)),
        ],
        input_output_aliases={0: 0},
    )(out, g0, g1, gl, gr)


def shards(
    fields, react_rate, mix_matrix, activation, inlet_ids, inlet_weights, outlet_ids, outlet_weights
):
    nf, rows, lanes = fields.shape
    n_grp = lax.axis_size("grp")
    n_blk = lax.axis_size("blk")
    g = lax.axis_index("grp")
    b = lax.axis_index("blk")
    exit_grp = n_grp - 2
    turb_grp = n_grp - 1
    flags = jnp.stack([g == exit_grp, g == turb_grp]).astype(jnp.float32)

    last_row = fields[:, -1, :]
    first_row = fields[:, 0, :]
    payload = jnp.concatenate([last_row, first_row[4:5]], axis=0)
    planes = payload[None]
    span = 1
    while span < n_blk:
        partner = [(i, i ^ span) for i in range(n_blk)]
        planes = jnp.concatenate([planes, lax.ppermute(planes, "blk", partner)], axis=0)
        span *= 2
    table = jnp.transpose(planes, (0, 2, 1)).reshape(n_blk * lanes, nf + 1)
    ids = jnp.concatenate([inlet_ids, outlet_ids], axis=0)
    ids = (jnp.bitwise_xor(ids // lanes, b) * lanes) + ids % lanes
    wts = jnp.concatenate([inlet_weights, outlet_weights], axis=0)
    swap = interpolate(flags, ids, wts, table)
    swapped = lax.ppermute(swap, "grp", [(exit_grp, turb_grp), (turb_grp, exit_grp)])

    halo_lo = lax.ppermute(last_row, "grp", [(i, i + 1) for i in range(n_grp - 2)])
    halo_hi = lax.ppermute(first_row, "grp", [(i + 1, i) for i in range(n_grp - 2)])
    lft = lax.ppermute(fields[:, :, lanes - 1], "blk", [(i, (i + 1) % n_blk) for i in range(n_blk)])
    rgt = lax.ppermute(fields[:, :, 0], "blk", [((i + 1) % n_blk, i) for i in range(n_blk)])

    out, elo, ehi, clo, chi = fused_step(
        fields, react_rate, mix_matrix, activation, flags, halo_lo, halo_hi, swapped, lft, rgt
    )

    g0 = lax.ppermute(ehi, "grp", [(i, i + 1) for i in range(n_grp - 2)])
    g1 = lax.ppermute(elo, "grp", [(i + 1, i) for i in range(n_grp - 2)])
    gl = lax.ppermute(chi, "blk", [(i, (i + 1) % n_blk) for i in range(n_blk)])
    gr = lax.ppermute(clo, "blk", [((i + 1) % n_blk, i) for i in range(n_blk)])
    low_w = 0.5 * (courant + diffusion)
    side_w = 0.5 * diffusion
    return fix_edges(out, g0, g1, gl, gr, low_w, side_w)


def solution(mesh):
    in_specs = (
        P(None, "grp", "blk"),
        P("grp", "blk"),
        P(),
        P(),
        P(None, "blk"),
        P(None, "blk"),
        P(None, "blk"),
        P(None, "blk"),
    )
    out_specs = P(None, "grp", "blk")
    return jax.shard_map(shards, mesh=mesh, in_specs=in_specs, out_specs=out_specs, check_vma=False)
```

```python
import functools

import jax
import jax.numpy as jnp
from jax import lax
from jax.experimental import pallas as pl
from jax.experimental.pallas import tpu as pltpu
from jax.sharding import PartitionSpec as P

courant = 0.5
diffusion = 0.1
source_step = 0.5

SUB = 8
LANE = 128


def tile_t(row):
    n = row.shape[1]
    return jnp.transpose(jnp.broadcast_to(row, (n, n)))


def step_kernel(nf, rows, lanes, mix_s, act_s, flag_s, f_hbm, rate_ref, hlo_ref, hhi_ref, sw_ref,
                lft_ref, rgt_ref, out_ref, elo_ref, ehi_ref, clo_ref, chi_ref, ext1, ext2, coef, sem):
    n_i = rows // SUB
    n_j = lanes // LANE
    top = SUB + rows
    right = LANE + lanes
    at_exit = flag_s[0] > 0.5
    at_turb = flag_s[1] > 0.5
    at_end = flag_s[0] + flag_s[1] > 0.5

    copy = pltpu.make_async_copy(f_hbm, ext1.at[:, SUB:top, LANE:right], sem.at[0])
    copy.start()
    zeros = jnp.zeros((rows, LANE), jnp.float32)
    for f in range(nf):
        inlet = sw_ref[f:f + 1, :]
        ext1[f, SUB - 1:SUB, LANE:right] = jnp.where(at_turb, inlet, hlo_ref[f:f + 1, :])
        ext2[f, SUB - 1:SUB, LANE:right] = jnp.where(at_turb, inlet, 0.0)
        ext1[f, SUB:top, 0:LANE] = tile_t(lft_ref[f:f + 1, :])
        ext1[f, SUB:top, right:right + LANE] = tile_t(rgt_ref[f:f + 1, :])
        ext2[f, SUB:top, 0:LANE] = zeros
        ext2[f, SUB:top, right:right + LANE] = zeros
    for f in range(nf):
        for g in range(nf):
            coef[f * nf + g] = jnp.full((SUB, LANE), mix_s[f, g], jnp.float32)
        coef[nf * nf + f] = jnp.full((SUB, LANE), -act_s[f], jnp.float32)
    copy.wait()

    def high_ghost(ext, halo_of):
        for f in range(nf):
            own = ext[f, top - 1:top, LANE:right]
            halo = halo_of(f)
            if f == 4:
                row = jnp.where(at_turb, own, jnp.where(at_exit, sw_ref[nf:nf + 1, :], halo))
            else:
                row = jnp.where(at_end, own, halo)
            ext[f, top:top + 1, LANE:right] = row

    high_ghost(ext1, lambda f: hhi_ref[f:f + 1, :])

    sub_id = lax.broadcasted_iota(jnp.int32, (SUB, LANE), 0)
    lane_id = lax.broadcasted_iota(jnp.int32, (SUB, LANE), 1)
    first_sub = sub_id == 0
    last_sub = sub_id == SUB - 1
    first_lane = lane_id == 0
    last_lane = lane_id == LANE - 1

    def tendency_tiles(src, r0, c0s, rate_ts):
        r = pl.multiple_of(r0 + SUB, SUB)
        r_up = pl.multiple_of(r0, SUB)
        r_dn = pl.multiple_of(r0 + 2 * SUB, SUB)
        cs = [pl.multiple_of(c0 + LANE, LANE) for c0 in c0s]
        reacts = []
        for c, rate_t in zip(cs, rate_ts):
            v4 = src[4, pl.ds(r, SUB), pl.ds(c, LANE)]
            heat = 1.0 + (jnp.maximum(v4, 0.0) + jnp.log1p(jnp.exp(-jnp.abs(v4))))
            inv_heat = 1.0 / heat
            reacts.append([
                rate_t * src[f, pl.ds(r, SUB), pl.ds(c, LANE)] * jnp.exp(coef[nf * nf + f] * inv_heat)
                for f in range(nf)
            ])
        tends = [[] for _ in cs]
        for f in range(nf):
            accs = [None] * len(cs)
            for g in range(nf):
                m = coef[f * nf + g]
                for h in range(len(cs)):
                    term = m * reacts[h][g]
                    accs[h] = term if accs[h] is None else accs[h] + term
            for h, c in enumerate(cs):
                c_w = pl.multiple_of(c - LANE, LANE)
                c_e = pl.multiple_of(c + LANE, LANE)
                v = src[f, pl.ds(r, SUB), pl.ds(c, LANE)]
                up = src[f, pl.ds(r_up, SUB), pl.ds(c, LANE)]
                down = src[f, pl.ds(r_dn, SUB), pl.ds(c, LANE)]
                west = src[f, pl.ds(r, SUB), pl.ds(c_w, LANE)]
                east = src[f, pl.ds(r, SUB), pl.ds(c_e, LANE)]
                backward = jnp.where(first_sub, pltpu.roll(up, 1, 0), pltpu.roll(v, 1, 0))
                forward = jnp.where(last_sub, pltpu.roll(down, SUB - 1, 0), pltpu.roll(v, SUB - 1, 0))
                left = jnp.where(first_lane, pltpu.roll(west, 1, 1), pltpu.roll(v, 1, 1))
                rgt = jnp.where(last_lane, pltpu.roll(east, LANE - 1, 1), pltpu.roll(v, LANE - 1, 1))
                advect = -courant * (v - backward)
                spread = diffusion * (backward + forward + left + rgt - 4.0 * v)
                tends[h].append((v, advect + spread + source_step * accs[h]))
        return tends

    pair = 2 if n_j % 2 == 0 else 1
    n_jp = n_j // pair

    def tile_offsets(t):
        i = t // n_jp
        jp = t % n_jp
        r0 = pl.multiple_of(i * SUB, SUB)
        c0s = [pl.multiple_of((jp * pair + h) * LANE, LANE) for h in range(pair)]
        return r0, c0s

    def stage_one(t, carry):
        r0, c0s = tile_offsets(t)
        rate_ts = [rate_ref[pl.ds(r0, SUB), pl.ds(c0, LANE)] for c0 in c0s]
        tends = tendency_tiles(ext1, r0, c0s, rate_ts)
        r = pl.multiple_of(r0 + SUB, SUB)
        for c0, tend in zip(c0s, tends):
            c = pl.multiple_of(c0 + LANE, LANE)
            for f in range(nf):
                v, tf = tend[f]
                ext2[f, pl.ds(r, SUB), pl.ds(c, LANE)] = v + tf
        return carry

    lax.fori_loop(0, n_i * n_jp, stage_one, 0)

    high_ghost(ext2, lambda f: jnp.zeros((1, lanes), jnp.float32))

    def stage_two(t, carry):
        r0, c0s = tile_offsets(t)
        rate_ts = [rate_ref[pl.ds(r0, SUB), pl.ds(c0, LANE)] for c0 in c0s]
        tends = tendency_tiles(ext2, r0, c0s, rate_ts)
        r = pl.multiple_of(r0 + SUB, SUB)
        for c0, tend in zip(c0s, tends):
            c = pl.multiple_of(c0 + LANE, LANE)
            for f in range(nf):
                v, tf = tend[f]
                base = ext1[f, pl.ds(r, SUB), pl.ds(c, LANE)]
                out_ref[f, pl.ds(r0, SUB), pl.ds(c0, LANE)] = 0.5 * (base + v + tf)
        return carry

    lax.fori_loop(0, n_i * n_jp, stage_two, 0)

    for f in range(nf):
        elo_ref[f:f + 1, :] = ext2[f, SUB:SUB + 1, LANE:right]
        ehi_ref[f:f + 1, :] = ext2[f, top - 1:top, LANE:right]
        west = jnp.transpose(ext2[f, SUB:top, LANE:2 * LANE])
        east = jnp.transpose(ext2[f, SUB:top, right - LANE:right])
        clo_ref[f:f + 1, :] = west[0:1, :]
        chi_ref[f:f + 1, :] = east[LANE - 1:LANE, :]


def fused_step(fields, rate, mix, act, flags, halo_lo, halo_hi, swapped, lft, rgt):
    nf, rows, lanes = fields.shape
    vmem = pltpu.VMEM
    smem = pl.BlockSpec(memory_space=pltpu.SMEM)
    vspec = pl.BlockSpec(memory_space=vmem)
    cells = rows * lanes
    cost = pl.CostEstimate(
        flops=2 * cells * nf * (2 * nf + 24),
        transcendentals=2 * cells * (nf + 3),
        bytes_accessed=4 * cells * (2 * nf + 1),
    )
    return pl.pallas_call(
        functools.partial(step_kernel, nf, rows, lanes),
        out_shape=(
            jax.ShapeDtypeStruct((nf, rows, lanes), jnp.float32),
            jax.ShapeDtypeStruct((nf, lanes), jnp.float32),
            jax.ShapeDtypeStruct((nf, lanes), jnp.float32),
            jax.ShapeDtypeStruct((nf, rows), jnp.float32),
            jax.ShapeDtypeStruct((nf, rows), jnp.float32),
        ),
        in_specs=[smem, smem, smem, pl.BlockSpec(memory_space=pl.ANY)] + [vspec] * 6,
        out_specs=(vspec,) * 5,
        scratch_shapes=[
            vmem((nf, rows + 2 * SUB, lanes + 2 * LANE), jnp.float32),
            vmem((nf, rows + 2 * SUB, lanes + 2 * LANE), jnp.float32),
            vmem((nf * nf + nf, SUB, LANE), jnp.float32),
            pltpu.SemaphoreType.DMA((1,)),
        ],
        compiler_params=pltpu.CompilerParams(vmem_limit_bytes=60 * 1024 * 1024),
        cost_estimate=cost,
    )(mix, act, flags, fields, rate, halo_lo, halo_hi, swapped, lft, rgt)


def interp_kernel(ks, flag_s, ids_s, w_s, table_ref, *refs):
    n_pass = (len(refs) - 2) // 2
    ins, o_ref, outs, acc = refs[:n_pass], refs[n_pass], refs[n_pass + 1:-1], refs[-1]
    lanes = o_ref.shape[1]
    half = jnp.where(flag_s[0] > 0.5, 0, ks)
    acc[...] = jnp.zeros(acc.shape, jnp.float32)
    width = table_ref.shape[1]

    @pl.when(flag_s[0] + flag_s[1] > 0.5)
    def _():
        def body(p, carry):
            total = None
            for k in range(ks):
                q = ids_s[half + k, p]
                term = w_s[half + k, p] * table_ref[pl.ds(q, 1), :]
                total = term if total is None else total + term
            acc[pl.ds(p, 1), 0:width] = total
            return carry

        lax.fori_loop(0, lanes, body, 0, unroll=8)

    o_ref[...] = jnp.transpose(acc[...])[0:o_ref.shape[0], :]
    for src, dst in zip(ins, outs):
        dst[...] = src[...]


def interpolate(flags, ids, weights, table, passed):
    ks2, lanes = ids.shape
    smem = pl.BlockSpec(memory_space=pltpu.SMEM)
    vspec = pl.BlockSpec(memory_space=pltpu.VMEM)
    return pl.pallas_call(
        functools.partial(interp_kernel, ks2 // 2),
        out_shape=(jax.ShapeDtypeStruct((table.shape[1], lanes), jnp.float32),)
        + tuple(jax.ShapeDtypeStruct(x.shape, x.dtype) for x in passed),
        in_specs=[smem, smem, smem] + [vspec] * (1 + len(passed)),
        out_specs=(vspec,) * (1 + len(passed)),
        scratch_shapes=[pltpu.VMEM((lanes, LANE), jnp.float32)],
    )(flags, ids, weights, table, *passed)


def fix_kernel(low_w, side_w, out_in, g0_ref, g1_ref, gl_ref, gr_ref, out_ref, rb, cb, sem):
    nf, rows, lanes = out_ref.shape
    mid = rows - 2 * SUB
    wins = [
        (out_ref.at[:, pl.ds(0, SUB), :], rb.at[0]),
        (out_ref.at[:, pl.ds(rows - SUB, SUB), :], rb.at[1]),
        (out_ref.at[:, pl.ds(SUB, mid), pl.ds(0, LANE)], cb.at[0]),
        (out_ref.at[:, pl.ds(SUB, mid), pl.ds(lanes - LANE, LANE)], cb.at[1]),
    ]
    loads = [pltpu.make_async_copy(hbm, buf, sem.at[s]) for s, (hbm, buf) in enumerate(wins)]
    for c in loads:
        c.start()
    for c in loads:
        c.wait()
    lane_id = lax.broadcasted_iota(jnp.int32, (rows, LANE), 1)
    row_lane = lax.broadcasted_iota(jnp.int32, (SUB, LANE), 1)
    for f in range(nf):
        west = jnp.where(lane_id == 0, side_w * tile_t(gl_ref[f:f + 1, :]), 0.0)
        east = jnp.where(lane_id == LANE - 1, side_w * tile_t(gr_ref[f:f + 1, :]), 0.0)
        cb[0, f] = cb[0, f] + west[SUB:rows - SUB]
        cb[1, f] = cb[1, f] + east[SUB:rows - SUB]
        for s, lo in ((0, 0), (1, rows - SUB)):
            rb[s, f, :, 0:LANE] = rb[s, f, :, 0:LANE] + west[lo:lo + SUB]
            rb[s, f, :, lanes - LANE:lanes] = rb[s, f, :, lanes - LANE:lanes] + east[lo:lo + SUB]
        rb[0, f, 0:1, :] = rb[0, f, 0:1, :] + low_w * g0_ref[f:f + 1, :]
        rb[1, f, SUB - 1:SUB, :] = rb[1, f, SUB - 1:SUB, :] + side_w * g1_ref[f:f + 1, :]
    stores = [pltpu.make_async_copy(buf, hbm, sem.at[s]) for s, (hbm, buf) in enumerate(wins)]
    for c in stores:
        c.start()
    for c in stores:
        c.wait()


def fix_edges(out, g0, g1, gl, gr, low_w, side_w):
    nf, rows, lanes = out.shape
    vspec = pl.BlockSpec(memory_space=pltpu.VMEM)
    anyspec = pl.BlockSpec(memory_space=pl.ANY)
    return pl.pallas_call(
        functools.partial(fix_kernel, low_w, side_w),
        out_shape=jax.ShapeDtypeStruct(out.shape, jnp.float32),
        in_specs=[anyspec, vspec, vspec, vspec, vspec],
        out_specs=anyspec,
        scratch_shapes=[
            pltpu.VMEM((2, nf, SUB, lanes), jnp.float32),
            pltpu.VMEM((2, nf, rows - 2 * SUB, LANE), jnp.float32),
            pltpu.SemaphoreType.DMA((4,)),
        ],
        input_output_aliases={0: 0},
    )(out, g0, g1, gl, gr)


def shards(
    fields, react_rate, mix_matrix, activation, inlet_ids, inlet_weights, outlet_ids, outlet_weights
):
    nf, rows, lanes = fields.shape
    n_grp = lax.axis_size("grp")
    n_blk = lax.axis_size("blk")
    g = lax.axis_index("grp")
    b = lax.axis_index("blk")
    exit_grp = n_grp - 2
    turb_grp = n_grp - 1
    flags = jnp.stack([g == exit_grp, g == turb_grp]).astype(jnp.float32)

    last_row = fields[:, -1, :]
    first_row = fields[:, 0, :]
    payload = jnp.concatenate([last_row, first_row[4:5]], axis=0)
    planes = payload[None]
    span = 1
    while span < n_blk:
        partner = [(i, i ^ span) for i in range(n_blk)]
        planes = jnp.concatenate([planes, lax.ppermute(planes, "blk", partner)], axis=0)
        span *= 2
    table = jnp.transpose(planes, (0, 2, 1)).reshape(n_blk * lanes, nf + 1)
    ids = jnp.concatenate([inlet_ids, outlet_ids], axis=0)
    ids = (jnp.bitwise_xor(ids // lanes, b) * lanes) + ids % lanes
    wts = jnp.concatenate([inlet_weights, outlet_weights], axis=0)
    halo_lo = lax.ppermute(last_row, "grp", [(i, i + 1) for i in range(n_grp - 2)])
    halo_hi = lax.ppermute(first_row, "grp", [(i + 1, i) for i in range(n_grp - 2)])
    lft = lax.ppermute(fields[:, :, lanes - 1], "blk", [(i, (i + 1) % n_blk) for i in range(n_blk)])
    rgt = lax.ppermute(fields[:, :, 0], "blk", [((i + 1) % n_blk, i) for i in range(n_blk)])

    swap, halo_lo, halo_hi, lft, rgt = interpolate(flags, ids, wts, table, (halo_lo, halo_hi, lft, rgt))
    swapped = lax.ppermute(swap, "grp", [(exit_grp, turb_grp), (turb_grp, exit_grp)])

    out, elo, ehi, clo, chi = fused_step(
        fields, react_rate, mix_matrix, activation, flags, halo_lo, halo_hi, swapped, lft, rgt
    )

    g0 = lax.ppermute(ehi, "grp", [(i, i + 1) for i in range(n_grp - 2)])
    g1 = lax.ppermute(elo, "grp", [(i + 1, i) for i in range(n_grp - 2)])
    gl = lax.ppermute(chi, "blk", [(i, (i + 1) % n_blk) for i in range(n_blk)])
    gr = lax.ppermute(clo, "blk", [((i + 1) % n_blk, i) for i in range(n_blk)])
    low_w = 0.5 * (courant + diffusion)
    side_w = 0.5 * diffusion
    return fix_edges(out, g0, g1, gl, gr, low_w, side_w)


def solution(mesh):
    in_specs = (
        P(None, "grp", "blk"),
        P("grp", "blk"),
        P(),
        P(),
        P(None, "blk"),
        P(None, "blk"),
        P(None, "blk"),
        P(None, "blk"),
    )
    out_specs = P(None, "grp", "blk")
    return jax.shard_map(shards, mesh=mesh, in_specs=in_specs, out_specs=out_specs, check_vma=False)
```

```python
import functools

import jax
import jax.numpy as jnp
from jax import lax
from jax.experimental import pallas as pl
from jax.experimental.pallas import tpu as pltpu
from jax.sharding import PartitionSpec as P

courant = 0.5
diffusion = 0.1
source_step = 0.5

SUB = 8
LANE = 128


def tile_t(row):
    n = row.shape[1]
    return jnp.transpose(jnp.broadcast_to(row, (n, n)))


def step_kernel(nf, rows, lanes, mix_s, act_s, flag_s, f_hbm, rate_ref, hlo_ref, hhi_ref, sw_ref,
                lft_ref, rgt_ref, out_ref, elo_ref, ehi_ref, clo_ref, chi_ref, ext1, ext2, coef, sem):
    n_i = rows // SUB
    n_j = lanes // LANE
    top = SUB + rows
    right = LANE + lanes
    at_exit = flag_s[0] > 0.5
    at_turb = flag_s[1] > 0.5
    at_end = flag_s[0] + flag_s[1] > 0.5

    copy = pltpu.make_async_copy(f_hbm, ext1.at[:, SUB:top, LANE:right], sem.at[0])
    copy.start()
    zeros = jnp.zeros((rows, LANE), jnp.float32)
    for f in range(nf):
        inlet = sw_ref[f:f + 1, :]
        ext1[f, SUB - 1:SUB, LANE:right] = jnp.where(at_turb, inlet, hlo_ref[f:f + 1, :])
        ext2[f, SUB - 1:SUB, LANE:right] = jnp.where(at_turb, inlet, 0.0)
        ext1[f, SUB:top, 0:LANE] = tile_t(lft_ref[f:f + 1, :])
        ext1[f, SUB:top, right:right + LANE] = tile_t(rgt_ref[f:f + 1, :])
        ext2[f, SUB:top, 0:LANE] = zeros
        ext2[f, SUB:top, right:right + LANE] = zeros
    for f in range(nf):
        for g in range(nf):
            coef[f * nf + g] = jnp.full((SUB, LANE), mix_s[f, g], jnp.float32)
        coef[nf * nf + f] = jnp.full((SUB, LANE), -act_s[f], jnp.float32)
    copy.wait()

    def high_ghost(ext, halo_of):
        for f in range(nf):
            own = ext[f, top - 1:top, LANE:right]
            halo = halo_of(f)
            if f == 4:
                row = jnp.where(at_turb, own, jnp.where(at_exit, sw_ref[nf:nf + 1, :], halo))
            else:
                row = jnp.where(at_end, own, halo)
            ext[f, top:top + 1, LANE:right] = row

    high_ghost(ext1, lambda f: hhi_ref[f:f + 1, :])

    sub_id = lax.broadcasted_iota(jnp.int32, (SUB, LANE), 0)
    lane_id = lax.broadcasted_iota(jnp.int32, (SUB, LANE), 1)
    first_sub = sub_id == 0
    last_sub = sub_id == SUB - 1
    first_lane = lane_id == 0
    last_lane = lane_id == LANE - 1

    def tendency_tiles(src, r0, c0s, rate_ts):
        r = pl.multiple_of(r0 + SUB, SUB)
        r_up = pl.multiple_of(r0, SUB)
        r_dn = pl.multiple_of(r0 + 2 * SUB, SUB)
        cs = [pl.multiple_of(c0 + LANE, LANE) for c0 in c0s]
        reacts = []
        for c, rate_t in zip(cs, rate_ts):
            v4 = src[4, pl.ds(r, SUB), pl.ds(c, LANE)]
            heat = 1.0 + (jnp.maximum(v4, 0.0) + jnp.log1p(jnp.exp(-jnp.abs(v4))))
            inv_heat = 1.0 / heat
            reacts.append([
                rate_t * src[f, pl.ds(r, SUB), pl.ds(c, LANE)] * jnp.exp(coef[nf * nf + f] * inv_heat)
                for f in range(nf)
            ])
        tends = [[] for _ in cs]
        for f in range(nf):
            accs = [None] * len(cs)
            for g in range(nf):
                m = coef[f * nf + g]
                for h in range(len(cs)):
                    term = m * reacts[h][g]
                    accs[h] = term if accs[h] is None else accs[h] + term
            for h, c in enumerate(cs):
                c_w = pl.multiple_of(c - LANE, LANE)
                c_e = pl.multiple_of(c + LANE, LANE)
                v = src[f, pl.ds(r, SUB), pl.ds(c, LANE)]
                up = src[f, pl.ds(r_up, SUB), pl.ds(c, LANE)]
                down = src[f, pl.ds(r_dn, SUB), pl.ds(c, LANE)]
                west = src[f, pl.ds(r, SUB), pl.ds(c_w, LANE)]
                east = src[f, pl.ds(r, SUB), pl.ds(c_e, LANE)]
                backward = jnp.where(first_sub, pltpu.roll(up, 1, 0), pltpu.roll(v, 1, 0))
                forward = jnp.where(last_sub, pltpu.roll(down, SUB - 1, 0), pltpu.roll(v, SUB - 1, 0))
                left = jnp.where(first_lane, pltpu.roll(west, 1, 1), pltpu.roll(v, 1, 1))
                rgt = jnp.where(last_lane, pltpu.roll(east, LANE - 1, 1), pltpu.roll(v, LANE - 1, 1))
                flow = (courant + diffusion) * backward + diffusion * (forward + left + rgt)
                flow = flow - (courant + 4.0 * diffusion) * v
                tends[h].append((v, flow + source_step * accs[h]))
        return tends

    pair = 2 if n_j % 2 == 0 else 1
    n_jp = n_j // pair

    def tile_offsets(t):
        i = t // n_jp
        jp = t % n_jp
        r0 = pl.multiple_of(i * SUB, SUB)
        c0s = [pl.multiple_of((jp * pair + h) * LANE, LANE) for h in range(pair)]
        return r0, c0s

    def stage_one(t, carry):
        r0, c0s = tile_offsets(t)
        rate_ts = [rate_ref[pl.ds(r0, SUB), pl.ds(c0, LANE)] for c0 in c0s]
        tends = tendency_tiles(ext1, r0, c0s, rate_ts)
        r = pl.multiple_of(r0 + SUB, SUB)
        for c0, tend in zip(c0s, tends):
            c = pl.multiple_of(c0 + LANE, LANE)
            for f in range(nf):
                v, tf = tend[f]
                ext2[f, pl.ds(r, SUB), pl.ds(c, LANE)] = v + tf
        return carry

    lax.fori_loop(0, n_i * n_jp, stage_one, 0)

    high_ghost(ext2, lambda f: jnp.zeros((1, lanes), jnp.float32))

    def stage_two(t, carry):
        r0, c0s = tile_offsets(t)
        rate_ts = [rate_ref[pl.ds(r0, SUB), pl.ds(c0, LANE)] for c0 in c0s]
        tends = tendency_tiles(ext2, r0, c0s, rate_ts)
        r = pl.multiple_of(r0 + SUB, SUB)
        for c0, tend in zip(c0s, tends):
            c = pl.multiple_of(c0 + LANE, LANE)
            for f in range(nf):
                v, tf = tend[f]
                base = ext1[f, pl.ds(r, SUB), pl.ds(c, LANE)]
                out_ref[f, pl.ds(r0, SUB), pl.ds(c0, LANE)] = 0.5 * (base + v + tf)
        return carry

    lax.fori_loop(0, n_i * n_jp, stage_two, 0)

    for f in range(nf):
        elo_ref[f:f + 1, :] = ext2[f, SUB:SUB + 1, LANE:right]
        ehi_ref[f:f + 1, :] = ext2[f, top - 1:top, LANE:right]
        west = jnp.transpose(ext2[f, SUB:top, LANE:2 * LANE])
        east = jnp.transpose(ext2[f, SUB:top, right - LANE:right])
        clo_ref[f:f + 1, :] = west[0:1, :]
        chi_ref[f:f + 1, :] = east[LANE - 1:LANE, :]


def fused_step(fields, rate, mix, act, flags, halo_lo, halo_hi, swapped, lft, rgt):
    nf, rows, lanes = fields.shape
    vmem = pltpu.VMEM
    smem = pl.BlockSpec(memory_space=pltpu.SMEM)
    vspec = pl.BlockSpec(memory_space=vmem)
    cells = rows * lanes
    cost = pl.CostEstimate(
        flops=2 * cells * nf * (2 * nf + 24),
        transcendentals=2 * cells * (nf + 3),
        bytes_accessed=4 * cells * (2 * nf + 1),
    )
    return pl.pallas_call(
        functools.partial(step_kernel, nf, rows, lanes),
        out_shape=(
            jax.ShapeDtypeStruct((nf, rows, lanes), jnp.float32),
            jax.ShapeDtypeStruct((nf, lanes), jnp.float32),
            jax.ShapeDtypeStruct((nf, lanes), jnp.float32),
            jax.ShapeDtypeStruct((nf, rows), jnp.float32),
            jax.ShapeDtypeStruct((nf, rows), jnp.float32),
        ),
        in_specs=[smem, smem, smem, pl.BlockSpec(memory_space=pl.ANY)] + [vspec] * 6,
        out_specs=(vspec,) * 5,
        scratch_shapes=[
            vmem((nf, rows + 2 * SUB, lanes + 2 * LANE), jnp.float32),
            vmem((nf, rows + 2 * SUB, lanes + 2 * LANE), jnp.float32),
            vmem((nf * nf + nf, SUB, LANE), jnp.float32),
            pltpu.SemaphoreType.DMA((1,)),
        ],
        compiler_params=pltpu.CompilerParams(vmem_limit_bytes=60 * 1024 * 1024),
        cost_estimate=cost,
    )(mix, act, flags, fields, rate, halo_lo, halo_hi, swapped, lft, rgt)


def interp_kernel(ks, flag_s, ids_s, w_s, table_ref, *refs):
    n_pass = (len(refs) - 2) // 2
    ins, o_ref, outs, acc = refs[:n_pass], refs[n_pass], refs[n_pass + 1:-1], refs[-1]
    lanes = o_ref.shape[1]
    half = jnp.where(flag_s[0] > 0.5, 0, ks)
    acc[...] = jnp.zeros(acc.shape, jnp.float32)
    width = table_ref.shape[1]

    @pl.when(flag_s[0] + flag_s[1] > 0.5)
    def _():
        def body(p, carry):
            total = None
            for k in range(ks):
                q = ids_s[half + k, p]
                term = w_s[half + k, p] * table_ref[pl.ds(q, 1), :]
                total = term if total is None else total + term
            acc[pl.ds(p, 1), 0:width] = total
            return carry

        lax.fori_loop(0, lanes, body, 0, unroll=8)

    o_ref[...] = jnp.transpose(acc[...])[0:o_ref.shape[0], :]
    for src, dst in zip(ins, outs):
        dst[...] = src[...]


def interpolate(flags, ids, weights, table, passed):
    ks2, lanes = ids.shape
    smem = pl.BlockSpec(memory_space=pltpu.SMEM)
    vspec = pl.BlockSpec(memory_space=pltpu.VMEM)
    return pl.pallas_call(
        functools.partial(interp_kernel, ks2 // 2),
        out_shape=(jax.ShapeDtypeStruct((table.shape[1], lanes), jnp.float32),)
        + tuple(jax.ShapeDtypeStruct(x.shape, x.dtype) for x in passed),
        in_specs=[smem, smem, smem] + [vspec] * (1 + len(passed)),
        out_specs=(vspec,) * (1 + len(passed)),
        scratch_shapes=[pltpu.VMEM((lanes, LANE), jnp.float32)],
    )(flags, ids, weights, table, *passed)


def fix_kernel(low_w, side_w, out_in, g0_ref, g1_ref, gl_ref, gr_ref, out_ref, rb, cb, sem):
    nf, rows, lanes = out_ref.shape
    mid = rows - 2 * SUB
    wins = [
        (out_ref.at[:, pl.ds(0, SUB), :], rb.at[0]),
        (out_ref.at[:, pl.ds(rows - SUB, SUB), :], rb.at[1]),
        (out_ref.at[:, pl.ds(SUB, mid), pl.ds(0, LANE)], cb.at[0]),
        (out_ref.at[:, pl.ds(SUB, mid), pl.ds(lanes - LANE, LANE)], cb.at[1]),
    ]
    loads = [pltpu.make_async_copy(hbm, buf, sem.at[s]) for s, (hbm, buf) in enumerate(wins)]
    for c in loads:
        c.start()
    for c in loads:
        c.wait()
    lane_id = lax.broadcasted_iota(jnp.int32, (rows, LANE), 1)
    row_lane = lax.broadcasted_iota(jnp.int32, (SUB, LANE), 1)
    for f in range(nf):
        west = jnp.where(lane_id == 0, side_w * tile_t(gl_ref[f:f + 1, :]), 0.0)
        east = jnp.where(lane_id == LANE - 1, side_w * tile_t(gr_ref[f:f + 1, :]), 0.0)
        cb[0, f] = cb[0, f] + west[SUB:rows - SUB]
        cb[1, f] = cb[1, f] + east[SUB:rows - SUB]
        for s, lo in ((0, 0), (1, rows - SUB)):
            rb[s, f, :, 0:LANE] = rb[s, f, :, 0:LANE] + west[lo:lo + SUB]
            rb[s, f, :, lanes - LANE:lanes] = rb[s, f, :, lanes - LANE:lanes] + east[lo:lo + SUB]
        rb[0, f, 0:1, :] = rb[0, f, 0:1, :] + low_w * g0_ref[f:f + 1, :]
        rb[1, f, SUB - 1:SUB, :] = rb[1, f, SUB - 1:SUB, :] + side_w * g1_ref[f:f + 1, :]
    stores = [pltpu.make_async_copy(buf, hbm, sem.at[s]) for s, (hbm, buf) in enumerate(wins)]
    for c in stores:
        c.start()
    for c in stores:
        c.wait()


def fix_edges(out, g0, g1, gl, gr, low_w, side_w):
    nf, rows, lanes = out.shape
    vspec = pl.BlockSpec(memory_space=pltpu.VMEM)
    anyspec = pl.BlockSpec(memory_space=pl.ANY)
    return pl.pallas_call(
        functools.partial(fix_kernel, low_w, side_w),
        out_shape=jax.ShapeDtypeStruct(out.shape, jnp.float32),
        in_specs=[anyspec, vspec, vspec, vspec, vspec],
        out_specs=anyspec,
        scratch_shapes=[
            pltpu.VMEM((2, nf, SUB, lanes), jnp.float32),
            pltpu.VMEM((2, nf, rows - 2 * SUB, LANE), jnp.float32),
            pltpu.SemaphoreType.DMA((4,)),
        ],
        input_output_aliases={0: 0},
    )(out, g0, g1, gl, gr)


def shards(
    fields, react_rate, mix_matrix, activation, inlet_ids, inlet_weights, outlet_ids, outlet_weights
):
    nf, rows, lanes = fields.shape
    n_grp = lax.axis_size("grp")
    n_blk = lax.axis_size("blk")
    g = lax.axis_index("grp")
    b = lax.axis_index("blk")
    exit_grp = n_grp - 2
    turb_grp = n_grp - 1
    flags = jnp.stack([g == exit_grp, g == turb_grp]).astype(jnp.float32)

    last_row = fields[:, -1, :]
    first_row = fields[:, 0, :]
    payload = jnp.concatenate([last_row, first_row[4:5]], axis=0)
    planes = [payload] + [
        lax.ppermute(payload, "blk", [(i, (i + d) % n_blk) for i in range(n_blk)])
        for d in range(1, n_blk)
    ]
    table = jnp.transpose(jnp.stack(planes), (0, 2, 1)).reshape(n_blk * lanes, nf + 1)
    ids = jnp.concatenate([inlet_ids, outlet_ids], axis=0)
    ids = ((b - ids // lanes) % n_blk) * lanes + ids % lanes
    wts = jnp.concatenate([inlet_weights, outlet_weights], axis=0)
    halo_lo = lax.ppermute(last_row, "grp", [(i, i + 1) for i in range(n_grp - 2)])
    halo_hi = lax.ppermute(first_row, "grp", [(i + 1, i) for i in range(n_grp - 2)])
    lft = lax.ppermute(fields[:, :, lanes - 1], "blk", [(i, (i + 1) % n_blk) for i in range(n_blk)])
    rgt = lax.ppermute(fields[:, :, 0], "blk", [((i + 1) % n_blk, i) for i in range(n_blk)])

    swap, halo_lo, halo_hi, lft, rgt = interpolate(flags, ids, wts, table, (halo_lo, halo_hi, lft, rgt))
    swapped = lax.ppermute(swap, "grp", [(exit_grp, turb_grp), (turb_grp, exit_grp)])

    out, elo, ehi, clo, chi = fused_step(
        fields, react_rate, mix_matrix, activation, flags, halo_lo, halo_hi, swapped, lft, rgt
    )

    g0 = lax.ppermute(ehi, "grp", [(i, i + 1) for i in range(n_grp - 2)])
    g1 = lax.ppermute(elo, "grp", [(i + 1, i) for i in range(n_grp - 2)])
    gl = lax.ppermute(chi, "blk", [(i, (i + 1) % n_blk) for i in range(n_blk)])
    gr = lax.ppermute(clo, "blk", [((i + 1) % n_blk, i) for i in range(n_blk)])
    low_w = 0.5 * (courant + diffusion)
    side_w = 0.5 * diffusion
    return fix_edges(out, g0, g1, gl, gr, low_w, side_w)


def solution(mesh):
    in_specs = (
        P(None, "grp", "blk"),
        P("grp", "blk"),
        P(),
        P(),
        P(None, "blk"),
        P(None, "blk"),
        P(None, "blk"),
        P(None, "blk"),
    )
    out_specs = P(None, "grp", "blk")
    return jax.shard_map(shards, mesh=mesh, in_specs=in_specs, out_specs=out_specs, check_vma=False)
```

```python
import functools

import jax
import jax.numpy as jnp
from jax import lax
from jax.experimental import pallas as pl
from jax.experimental.pallas import tpu as pltpu
from jax.sharding import PartitionSpec as P

courant = 0.5
diffusion = 0.1
source_step = 0.5

SUB = 8
LANE = 128


def tile_t(row):
    n = row.shape[1]
    return jnp.transpose(jnp.broadcast_to(row, (n, n)))


def step_kernel(nf, rows, lanes, phase, *refs):
    if phase == 0:
        mix_s, act_s, f_hbm, rate_ref, lft_ref, rgt_ref, first_ref, ext1, coef, sem = refs
    else:
        (mix_s, act_s, flag_s, f_hbm, p_hbm, rate_ref, hlo_ref, hhi_ref, sw_ref, lft_ref, rgt_ref,
         out_ref, elo_ref, ehi_ref, clo_ref, chi_ref, ext1, ext2, coef, sem) = refs
    n_i = rows // SUB
    n_j = lanes // LANE
    top = SUB + rows
    right = LANE + lanes

    copy = pltpu.make_async_copy(f_hbm, ext1.at[:, SUB:top, LANE:right], sem.at[0])
    copy.start()
    if phase == 1:
        part = pltpu.make_async_copy(p_hbm, ext2.at[:, SUB:top, LANE:right], sem.at[1])
        part.start()
        at_exit = flag_s[0] > 0.5
        at_turb = flag_s[1] > 0.5
        at_end = flag_s[0] + flag_s[1] > 0.5
    zeros = jnp.zeros((rows, LANE), jnp.float32)
    for f in range(nf):
        if phase == 1:
            inlet = sw_ref[f:f + 1, :]
            ext1[f, SUB - 1:SUB, LANE:right] = jnp.where(at_turb, inlet, hlo_ref[f:f + 1, :])
            ext2[f, SUB - 1:SUB, LANE:right] = jnp.where(at_turb, inlet, 0.0)
            ext2[f, SUB:top, 0:LANE] = zeros
            ext2[f, SUB:top, right:right + LANE] = zeros
        ext1[f, SUB:top, 0:LANE] = tile_t(lft_ref[f:f + 1, :])
        ext1[f, SUB:top, right:right + LANE] = tile_t(rgt_ref[f:f + 1, :])
    for f in range(nf):
        for g in range(nf):
            coef[f * nf + g] = jnp.full((SUB, LANE), mix_s[f, g], jnp.float32)
        coef[nf * nf + f] = jnp.full((SUB, LANE), -act_s[f], jnp.float32)
    copy.wait()

    def high_ghost(ext, halo_of):
        for f in range(nf):
            own = ext[f, top - 1:top, LANE:right]
            halo = halo_of(f)
            if f == 4:
                row = jnp.where(at_turb, own, jnp.where(at_exit, sw_ref[nf:nf + 1, :], halo))
            else:
                row = jnp.where(at_end, own, halo)
            ext[f, top:top + 1, LANE:right] = row

    if phase == 1:
        high_ghost(ext1, lambda f: hhi_ref[f:f + 1, :])

    sub_id = lax.broadcasted_iota(jnp.int32, (SUB, LANE), 0)
    lane_id = lax.broadcasted_iota(jnp.int32, (SUB, LANE), 1)
    first_sub = sub_id == 0
    last_sub = sub_id == SUB - 1
    first_lane = lane_id == 0
    last_lane = lane_id == LANE - 1

    def tendency_tiles(src, r0, c0s, rate_ts):
        r = pl.multiple_of(r0 + SUB, SUB)
        r_up = pl.multiple_of(r0, SUB)
        r_dn = pl.multiple_of(r0 + 2 * SUB, SUB)
        cs = [pl.multiple_of(c0 + LANE, LANE) for c0 in c0s]
        reacts = []
        for c, rate_t in zip(cs, rate_ts):
            v4 = src[4, pl.ds(r, SUB), pl.ds(c, LANE)]
            heat = 1.0 + (jnp.maximum(v4, 0.0) + jnp.log1p(jnp.exp(-jnp.abs(v4))))
            inv_heat = 1.0 / heat
            reacts.append([
                rate_t * src[f, pl.ds(r, SUB), pl.ds(c, LANE)] * jnp.exp(coef[nf * nf + f] * inv_heat)
                for f in range(nf)
            ])
        tends = [[] for _ in cs]
        for f in range(nf):
            accs = [None] * len(cs)
            for g in range(nf):
                m = coef[f * nf + g]
                for h in range(len(cs)):
                    term = m * reacts[h][g]
                    accs[h] = term if accs[h] is None else accs[h] + term
            for h, c in enumerate(cs):
                c_w = pl.multiple_of(c - LANE, LANE)
                c_e = pl.multiple_of(c + LANE, LANE)
                v = src[f, pl.ds(r, SUB), pl.ds(c, LANE)]
                up = src[f, pl.ds(r_up, SUB), pl.ds(c, LANE)]
                down = src[f, pl.ds(r_dn, SUB), pl.ds(c, LANE)]
                west = src[f, pl.ds(r, SUB), pl.ds(c_w, LANE)]
                east = src[f, pl.ds(r, SUB), pl.ds(c_e, LANE)]
                backward = jnp.where(first_sub, pltpu.roll(up, 1, 0), pltpu.roll(v, 1, 0))
                forward = jnp.where(last_sub, pltpu.roll(down, SUB - 1, 0), pltpu.roll(v, SUB - 1, 0))
                left = jnp.where(first_lane, pltpu.roll(west, 1, 1), pltpu.roll(v, 1, 1))
                rgt = jnp.where(last_lane, pltpu.roll(east, LANE - 1, 1), pltpu.roll(v, LANE - 1, 1))
                advect = -courant * (v - backward)
                spread = diffusion * (backward + forward + left + rgt - 4.0 * v)
                tends[h].append((v, advect + spread + source_step * accs[h]))
        return tends

    pair = 2 if n_j % 2 == 0 else 1
    n_jp = n_j // pair

    def offsets(i, jp):
        r0 = pl.multiple_of(i * SUB, SUB)
        c0s = [pl.multiple_of((jp * pair + h) * LANE, LANE) for h in range(pair)]
        return r0, c0s

    def stage_one(i, jp, dst, at):
        r0, c0s = offsets(i, jp)
        rate_ts = [rate_ref[pl.ds(r0, SUB), pl.ds(c0, LANE)] for c0 in c0s]
        tends = tendency_tiles(ext1, r0, c0s, rate_ts)
        for c0, tend in zip(c0s, tends):
            for f in range(nf):
                v, tf = tend[f]
                dst[f, pl.ds(at + r0, SUB), pl.ds(at // SUB * LANE + c0, LANE)] = v + tf

    if phase == 0:
        def inner(t, carry):
            stage_one(1 + t // n_jp, t % n_jp, first_ref, 0)
            return carry

        lax.fori_loop(0, (n_i - 2) * n_jp, inner, 0)
        edge = jnp.zeros((nf, SUB, lanes), jnp.float32)
        first_ref[:, 0:SUB, :] = edge
        first_ref[:, rows - SUB:rows, :] = edge
        return

    part.wait()

    def outer(t, carry):
        i = jnp.where(t < n_jp, 0, n_i - 1)
        stage_one(i, t % n_jp, ext2, SUB)
        return carry

    lax.fori_loop(0, 2 * n_jp, outer, 0)

    high_ghost(ext2, lambda f: jnp.zeros((1, lanes), jnp.float32))

    def stage_two(t, carry):
        r0, c0s = offsets(t // n_jp, t % n_jp)
        rate_ts = [rate_ref[pl.ds(r0, SUB), pl.ds(c0, LANE)] for c0 in c0s]
        tends = tendency_tiles(ext2, r0, c0s, rate_ts)
        r = pl.multiple_of(r0 + SUB, SUB)
        for c0, tend in zip(c0s, tends):
            c = pl.multiple_of(c0 + LANE, LANE)
            for f in range(nf):
                v, tf = tend[f]
                base = ext1[f, pl.ds(r, SUB), pl.ds(c, LANE)]
                out_ref[f, pl.ds(r0, SUB), pl.ds(c0, LANE)] = 0.5 * (base + v + tf)
        return carry

    lax.fori_loop(0, n_i * n_jp, stage_two, 0)

    for f in range(nf):
        elo_ref[f:f + 1, :] = ext2[f, SUB:SUB + 1, LANE:right]
        ehi_ref[f:f + 1, :] = ext2[f, top - 1:top, LANE:right]
        west = jnp.transpose(ext2[f, SUB:top, LANE:2 * LANE])
        east = jnp.transpose(ext2[f, SUB:top, right - LANE:right])
        clo_ref[f:f + 1, :] = west[0:1, :]
        chi_ref[f:f + 1, :] = east[LANE - 1:LANE, :]


def step_cost(cells, nf, share):
    return pl.CostEstimate(
        flops=int(share * 2 * cells * nf * (2 * nf + 24)),
        transcendentals=int(share * 2 * cells * (nf + 3)),
        bytes_accessed=4 * cells * (2 * nf + 1),
    )


def interior_stage(fields, rate, mix, act, lft, rgt):
    nf, rows, lanes = fields.shape
    vmem = pltpu.VMEM
    smem = pl.BlockSpec(memory_space=pltpu.SMEM)
    vspec = pl.BlockSpec(memory_space=vmem)
    return pl.pallas_call(
        functools.partial(step_kernel, nf, rows, lanes, 0),
        out_shape=jax.ShapeDtypeStruct((nf, rows, lanes), jnp.float32),
        in_specs=[smem, smem, pl.BlockSpec(memory_space=pl.ANY)] + [vspec] * 3,
        out_specs=vspec,
        scratch_shapes=[
            vmem((nf, rows + 2 * SUB, lanes + 2 * LANE), jnp.float32),
            vmem((nf * nf + nf, SUB, LANE), jnp.float32),
            pltpu.SemaphoreType.DMA((1,)),
        ],
        compiler_params=pltpu.CompilerParams(vmem_limit_bytes=60 * 1024 * 1024),
        cost_estimate=step_cost(rows * lanes, nf, 0.45),
    )(mix, act, fields, rate, lft, rgt)


def fused_step(fields, part, rate, mix, act, flags, halo_lo, halo_hi, swapped, lft, rgt):
    nf, rows, lanes = fields.shape
    vmem = pltpu.VMEM
    smem = pl.BlockSpec(memory_space=pltpu.SMEM)
    vspec = pl.BlockSpec(memory_space=vmem)
    anyspec = pl.BlockSpec(memory_space=pl.ANY)
    return pl.pallas_call(
        functools.partial(step_kernel, nf, rows, lanes, 1),
        out_shape=(
            jax.ShapeDtypeStruct((nf, rows, lanes), jnp.float32),
            jax.ShapeDtypeStruct((nf, lanes), jnp.float32),
            jax.ShapeDtypeStruct((nf, lanes), jnp.float32),
            jax.ShapeDtypeStruct((nf, rows), jnp.float32),
            jax.ShapeDtypeStruct((nf, rows), jnp.float32),
        ),
        in_specs=[smem, smem, smem, anyspec, anyspec] + [vspec] * 6,
        out_specs=(vspec,) * 5,
        scratch_shapes=[
            vmem((nf, rows + 2 * SUB, lanes + 2 * LANE), jnp.float32),
            vmem((nf, rows + 2 * SUB, lanes + 2 * LANE), jnp.float32),
            vmem((nf * nf + nf, SUB, LANE), jnp.float32),
            pltpu.SemaphoreType.DMA((2,)),
        ],
        compiler_params=pltpu.CompilerParams(vmem_limit_bytes=60 * 1024 * 1024),
        cost_estimate=step_cost(rows * lanes, nf, 0.55),
    )(mix, act, flags, fields, part, rate, halo_lo, halo_hi, swapped, lft, rgt)


def interp_kernel(ks, flag_s, ids_s, w_s, table_ref, *refs):
    n_pass = (len(refs) - 2) // 2
    ins, o_ref, outs, acc = refs[:n_pass], refs[n_pass], refs[n_pass + 1:-1], refs[-1]
    lanes = o_ref.shape[1]
    half = jnp.where(flag_s[0] > 0.5, 0, ks)
    acc[...] = jnp.zeros(acc.shape, jnp.float32)
    width = table_ref.shape[1]

    @pl.when(flag_s[0] + flag_s[1] > 0.5)
    def _():
        def body(p, carry):
            total = None
            for k in range(ks):
                q = ids_s[half + k, p]
                term = w_s[half + k, p] * table_ref[pl.ds(q, 1), :]
                total = term if total is None else total + term
            acc[pl.ds(p, 1), 0:width] = total
            return carry

        lax.fori_loop(0, lanes, body, 0, unroll=8)

    o_ref[...] = jnp.transpose(acc[...])[0:o_ref.shape[0], :]
    for src, dst in zip(ins, outs):
        dst[...] = src[...]


def interpolate(flags, ids, weights, table, passed):
    ks2, lanes = ids.shape
    smem = pl.BlockSpec(memory_space=pltpu.SMEM)
    vspec = pl.BlockSpec(memory_space=pltpu.VMEM)
    return pl.pallas_call(
        functools.partial(interp_kernel, ks2 // 2),
        out_shape=(jax.ShapeDtypeStruct((table.shape[1], lanes), jnp.float32),)
        + tuple(jax.ShapeDtypeStruct(x.shape, x.dtype) for x in passed),
        in_specs=[smem, smem, smem] + [vspec] * (1 + len(passed)),
        out_specs=(vspec,) * (1 + len(passed)),
        scratch_shapes=[pltpu.VMEM((lanes, LANE), jnp.float32)],
    )(flags, ids, weights, table, *passed)


def fix_kernel(low_w, side_w, out_in, g0_ref, g1_ref, gl_ref, gr_ref, out_ref, rb, cb, sem):
    nf, rows, lanes = out_ref.shape
    mid = rows - 2 * SUB
    wins = [
        (out_ref.at[:, pl.ds(0, SUB), :], rb.at[0]),
        (out_ref.at[:, pl.ds(rows - SUB, SUB), :], rb.at[1]),
        (out_ref.at[:, pl.ds(SUB, mid), pl.ds(0, LANE)], cb.at[0]),
        (out_ref.at[:, pl.ds(SUB, mid), pl.ds(lanes - LANE, LANE)], cb.at[1]),
    ]
    loads = [pltpu.make_async_copy(hbm, buf, sem.at[s]) for s, (hbm, buf) in enumerate(wins)]
    for c in loads:
        c.start()
    for c in loads:
        c.wait()
    lane_id = lax.broadcasted_iota(jnp.int32, (rows, LANE), 1)
    row_lane = lax.broadcasted_iota(jnp.int32, (SUB, LANE), 1)
    for f in range(nf):
        west = jnp.where(lane_id == 0, side_w * tile_t(gl_ref[f:f + 1, :]), 0.0)
        east = jnp.where(lane_id == LANE - 1, side_w * tile_t(gr_ref[f:f + 1, :]), 0.0)
        cb[0, f] = cb[0, f] + west[SUB:rows - SUB]
        cb[1, f] = cb[1, f] + east[SUB:rows - SUB]
        for s, lo in ((0, 0), (1, rows - SUB)):
            rb[s, f, :, 0:LANE] = rb[s, f, :, 0:LANE] + west[lo:lo + SUB]
            rb[s, f, :, lanes - LANE:lanes] = rb[s, f, :, lanes - LANE:lanes] + east[lo:lo + SUB]
        rb[0, f, 0:1, :] = rb[0, f, 0:1, :] + low_w * g0_ref[f:f + 1, :]
        rb[1, f, SUB - 1:SUB, :] = rb[1, f, SUB - 1:SUB, :] + side_w * g1_ref[f:f + 1, :]
    stores = [pltpu.make_async_copy(buf, hbm, sem.at[s]) for s, (hbm, buf) in enumerate(wins)]
    for c in stores:
        c.start()
    for c in stores:
        c.wait()


def fix_edges(out, g0, g1, gl, gr, low_w, side_w):
    nf, rows, lanes = out.shape
    vspec = pl.BlockSpec(memory_space=pltpu.VMEM)
    anyspec = pl.BlockSpec(memory_space=pl.ANY)
    return pl.pallas_call(
        functools.partial(fix_kernel, low_w, side_w),
        out_shape=jax.ShapeDtypeStruct(out.shape, jnp.float32),
        in_specs=[anyspec, vspec, vspec, vspec, vspec],
        out_specs=anyspec,
        scratch_shapes=[
            pltpu.VMEM((2, nf, SUB, lanes), jnp.float32),
            pltpu.VMEM((2, nf, rows - 2 * SUB, LANE), jnp.float32),
            pltpu.SemaphoreType.DMA((4,)),
        ],
        input_output_aliases={0: 0},
    )(out, g0, g1, gl, gr)


def shards(
    fields, react_rate, mix_matrix, activation, inlet_ids, inlet_weights, outlet_ids, outlet_weights
):
    nf, rows, lanes = fields.shape
    n_grp = lax.axis_size("grp")
    n_blk = lax.axis_size("blk")
    g = lax.axis_index("grp")
    b = lax.axis_index("blk")
    exit_grp = n_grp - 2
    turb_grp = n_grp - 1
    flags = jnp.stack([g == exit_grp, g == turb_grp]).astype(jnp.float32)

    last_row = fields[:, -1, :]
    first_row = fields[:, 0, :]
    payload = jnp.concatenate([last_row, first_row[4:5]], axis=0)
    planes = payload[None]
    span = 1
    while span < n_blk:
        partner = [(i, i ^ span) for i in range(n_blk)]
        planes = jnp.concatenate([planes, lax.ppermute(planes, "blk", partner)], axis=0)
        span *= 2
    table = jnp.transpose(planes, (0, 2, 1)).reshape(n_blk * lanes, nf + 1)
    ids = jnp.concatenate([inlet_ids, outlet_ids], axis=0)
    ids = (jnp.bitwise_xor(ids // lanes, b) * lanes) + ids % lanes
    wts = jnp.concatenate([inlet_weights, outlet_weights], axis=0)
    halo_lo = lax.ppermute(last_row, "grp", [(i, i + 1) for i in range(n_grp - 2)])
    halo_hi = lax.ppermute(first_row, "grp", [(i + 1, i) for i in range(n_grp - 2)])
    lft = lax.ppermute(fields[:, :, lanes - 1], "blk", [(i, (i + 1) % n_blk) for i in range(n_blk)])
    rgt = lax.ppermute(fields[:, :, 0], "blk", [((i + 1) % n_blk, i) for i in range(n_blk)])

    part = interior_stage(fields, react_rate, mix_matrix, activation, lft, rgt)
    swap, halo_lo, halo_hi, _ = interpolate(
        flags, ids, wts, table, (halo_lo, halo_hi, part[:, 0:SUB, 0:LANE])
    )
    swapped = lax.ppermute(swap, "grp", [(exit_grp, turb_grp), (turb_grp, exit_grp)])

    out, elo, ehi, clo, chi = fused_step(
        fields, part, react_rate, mix_matrix, activation, flags, halo_lo, halo_hi, swapped, lft, rgt
    )

    g0 = lax.ppermute(ehi, "grp", [(i, i + 1) for i in range(n_grp - 2)])
    g1 = lax.ppermute(elo, "grp", [(i + 1, i) for i in range(n_grp - 2)])
    gl = lax.ppermute(chi, "blk", [(i, (i + 1) % n_blk) for i in range(n_blk)])
    gr = lax.ppermute(clo, "blk", [((i + 1) % n_blk, i) for i in range(n_blk)])
    low_w = 0.5 * (courant + diffusion)
    side_w = 0.5 * diffusion
    return fix_edges(out, g0, g1, gl, gr, low_w, side_w)


def solution(mesh):
    in_specs = (
        P(None, "grp", "blk"),
        P("grp", "blk"),
        P(),
        P(),
        P(None, "blk"),
        P(None, "blk"),
        P(None, "blk"),
        P(None, "blk"),
    )
    out_specs = P(None, "grp", "blk")
    return jax.shard_map(shards, mesh=mesh, in_specs=in_specs, out_specs=out_specs, check_vma=False)
```

```python
import functools

import jax
import jax.numpy as jnp
from jax import lax
from jax.experimental import pallas as pl
from jax.experimental.pallas import tpu as pltpu
from jax.sharding import PartitionSpec as P

courant = 0.5
diffusion = 0.1
source_step = 0.5

SUB = 8
LANE = 128


def tile_t(row):
    n = row.shape[1]
    return jnp.transpose(jnp.broadcast_to(row, (n, n)))


def step_kernel(nf, rows, lanes, mix_s, act_s, flag_s, f_hbm, rate_ref, hlo_ref, hhi_ref, sw_ref,
                lft_ref, rgt_ref, out_ref, elo_ref, ehi_ref, clo_ref, chi_ref, ext1, ext2, coef, sem):
    n_i = rows // SUB
    n_j = lanes // LANE
    top = SUB + rows
    right = LANE + lanes
    at_exit = flag_s[0] > 0.5
    at_turb = flag_s[1] > 0.5
    at_end = flag_s[0] + flag_s[1] > 0.5

    copy = pltpu.make_async_copy(f_hbm, ext1.at[:, SUB:top, LANE:right], sem.at[0])
    copy.start()
    zeros = jnp.zeros((rows, LANE), jnp.float32)
    for f in range(nf):
        inlet = sw_ref[f:f + 1, :]
        ext1[f, SUB - 1:SUB, LANE:right] = jnp.where(at_turb, inlet, hlo_ref[f:f + 1, :])
        ext2[f, SUB - 1:SUB, LANE:right] = jnp.where(at_turb, inlet, 0.0)
        ext1[f, SUB:top, 0:LANE] = tile_t(lft_ref[f:f + 1, :])
        ext1[f, SUB:top, right:right + LANE] = tile_t(rgt_ref[f:f + 1, :])
        ext2[f, SUB:top, 0:LANE] = zeros
        ext2[f, SUB:top, right:right + LANE] = zeros
    for f in range(nf):
        for g in range(nf):
            coef[f * nf + g] = jnp.full((SUB, LANE), mix_s[f, g], jnp.float32)
        coef[nf * nf + f] = jnp.full((SUB, LANE), -act_s[f], jnp.float32)
    copy.wait()

    def high_ghost(ext, halo_of):
        for f in range(nf):
            own = ext[f, top - 1:top, LANE:right]
            halo = halo_of(f)
            if f == 4:
                row = jnp.where(at_turb, own, jnp.where(at_exit, sw_ref[nf:nf + 1, :], halo))
            else:
                row = jnp.where(at_end, own, halo)
            ext[f, top:top + 1, LANE:right] = row

    high_ghost(ext1, lambda f: hhi_ref[f:f + 1, :])

    sub_id = lax.broadcasted_iota(jnp.int32, (SUB, LANE), 0)
    lane_id = lax.broadcasted_iota(jnp.int32, (SUB, LANE), 1)
    first_sub = sub_id == 0
    last_sub = sub_id == SUB - 1
    first_lane = lane_id == 0
    last_lane = lane_id == LANE - 1

    def tendency_tiles(src, r0, c0s, rate_ts):
        r = pl.multiple_of(r0 + SUB, SUB)
        r_up = pl.multiple_of(r0, SUB)
        r_dn = pl.multiple_of(r0 + 2 * SUB, SUB)
        cs = [pl.multiple_of(c0 + LANE, LANE) for c0 in c0s]
        reacts = []
        for c, rate_t in zip(cs, rate_ts):
            v4 = src[4, pl.ds(r, SUB), pl.ds(c, LANE)]
            heat = 1.0 + (jnp.maximum(v4, 0.0) + jnp.log1p(jnp.exp(-jnp.abs(v4))))
            inv_heat = 1.0 / heat
            reacts.append([
                rate_t * src[f, pl.ds(r, SUB), pl.ds(c, LANE)] * jnp.exp(coef[nf * nf + f] * inv_heat)
                for f in range(nf)
            ])
        tends = [[] for _ in cs]
        for f in range(nf):
            accs = [None] * len(cs)
            for g in range(nf):
                m = coef[f * nf + g]
                for h in range(len(cs)):
                    term = m * reacts[h][g]
                    accs[h] = term if accs[h] is None else accs[h] + term
            for h, c in enumerate(cs):
                c_w = pl.multiple_of(c - LANE, LANE)
                c_e = pl.multiple_of(c + LANE, LANE)
                v = src[f, pl.ds(r, SUB), pl.ds(c, LANE)]
                up = src[f, pl.ds(r_up, SUB), pl.ds(c, LANE)]
                down = src[f, pl.ds(r_dn, SUB), pl.ds(c, LANE)]
                west = src[f, pl.ds(r, SUB), pl.ds(c_w, LANE)]
                east = src[f, pl.ds(r, SUB), pl.ds(c_e, LANE)]
                backward = jnp.where(first_sub, pltpu.roll(up, 1, 0), pltpu.roll(v, 1, 0))
                forward = jnp.where(last_sub, pltpu.roll(down, SUB - 1, 0), pltpu.roll(v, SUB - 1, 0))
                left = jnp.where(first_lane, pltpu.roll(west, 1, 1), pltpu.roll(v, 1, 1))
                rgt = jnp.where(last_lane, pltpu.roll(east, LANE - 1, 1), pltpu.roll(v, LANE - 1, 1))
                advect = -courant * (v - backward)
                spread = diffusion * (backward + forward + left + rgt - 4.0 * v)
                tends[h].append((v, advect + spread + source_step * accs[h]))
        return tends

    pair = 2 if n_j % 2 == 0 else 1
    n_jp = n_j // pair

    def tile_offsets(t):
        i = t // n_jp
        jp = t % n_jp
        r0 = pl.multiple_of(i * SUB, SUB)
        c0s = [pl.multiple_of((jp * pair + h) * LANE, LANE) for h in range(pair)]
        return r0, c0s

    def stage_one(t, carry):
        r0, c0s = tile_offsets(t)
        rate_ts = [rate_ref[pl.ds(r0, SUB), pl.ds(c0, LANE)] for c0 in c0s]
        tends = tendency_tiles(ext1, r0, c0s, rate_ts)
        r = pl.multiple_of(r0 + SUB, SUB)
        for c0, tend in zip(c0s, tends):
            c = pl.multiple_of(c0 + LANE, LANE)
            for f in range(nf):
                v, tf = tend[f]
                ext2[f, pl.ds(r, SUB), pl.ds(c, LANE)] = v + tf
        return carry

    lax.fori_loop(0, n_i * n_jp, stage_one, 0)

    high_ghost(ext2, lambda f: jnp.zeros((1, lanes), jnp.float32))

    def stage_two(t, carry):
        r0, c0s = tile_offsets(t)
        rate_ts = [rate_ref[pl.ds(r0, SUB), pl.ds(c0, LANE)] for c0 in c0s]
        tends = tendency_tiles(ext2, r0, c0s, rate_ts)
        r = pl.multiple_of(r0 + SUB, SUB)
        for c0, tend in zip(c0s, tends):
            c = pl.multiple_of(c0 + LANE, LANE)
            for f in range(nf):
                v, tf = tend[f]
                base = ext1[f, pl.ds(r, SUB), pl.ds(c, LANE)]
                out_ref[f, pl.ds(r0, SUB), pl.ds(c0, LANE)] = 0.5 * (base + v + tf)
        return carry

    lax.fori_loop(0, n_i * n_jp, stage_two, 0)

    for f in range(nf):
        elo_ref[f:f + 1, :] = ext2[f, SUB:SUB + 1, LANE:right]
        ehi_ref[f:f + 1, :] = ext2[f, top - 1:top, LANE:right]
        west = jnp.transpose(ext2[f, SUB:top, LANE:2 * LANE])
        east = jnp.transpose(ext2[f, SUB:top, right - LANE:right])
        clo_ref[f:f + 1, :] = west[0:1, :]
        chi_ref[f:f + 1, :] = east[LANE - 1:LANE, :]


def fused_step(fields, rate, mix, act, flags, halo_lo, halo_hi, swapped, lft, rgt):
    nf, rows, lanes = fields.shape
    vmem = pltpu.VMEM
    smem = pl.BlockSpec(memory_space=pltpu.SMEM)
    vspec = pl.BlockSpec(memory_space=vmem)
    cells = rows * lanes
    cost = pl.CostEstimate(
        flops=2 * cells * nf * (2 * nf + 24),
        transcendentals=2 * cells * (nf + 3),
        bytes_accessed=4 * cells * (2 * nf + 1),
    )
    return pl.pallas_call(
        functools.partial(step_kernel, nf, rows, lanes),
        out_shape=(
            jax.ShapeDtypeStruct((nf, rows, lanes), jnp.float32),
            jax.ShapeDtypeStruct((nf, lanes), jnp.float32),
            jax.ShapeDtypeStruct((nf, lanes), jnp.float32),
            jax.ShapeDtypeStruct((nf, rows), jnp.float32),
            jax.ShapeDtypeStruct((nf, rows), jnp.float32),
        ),
        in_specs=[smem, smem, smem, pl.BlockSpec(memory_space=pl.ANY)] + [vspec] * 6,
        out_specs=(vspec,) * 5,
        scratch_shapes=[
            vmem((nf, rows + 2 * SUB, lanes + 2 * LANE), jnp.float32),
            vmem((nf, rows + 2 * SUB, lanes + 2 * LANE), jnp.float32),
            vmem((nf * nf + nf, SUB, LANE), jnp.float32),
            pltpu.SemaphoreType.DMA((1,)),
        ],
        compiler_params=pltpu.CompilerParams(vmem_limit_bytes=60 * 1024 * 1024),
        cost_estimate=cost,
    )(mix, act, flags, fields, rate, halo_lo, halo_hi, swapped, lft, rgt)


def interp_kernel(ks, flag_s, ids_s, w_s, table_ref, *refs):
    n_pass = (len(refs) - 2) // 2
    ins, o_ref, outs, acc = refs[:n_pass], refs[n_pass], refs[n_pass + 1:-1], refs[-1]
    lanes = o_ref.shape[1]
    half = jnp.where(flag_s[0] > 0.5, 0, ks)
    acc[...] = jnp.zeros(acc.shape, jnp.float32)
    width = table_ref.shape[2]

    sub = lax.broadcasted_iota(jnp.int32, (SUB, width), 0)

    @pl.when(flag_s[0] + flag_s[1] > 0.5)
    def _():
        def group(pg, carry):
            tile = jnp.zeros((SUB, width), jnp.float32)
            for s in range(SUB):
                p = pg * SUB + s
                total = None
                for k in range(ks):
                    q = ids_s[half + k, p]
                    rows8 = table_ref[q // SUB]
                    term = jnp.where(sub == q % SUB, rows8, 0.0) * w_s[half + k, p]
                    total = term if total is None else total + term
                for shift in (4, 2, 1):
                    total = total + pltpu.roll(total, shift, 0)
                tile = jnp.where(sub == s, total, tile)
            acc[pl.ds(pl.multiple_of(pg * SUB, SUB), SUB), 0:width] = tile
            return carry

        lax.fori_loop(0, lanes // SUB, group, 0)

    o_ref[...] = jnp.transpose(acc[...])[0:o_ref.shape[0], :]
    for src, dst in zip(ins, outs):
        dst[...] = src[...]


def interpolate(flags, ids, weights, table, passed):
    ks2, lanes = ids.shape
    smem = pl.BlockSpec(memory_space=pltpu.SMEM)
    vspec = pl.BlockSpec(memory_space=pltpu.VMEM)
    return pl.pallas_call(
        functools.partial(interp_kernel, ks2 // 2),
        out_shape=(jax.ShapeDtypeStruct((table.shape[2], lanes), jnp.float32),)
        + tuple(jax.ShapeDtypeStruct(x.shape, x.dtype) for x in passed),
        in_specs=[smem, smem, smem] + [vspec] * (1 + len(passed)),
        out_specs=(vspec,) * (1 + len(passed)),
        scratch_shapes=[pltpu.VMEM((lanes, LANE), jnp.float32)],
    )(flags, ids, weights, table, *passed)


def fix_kernel(low_w, side_w, out_in, g0_ref, g1_ref, gl_ref, gr_ref, out_ref, rb, cb, sem):
    nf, rows, lanes = out_ref.shape
    mid = rows - 2 * SUB
    wins = [
        (out_ref.at[:, pl.ds(0, SUB), :], rb.at[0]),
        (out_ref.at[:, pl.ds(rows - SUB, SUB), :], rb.at[1]),
        (out_ref.at[:, pl.ds(SUB, mid), pl.ds(0, LANE)], cb.at[0]),
        (out_ref.at[:, pl.ds(SUB, mid), pl.ds(lanes - LANE, LANE)], cb.at[1]),
    ]
    loads = [pltpu.make_async_copy(hbm, buf, sem.at[s]) for s, (hbm, buf) in enumerate(wins)]
    for c in loads:
        c.start()
    for c in loads:
        c.wait()
    lane_id = lax.broadcasted_iota(jnp.int32, (rows, LANE), 1)
    row_lane = lax.broadcasted_iota(jnp.int32, (SUB, LANE), 1)
    for f in range(nf):
        west = jnp.where(lane_id == 0, side_w * tile_t(gl_ref[f:f + 1, :]), 0.0)
        east = jnp.where(lane_id == LANE - 1, side_w * tile_t(gr_ref[f:f + 1, :]), 0.0)
        cb[0, f] = cb[0, f] + west[SUB:rows - SUB]
        cb[1, f] = cb[1, f] + east[SUB:rows - SUB]
        for s, lo in ((0, 0), (1, rows - SUB)):
            rb[s, f, :, 0:LANE] = rb[s, f, :, 0:LANE] + west[lo:lo + SUB]
            rb[s, f, :, lanes - LANE:lanes] = rb[s, f, :, lanes - LANE:lanes] + east[lo:lo + SUB]
        rb[0, f, 0:1, :] = rb[0, f, 0:1, :] + low_w * g0_ref[f:f + 1, :]
        rb[1, f, SUB - 1:SUB, :] = rb[1, f, SUB - 1:SUB, :] + side_w * g1_ref[f:f + 1, :]
    stores = [pltpu.make_async_copy(buf, hbm, sem.at[s]) for s, (hbm, buf) in enumerate(wins)]
    for c in stores:
        c.start()
    for c in stores:
        c.wait()


def fix_edges(out, g0, g1, gl, gr, low_w, side_w):
    nf, rows, lanes = out.shape
    vspec = pl.BlockSpec(memory_space=pltpu.VMEM)
    anyspec = pl.BlockSpec(memory_space=pl.ANY)
    return pl.pallas_call(
        functools.partial(fix_kernel, low_w, side_w),
        out_shape=jax.ShapeDtypeStruct(out.shape, jnp.float32),
        in_specs=[anyspec, vspec, vspec, vspec, vspec],
        out_specs=anyspec,
        scratch_shapes=[
            pltpu.VMEM((2, nf, SUB, lanes), jnp.float32),
            pltpu.VMEM((2, nf, rows - 2 * SUB, LANE), jnp.float32),
            pltpu.SemaphoreType.DMA((4,)),
        ],
        input_output_aliases={0: 0},
    )(out, g0, g1, gl, gr)


def shards(
    fields, react_rate, mix_matrix, activation, inlet_ids, inlet_weights, outlet_ids, outlet_weights
):
    nf, rows, lanes = fields.shape
    n_grp = lax.axis_size("grp")
    n_blk = lax.axis_size("blk")
    g = lax.axis_index("grp")
    b = lax.axis_index("blk")
    exit_grp = n_grp - 2
    turb_grp = n_grp - 1
    flags = jnp.stack([g == exit_grp, g == turb_grp]).astype(jnp.float32)

    last_row = fields[:, -1, :]
    first_row = fields[:, 0, :]
    payload = jnp.concatenate([last_row, first_row[4:5]], axis=0)
    planes = payload[None]
    span = 1
    while span < n_blk:
        partner = [(i, i ^ span) for i in range(n_blk)]
        planes = jnp.concatenate([planes, lax.ppermute(planes, "blk", partner)], axis=0)
        span *= 2
    table = jnp.transpose(planes, (0, 2, 1)).reshape(n_blk * lanes // SUB, SUB, nf + 1)
    ids = jnp.concatenate([inlet_ids, outlet_ids], axis=0)
    ids = (jnp.bitwise_xor(ids // lanes, b) * lanes) + ids % lanes
    wts = jnp.concatenate([inlet_weights, outlet_weights], axis=0)
    halo_lo = lax.ppermute(last_row, "grp", [(i, i + 1) for i in range(n_grp - 2)])
    halo_hi = lax.ppermute(first_row, "grp", [(i + 1, i) for i in range(n_grp - 2)])
    lft = lax.ppermute(fields[:, :, lanes - 1], "blk", [(i, (i + 1) % n_blk) for i in range(n_blk)])
    rgt = lax.ppermute(fields[:, :, 0], "blk", [((i + 1) % n_blk, i) for i in range(n_blk)])

    swap, halo_lo, halo_hi, lft, rgt = interpolate(flags, ids, wts, table, (halo_lo, halo_hi, lft, rgt))
    swapped = lax.ppermute(swap, "grp", [(exit_grp, turb_grp), (turb_grp, exit_grp)])

    out, elo, ehi, clo, chi = fused_step(
        fields, react_rate, mix_matrix, activation, flags, halo_lo, halo_hi, swapped, lft, rgt
    )

    g0 = lax.ppermute(ehi, "grp", [(i, i + 1) for i in range(n_grp - 2)])
    g1 = lax.ppermute(elo, "grp", [(i + 1, i) for i in range(n_grp - 2)])
    gl = lax.ppermute(chi, "blk", [(i, (i + 1) % n_blk) for i in range(n_blk)])
    gr = lax.ppermute(clo, "blk", [((i + 1) % n_blk, i) for i in range(n_blk)])
    low_w = 0.5 * (courant + diffusion)
    side_w = 0.5 * diffusion
    return fix_edges(out, g0, g1, gl, gr, low_w, side_w)


def solution(mesh):
    in_specs = (
        P(None, "grp", "blk"),
        P("grp", "blk"),
        P(),
        P(),
        P(None, "blk"),
        P(None, "blk"),
        P(None, "blk"),
        P(None, "blk"),
    )
    out_specs = P(None, "grp", "blk")
    return jax.shard_map(shards, mesh=mesh, in_specs=in_specs, out_specs=out_specs, check_vma=False)
```

```python
import functools

import jax
import jax.numpy as jnp
from jax import lax
from jax.experimental import pallas as pl
from jax.experimental.pallas import tpu as pltpu
from jax.sharding import PartitionSpec as P

courant = 0.5
diffusion = 0.1
source_step = 0.5

SUB = 8
LANE = 128


def tile_t(row):
    n = row.shape[1]
    return jnp.transpose(jnp.broadcast_to(row, (n, n)))


def step_kernel(nf, rows, lanes, mix_s, act_s, flag_s, f_hbm, rate_ref, hlo_ref, hhi_ref, sw_ref,
                lft_ref, rgt_ref, out_ref, elo_ref, ehi_ref, clo_ref, chi_ref, ext1, ext2, coef, sem):
    n_i = rows // SUB
    n_j = lanes // LANE
    top = SUB + rows
    right = LANE + lanes
    at_exit = flag_s[0] > 0.5
    at_turb = flag_s[1] > 0.5
    at_end = flag_s[0] + flag_s[1] > 0.5

    copy = pltpu.make_async_copy(f_hbm, ext1.at[:, SUB:top, LANE:right], sem.at[0])
    copy.start()
    zeros = jnp.zeros((rows, LANE), jnp.float32)
    for f in range(nf):
        inlet = sw_ref[f:f + 1, :]
        ext1[f, SUB - 1:SUB, LANE:right] = jnp.where(at_turb, inlet, hlo_ref[f:f + 1, :])
        ext2[f, SUB - 1:SUB, LANE:right] = jnp.where(at_turb, inlet, 0.0)
        ext1[f, SUB:top, 0:LANE] = tile_t(lft_ref[f:f + 1, :])
        ext1[f, SUB:top, right:right + LANE] = tile_t(rgt_ref[f:f + 1, :])
        ext2[f, SUB:top, 0:LANE] = zeros
        ext2[f, SUB:top, right:right + LANE] = zeros
    for f in range(nf):
        for g in range(nf):
            coef[f * nf + g] = jnp.full((SUB, LANE), mix_s[f, g], jnp.float32)
        coef[nf * nf + f] = jnp.full((SUB, LANE), -act_s[f], jnp.float32)
    copy.wait()

    def high_ghost(ext, halo_of):
        for f in range(nf):
            own = ext[f, top - 1:top, LANE:right]
            halo = halo_of(f)
            if f == 4:
                row = jnp.where(at_turb, own, jnp.where(at_exit, sw_ref[nf:nf + 1, :], halo))
            else:
                row = jnp.where(at_end, own, halo)
            ext[f, top:top + 1, LANE:right] = row

    high_ghost(ext1, lambda f: hhi_ref[f:f + 1, :])

    sub_id = lax.broadcasted_iota(jnp.int32, (SUB, LANE), 0)
    lane_id = lax.broadcasted_iota(jnp.int32, (SUB, LANE), 1)
    first_sub = sub_id == 0
    last_sub = sub_id == SUB - 1
    first_lane = lane_id == 0
    last_lane = lane_id == LANE - 1

    def tendency_tiles(src, r0, c0s, rate_ts):
        r = pl.multiple_of(r0 + SUB, SUB)
        r_up = pl.multiple_of(r0, SUB)
        r_dn = pl.multiple_of(r0 + 2 * SUB, SUB)
        cs = [pl.multiple_of(c0 + LANE, LANE) for c0 in c0s]
        reacts = []
        for c, rate_t in zip(cs, rate_ts):
            v4 = src[4, pl.ds(r, SUB), pl.ds(c, LANE)]
            heat = 1.0 + (jnp.maximum(v4, 0.0) + jnp.log1p(jnp.exp(-jnp.abs(v4))))
            inv_heat = 1.0 / heat
            reacts.append([
                rate_t * src[f, pl.ds(r, SUB), pl.ds(c, LANE)] * jnp.exp(coef[nf * nf + f] * inv_heat)
                for f in range(nf)
            ])
        tends = [[] for _ in cs]
        for f in range(nf):
            accs = [None] * len(cs)
            for g in range(nf):
                m = coef[f * nf + g]
                for h in range(len(cs)):
                    term = m * reacts[h][g]
                    accs[h] = term if accs[h] is None else accs[h] + term
            for h, c in enumerate(cs):
                c_w = pl.multiple_of(c - LANE, LANE)
                c_e = pl.multiple_of(c + LANE, LANE)
                v = src[f, pl.ds(r, SUB), pl.ds(c, LANE)]
                up = src[f, pl.ds(r_up, SUB), pl.ds(c, LANE)]
                down = src[f, pl.ds(r_dn, SUB), pl.ds(c, LANE)]
                west = src[f, pl.ds(r, SUB), pl.ds(c_w, LANE)]
                east = src[f, pl.ds(r, SUB), pl.ds(c_e, LANE)]
                backward = jnp.where(first_sub, pltpu.roll(up, 1, 0), pltpu.roll(v, 1, 0))
                forward = jnp.where(last_sub, pltpu.roll(down, SUB - 1, 0), pltpu.roll(v, SUB - 1, 0))
                left = jnp.where(first_lane, pltpu.roll(west, 1, 1), pltpu.roll(v, 1, 1))
                rgt = jnp.where(last_lane, pltpu.roll(east, LANE - 1, 1), pltpu.roll(v, LANE - 1, 1))
                advect = -courant * (v - backward)
                spread = diffusion * (backward + forward + left + rgt - 4.0 * v)
                tends[h].append((v, advect + spread + source_step * accs[h]))
        return tends

    pair = 2 if n_j % 2 == 0 else 1
    n_jp = n_j // pair

    def tile_offsets(t):
        i = t // n_jp
        jp = t % n_jp
        r0 = pl.multiple_of(i * SUB, SUB)
        c0s = [pl.multiple_of((jp * pair + h) * LANE, LANE) for h in range(pair)]
        return r0, c0s

    def stage_one(t, carry):
        r0, c0s = tile_offsets(t)
        rate_ts = [rate_ref[pl.ds(r0, SUB), pl.ds(c0, LANE)] for c0 in c0s]
        tends = tendency_tiles(ext1, r0, c0s, rate_ts)
        r = pl.multiple_of(r0 + SUB, SUB)
        for c0, tend in zip(c0s, tends):
            c = pl.multiple_of(c0 + LANE, LANE)
            for f in range(nf):
                v, tf = tend[f]
                ext2[f, pl.ds(r, SUB), pl.ds(c, LANE)] = v + tf
        return carry

    lax.fori_loop(0, n_i * n_jp, stage_one, 0)

    high_ghost(ext2, lambda f: jnp.zeros((1, lanes), jnp.float32))

    def stage_two(t, carry):
        r0, c0s = tile_offsets(t)
        rate_ts = [rate_ref[pl.ds(r0, SUB), pl.ds(c0, LANE)] for c0 in c0s]
        tends = tendency_tiles(ext2, r0, c0s, rate_ts)
        r = pl.multiple_of(r0 + SUB, SUB)
        for c0, tend in zip(c0s, tends):
            c = pl.multiple_of(c0 + LANE, LANE)
            for f in range(nf):
                v, tf = tend[f]
                base = ext1[f, pl.ds(r, SUB), pl.ds(c, LANE)]
                out_ref[f, pl.ds(r0, SUB), pl.ds(c0, LANE)] = 0.5 * (base + v + tf)
        return carry

    lax.fori_loop(0, n_i * n_jp, stage_two, 0)

    for f in range(nf):
        elo_ref[f:f + 1, :] = ext2[f, SUB:SUB + 1, LANE:right]
        ehi_ref[f:f + 1, :] = ext2[f, top - 1:top, LANE:right]
        west = jnp.transpose(ext2[f, SUB:top, LANE:2 * LANE])
        east = jnp.transpose(ext2[f, SUB:top, right - LANE:right])
        clo_ref[f:f + 1, :] = west[0:1, :]
        chi_ref[f:f + 1, :] = east[LANE - 1:LANE, :]


def fused_step(fields, rate, mix, act, flags, halo_lo, halo_hi, swapped, lft, rgt):
    nf, rows, lanes = fields.shape
    vmem = pltpu.VMEM
    smem = pl.BlockSpec(memory_space=pltpu.SMEM)
    vspec = pl.BlockSpec(memory_space=vmem)
    cells = rows * lanes
    cost = pl.CostEstimate(
        flops=2 * cells * nf * (2 * nf + 24),
        transcendentals=2 * cells * (nf + 3),
        bytes_accessed=4 * cells * (2 * nf + 1),
    )
    return pl.pallas_call(
        functools.partial(step_kernel, nf, rows, lanes),
        out_shape=(
            jax.ShapeDtypeStruct((nf, rows, lanes), jnp.float32),
            jax.ShapeDtypeStruct((nf, lanes), jnp.float32),
            jax.ShapeDtypeStruct((nf, lanes), jnp.float32),
            jax.ShapeDtypeStruct((nf, rows), jnp.float32),
            jax.ShapeDtypeStruct((nf, rows), jnp.float32),
        ),
        in_specs=[smem, smem, smem, pl.BlockSpec(memory_space=pl.ANY)] + [vspec] * 6,
        out_specs=(vspec,) * 5,
        scratch_shapes=[
            vmem((nf, rows + 2 * SUB, lanes + 2 * LANE), jnp.float32),
            vmem((nf, rows + 2 * SUB, lanes + 2 * LANE), jnp.float32),
            vmem((nf * nf + nf, SUB, LANE), jnp.float32),
            pltpu.SemaphoreType.DMA((1,)),
        ],
        compiler_params=pltpu.CompilerParams(vmem_limit_bytes=60 * 1024 * 1024),
        cost_estimate=cost,
    )(mix, act, flags, fields, rate, halo_lo, halo_hi, swapped, lft, rgt)


def interp_kernel(ks, flag_s, ids_s, w_s, table_ref, *refs):
    n_pass = (len(refs) - 2) // 2
    ins, o_ref, outs, acc = refs[:n_pass], refs[n_pass], refs[n_pass + 1:-1], refs[-1]
    lanes = o_ref.shape[1]
    half = jnp.where(flag_s[0] > 0.5, 0, ks)
    acc[...] = jnp.zeros(acc.shape, jnp.float32)
    width = table_ref.shape[1]

    @pl.when(flag_s[0] + flag_s[1] > 0.5)
    def _():
        def body(p, carry):
            total = None
            for k in range(ks):
                q = ids_s[half + k, p]
                term = w_s[half + k, p] * table_ref[pl.ds(q, 1), :]
                total = term if total is None else total + term
            acc[pl.ds(p, 1), 0:width] = total
            return carry

        lax.fori_loop(0, lanes, body, 0, unroll=8)

    o_ref[...] = jnp.transpose(acc[...])[0:o_ref.shape[0], :]
    for src, dst in zip(ins, outs):
        dst[...] = src[...]


def interpolate(flags, ids, weights, table, passed):
    ks2, lanes = ids.shape
    smem = pl.BlockSpec(memory_space=pltpu.SMEM)
    vspec = pl.BlockSpec(memory_space=pltpu.VMEM)
    return pl.pallas_call(
        functools.partial(interp_kernel, ks2 // 2),
        out_shape=(jax.ShapeDtypeStruct((table.shape[1], lanes), jnp.float32),)
        + tuple(jax.ShapeDtypeStruct(x.shape, x.dtype) for x in passed),
        in_specs=[smem, smem, smem] + [vspec] * (1 + len(passed)),
        out_specs=(vspec,) * (1 + len(passed)),
        scratch_shapes=[pltpu.VMEM((lanes, LANE), jnp.float32)],
    )(flags, ids, weights, table, *passed)


def fix_kernel(low_w, side_w, out_in, g0_ref, g1_ref, gl_ref, gr_ref, out_ref, rb, cb, sem):
    nf, rows, lanes = out_ref.shape
    mid = rows - 2 * SUB
    wins = [
        (out_ref.at[:, pl.ds(0, SUB), :], rb.at[0]),
        (out_ref.at[:, pl.ds(rows - SUB, SUB), :], rb.at[1]),
        (out_ref.at[:, pl.ds(SUB, mid), pl.ds(0, LANE)], cb.at[0]),
        (out_ref.at[:, pl.ds(SUB, mid), pl.ds(lanes - LANE, LANE)], cb.at[1]),
    ]
    loads = [pltpu.make_async_copy(hbm, buf, sem.at[s]) for s, (hbm, buf) in enumerate(wins)]
    for c in loads:
        c.start()
    for c in loads:
        c.wait()
    lane_id = lax.broadcasted_iota(jnp.int32, (rows, LANE), 1)
    row_lane = lax.broadcasted_iota(jnp.int32, (SUB, LANE), 1)
    for f in range(nf):
        west = jnp.where(lane_id == 0, side_w * tile_t(gl_ref[f:f + 1, :]), 0.0)
        east = jnp.where(lane_id == LANE - 1, side_w * tile_t(gr_ref[f:f + 1, :]), 0.0)
        cb[0, f] = cb[0, f] + west[SUB:rows - SUB]
        cb[1, f] = cb[1, f] + east[SUB:rows - SUB]
        for s, lo in ((0, 0), (1, rows - SUB)):
            rb[s, f, :, 0:LANE] = rb[s, f, :, 0:LANE] + west[lo:lo + SUB]
            rb[s, f, :, lanes - LANE:lanes] = rb[s, f, :, lanes - LANE:lanes] + east[lo:lo + SUB]
        rb[0, f, 0:1, :] = rb[0, f, 0:1, :] + low_w * g0_ref[f:f + 1, :]
        rb[1, f, SUB - 1:SUB, :] = rb[1, f, SUB - 1:SUB, :] + side_w * g1_ref[f:f + 1, :]
    stores = [pltpu.make_async_copy(buf, hbm, sem.at[s]) for s, (hbm, buf) in enumerate(wins)]
    for c in stores:
        c.start()
    for c in stores:
        c.wait()


def fix_edges(out, g0, g1, gl, gr, low_w, side_w):
    nf, rows, lanes = out.shape
    vspec = pl.BlockSpec(memory_space=pltpu.VMEM)
    anyspec = pl.BlockSpec(memory_space=pl.ANY)
    return pl.pallas_call(
        functools.partial(fix_kernel, low_w, side_w),
        out_shape=jax.ShapeDtypeStruct(out.shape, jnp.float32),
        in_specs=[anyspec, vspec, vspec, vspec, vspec],
        out_specs=anyspec,
        scratch_shapes=[
            pltpu.VMEM((2, nf, SUB, lanes), jnp.float32),
            pltpu.VMEM((2, nf, rows - 2 * SUB, LANE), jnp.float32),
            pltpu.SemaphoreType.DMA((4,)),
        ],
        input_output_aliases={0: 0},
    )(out, g0, g1, gl, gr)


def shards(
    fields, react_rate, mix_matrix, activation, inlet_ids, inlet_weights, outlet_ids, outlet_weights
):
    nf, rows, lanes = fields.shape
    n_grp = lax.axis_size("grp")
    n_blk = lax.axis_size("blk")
    g = lax.axis_index("grp")
    b = lax.axis_index("blk")
    exit_grp = n_grp - 2
    turb_grp = n_grp - 1
    flags = jnp.stack([g == exit_grp, g == turb_grp]).astype(jnp.float32)

    last_row = fields[:, -1, :]
    first_row = fields[:, 0, :]
    payload = jnp.concatenate([last_row, first_row[4:5]], axis=0)
    planes = payload[None]
    spans = []
    span = n_blk // 2
    while span >= 1:
        spans.append(span)
        partner = [(i, i ^ span) for i in range(n_blk)]
        planes = jnp.concatenate([planes, lax.ppermute(planes, "blk", partner)], axis=0)
        span //= 2
    table = jnp.transpose(planes, (0, 2, 1)).reshape(n_blk * lanes, nf + 1)
    ids = jnp.concatenate([inlet_ids, outlet_ids], axis=0)
    m = jnp.bitwise_xor(ids // lanes, b)
    slot = jnp.zeros_like(m)
    for r, span in enumerate(spans):
        slot = slot + ((m // span) % 2) * (1 << r)
    ids = slot * lanes + ids % lanes
    wts = jnp.concatenate([inlet_weights, outlet_weights], axis=0)
    halo_lo = lax.ppermute(last_row, "grp", [(i, i + 1) for i in range(n_grp - 2)])
    halo_hi = lax.ppermute(first_row, "grp", [(i + 1, i) for i in range(n_grp - 2)])
    lft = lax.ppermute(fields[:, :, lanes - 1], "blk", [(i, (i + 1) % n_blk) for i in range(n_blk)])
    rgt = lax.ppermute(fields[:, :, 0], "blk", [((i + 1) % n_blk, i) for i in range(n_blk)])

    swap, halo_lo, halo_hi, lft, rgt = interpolate(flags, ids, wts, table, (halo_lo, halo_hi, lft, rgt))
    swapped = lax.ppermute(swap, "grp", [(exit_grp, turb_grp), (turb_grp, exit_grp)])

    out, elo, ehi, clo, chi = fused_step(
        fields, react_rate, mix_matrix, activation, flags, halo_lo, halo_hi, swapped, lft, rgt
    )

    g0 = lax.ppermute(ehi, "grp", [(i, i + 1) for i in range(n_grp - 2)])
    g1 = lax.ppermute(elo, "grp", [(i + 1, i) for i in range(n_grp - 2)])
    gl = lax.ppermute(chi, "blk", [(i, (i + 1) % n_blk) for i in range(n_blk)])
    gr = lax.ppermute(clo, "blk", [((i + 1) % n_blk, i) for i in range(n_blk)])
    low_w = 0.5 * (courant + diffusion)
    side_w = 0.5 * diffusion
    return fix_edges(out, g0, g1, gl, gr, low_w, side_w)


def solution(mesh):
    in_specs = (
        P(None, "grp", "blk"),
        P("grp", "blk"),
        P(),
        P(),
        P(None, "blk"),
        P(None, "blk"),
        P(None, "blk"),
        P(None, "blk"),
    )
    out_specs = P(None, "grp", "blk")
    return jax.shard_map(shards, mesh=mesh, in_specs=in_specs, out_specs=out_specs, check_vma=False)
```

```python
import functools

import jax
import jax.numpy as jnp
from jax import lax
from jax.experimental import pallas as pl
from jax.experimental.pallas import tpu as pltpu
from jax.sharding import PartitionSpec as P

courant = 0.5
diffusion = 0.1
source_step = 0.5

SUB = 8
LANE = 128


def tile_t(row):
    n = row.shape[1]
    return jnp.transpose(jnp.broadcast_to(row, (n, n)))


def step_kernel(nf, rows, lanes, mix_s, act_s, flag_s, f_hbm, rate_ref, hlo_ref, hhi_ref, sw_ref,
                lft_ref, rgt_ref, out_ref, elo_ref, ehi_ref, clo_ref, chi_ref, ext1, ext2, coef, sem):
    n_i = rows // SUB
    n_j = lanes // LANE
    top = SUB + rows
    right = LANE + lanes
    at_exit = flag_s[0] > 0.5
    at_turb = flag_s[1] > 0.5
    at_end = flag_s[0] + flag_s[1] > 0.5

    copy = pltpu.make_async_copy(f_hbm, ext1.at[:, SUB:top, LANE:right], sem.at[0])
    copy.start()
    zeros = jnp.zeros((rows, LANE), jnp.float32)
    for f in range(nf):
        inlet = sw_ref[f:f + 1, :]
        ext1[f, SUB - 1:SUB, LANE:right] = jnp.where(at_turb, inlet, hlo_ref[f:f + 1, :])
        ext2[f, SUB - 1:SUB, LANE:right] = jnp.where(at_turb, inlet, 0.0)
        ext1[f, SUB:top, 0:LANE] = tile_t(lft_ref[f:f + 1, :])
        ext1[f, SUB:top, right:right + LANE] = tile_t(rgt_ref[f:f + 1, :])
        ext2[f, SUB:top, 0:LANE] = zeros
        ext2[f, SUB:top, right:right + LANE] = zeros
    for f in range(nf):
        for g in range(nf):
            coef[f * nf + g] = jnp.full((SUB, LANE), mix_s[f, g], jnp.float32)
        coef[nf * nf + f] = jnp.full((SUB, LANE), -act_s[f], jnp.float32)
    copy.wait()

    def high_ghost(ext, halo_of):
        for f in range(nf):
            own = ext[f, top - 1:top, LANE:right]
            halo = halo_of(f)
            if f == 4:
                row = jnp.where(at_turb, own, jnp.where(at_exit, sw_ref[nf:nf + 1, :], halo))
            else:
                row = jnp.where(at_end, own, halo)
            ext[f, top:top + 1, LANE:right] = row

    high_ghost(ext1, lambda f: hhi_ref[f:f + 1, :])

    sub_id = lax.broadcasted_iota(jnp.int32, (SUB, LANE), 0)
    lane_id = lax.broadcasted_iota(jnp.int32, (SUB, LANE), 1)
    first_sub = sub_id == 0
    last_sub = sub_id == SUB - 1
    first_lane = lane_id == 0
    last_lane = lane_id == LANE - 1

    def tendency_tiles(src, r0, c0s, rate_ts):
        r = pl.multiple_of(r0 + SUB, SUB)
        r_up = pl.multiple_of(r0, SUB)
        r_dn = pl.multiple_of(r0 + 2 * SUB, SUB)
        cs = [pl.multiple_of(c0 + LANE, LANE) for c0 in c0s]
        reacts = []
        for c, rate_t in zip(cs, rate_ts):
            v4 = src[4, pl.ds(r, SUB), pl.ds(c, LANE)]
            heat = 1.0 + (jnp.maximum(v4, 0.0) + jnp.log1p(jnp.exp(-jnp.abs(v4))))
            inv_heat = 1.0 / heat
            reacts.append([
                rate_t * src[f, pl.ds(r, SUB), pl.ds(c, LANE)] * jnp.exp(coef[nf * nf + f] * inv_heat)
                for f in range(nf)
            ])
        tends = [[] for _ in cs]
        for f in range(nf):
            accs = [None] * len(cs)
            for g in range(nf):
                m = coef[f * nf + g]
                for h in range(len(cs)):
                    term = m * reacts[h][g]
                    accs[h] = term if accs[h] is None else accs[h] + term
            for h, c in enumerate(cs):
                c_w = pl.multiple_of(c - LANE, LANE)
                c_e = pl.multiple_of(c + LANE, LANE)
                v = src[f, pl.ds(r, SUB), pl.ds(c, LANE)]
                up = src[f, pl.ds(r_up, SUB), pl.ds(c, LANE)]
                down = src[f, pl.ds(r_dn, SUB), pl.ds(c, LANE)]
                west = src[f, pl.ds(r, SUB), pl.ds(c_w, LANE)]
                east = src[f, pl.ds(r, SUB), pl.ds(c_e, LANE)]
                backward = jnp.where(first_sub, pltpu.roll(up, 1, 0), pltpu.roll(v, 1, 0))
                forward = jnp.where(last_sub, pltpu.roll(down, SUB - 1, 0), pltpu.roll(v, SUB - 1, 0))
                left = jnp.where(first_lane, pltpu.roll(west, 1, 1), pltpu.roll(v, 1, 1))
                rgt = jnp.where(last_lane, pltpu.roll(east, LANE - 1, 1), pltpu.roll(v, LANE - 1, 1))
                advect = -courant * (v - backward)
                spread = diffusion * (backward + forward + left + rgt - 4.0 * v)
                tends[h].append((v, advect + spread + source_step * accs[h]))
        return tends

    pair = 2 if n_j % 2 == 0 else 1
    n_jp = n_j // pair

    def tile_offsets(t):
        i = t // n_jp
        jp = t % n_jp
        r0 = pl.multiple_of(i * SUB, SUB)
        c0s = [pl.multiple_of((jp * pair + h) * LANE, LANE) for h in range(pair)]
        return r0, c0s

    def stage_one(t, carry):
        r0, c0s = tile_offsets(t)
        rate_ts = [rate_ref[pl.ds(r0, SUB), pl.ds(c0, LANE)] for c0 in c0s]
        tends = tendency_tiles(ext1, r0, c0s, rate_ts)
        r = pl.multiple_of(r0 + SUB, SUB)
        for c0, tend in zip(c0s, tends):
            c = pl.multiple_of(c0 + LANE, LANE)
            for f in range(nf):
                v, tf = tend[f]
                ext2[f, pl.ds(r, SUB), pl.ds(c, LANE)] = v + tf
        return carry

    lax.fori_loop(0, n_i * n_jp, stage_one, 0)

    high_ghost(ext2, lambda f: jnp.zeros((1, lanes), jnp.float32))

    def stage_two(t, carry):
        r0, c0s = tile_offsets(t)
        rate_ts = [rate_ref[pl.ds(r0, SUB), pl.ds(c0, LANE)] for c0 in c0s]
        tends = tendency_tiles(ext2, r0, c0s, rate_ts)
        r = pl.multiple_of(r0 + SUB, SUB)
        for c0, tend in zip(c0s, tends):
            c = pl.multiple_of(c0 + LANE, LANE)
            for f in range(nf):
                v, tf = tend[f]
                base = ext1[f, pl.ds(r, SUB), pl.ds(c, LANE)]
                out_ref[f, pl.ds(r0, SUB), pl.ds(c0, LANE)] = 0.5 * (base + v + tf)
        return carry

    lax.fori_loop(0, n_i * n_jp, stage_two, 0)

    for f in range(nf):
        elo_ref[f:f + 1, :] = ext2[f, SUB:SUB + 1, LANE:right]
        ehi_ref[f:f + 1, :] = ext2[f, top - 1:top, LANE:right]
        west = jnp.transpose(ext2[f, SUB:top, LANE:2 * LANE])
        east = jnp.transpose(ext2[f, SUB:top, right - LANE:right])
        clo_ref[f:f + 1, :] = west[0:1, :]
        chi_ref[f:f + 1, :] = east[LANE - 1:LANE, :]


def fused_step(fields, rate, mix, act, flags, halo_lo, halo_hi, swapped, lft, rgt):
    nf, rows, lanes = fields.shape
    vmem = pltpu.VMEM
    smem = pl.BlockSpec(memory_space=pltpu.SMEM)
    vspec = pl.BlockSpec(memory_space=vmem)
    cells = rows * lanes
    cost = pl.CostEstimate(
        flops=2 * cells * nf * (2 * nf + 24),
        transcendentals=2 * cells * (nf + 3),
        bytes_accessed=4 * cells * (2 * nf + 1),
    )
    return pl.pallas_call(
        functools.partial(step_kernel, nf, rows, lanes),
        out_shape=(
            jax.ShapeDtypeStruct((nf, rows, lanes), jnp.float32),
            jax.ShapeDtypeStruct((nf, lanes), jnp.float32),
            jax.ShapeDtypeStruct((nf, lanes), jnp.float32),
            jax.ShapeDtypeStruct((nf, rows), jnp.float32),
            jax.ShapeDtypeStruct((nf, rows), jnp.float32),
        ),
        in_specs=[smem, smem, smem, pl.BlockSpec(memory_space=pl.ANY)] + [vspec] * 6,
        out_specs=(vspec,) * 5,
        scratch_shapes=[
            vmem((nf, rows + 2 * SUB, lanes + 2 * LANE), jnp.float32),
            vmem((nf, rows + 2 * SUB, lanes + 2 * LANE), jnp.float32),
            vmem((nf * nf + nf, SUB, LANE), jnp.float32),
            pltpu.SemaphoreType.DMA((1,)),
        ],
        compiler_params=pltpu.CompilerParams(vmem_limit_bytes=60 * 1024 * 1024),
        cost_estimate=cost,
    )(mix, act, flags, fields, rate, halo_lo, halo_hi, swapped, lft, rgt)


def interp_kernel(ks, flag_s, ids_s, wt_ref, table_ref, *refs):
    n_pass = (len(refs) - 3) // 2
    ins, o_ref, outs, acc, picked = refs[:n_pass], refs[n_pass], refs[n_pass + 1:-2], refs[-2], refs[-1]
    lanes = o_ref.shape[1]
    width = table_ref.shape[1]
    acc[...] = jnp.zeros(acc.shape, jnp.float32)

    @pl.when(flag_s[0] + flag_s[1] > 0.5)
    def _():
        def group(pg, carry):
            p0 = pl.multiple_of(pg * SUB, SUB)
            for s in range(SUB):
                for k in range(ks):
                    q = ids_s[k, p0 + s]
                    picked[k, pl.ds(p0 + s, 1), :] = table_ref[pl.ds(q, 1), :]
            return carry

        lax.fori_loop(0, lanes // SUB, group, 0)
        total = wt_ref[:, 0:1] * picked[0]
        for k in range(1, ks):
            total = total + wt_ref[:, k:k + 1] * picked[k]
        acc[:, 0:width] = total

    o_ref[...] = jnp.transpose(acc[...])[0:o_ref.shape[0], :]
    for src, dst in zip(ins, outs):
        dst[...] = src[...]


def interpolate(flags, ids, wt, table, passed):
    ks, lanes = ids.shape
    smem = pl.BlockSpec(memory_space=pltpu.SMEM)
    vspec = pl.BlockSpec(memory_space=pltpu.VMEM)
    width = table.shape[1]
    return pl.pallas_call(
        functools.partial(interp_kernel, ks),
        out_shape=(jax.ShapeDtypeStruct((width, lanes), jnp.float32),)
        + tuple(jax.ShapeDtypeStruct(x.shape, x.dtype) for x in passed),
        in_specs=[smem, smem] + [vspec] * (2 + len(passed)),
        out_specs=(vspec,) * (1 + len(passed)),
        scratch_shapes=[
            pltpu.VMEM((lanes, LANE), jnp.float32),
            pltpu.VMEM((ks, lanes, width), jnp.float32),
        ],
    )(flags, ids, wt, table, *passed)


def fix_kernel(low_w, side_w, out_in, g0_ref, g1_ref, gl_ref, gr_ref, out_ref, rb, cb, sem):
    nf, rows, lanes = out_ref.shape
    mid = rows - 2 * SUB
    wins = [
        (out_ref.at[:, pl.ds(0, SUB), :], rb.at[0]),
        (out_ref.at[:, pl.ds(rows - SUB, SUB), :], rb.at[1]),
        (out_ref.at[:, pl.ds(SUB, mid), pl.ds(0, LANE)], cb.at[0]),
        (out_ref.at[:, pl.ds(SUB, mid), pl.ds(lanes - LANE, LANE)], cb.at[1]),
    ]
    loads = [pltpu.make_async_copy(hbm, buf, sem.at[s]) for s, (hbm, buf) in enumerate(wins)]
    for c in loads:
        c.start()
    for c in loads:
        c.wait()
    lane_id = lax.broadcasted_iota(jnp.int32, (rows, LANE), 1)
    row_lane = lax.broadcasted_iota(jnp.int32, (SUB, LANE), 1)
    for f in range(nf):
        west = jnp.where(lane_id == 0, side_w * tile_t(gl_ref[f:f + 1, :]), 0.0)
        east = jnp.where(lane_id == LANE - 1, side_w * tile_t(gr_ref[f:f + 1, :]), 0.0)
        cb[0, f] = cb[0, f] + west[SUB:rows - SUB]
        cb[1, f] = cb[1, f] + east[SUB:rows - SUB]
        for s, lo in ((0, 0), (1, rows - SUB)):
            rb[s, f, :, 0:LANE] = rb[s, f, :, 0:LANE] + west[lo:lo + SUB]
            rb[s, f, :, lanes - LANE:lanes] = rb[s, f, :, lanes - LANE:lanes] + east[lo:lo + SUB]
        rb[0, f, 0:1, :] = rb[0, f, 0:1, :] + low_w * g0_ref[f:f + 1, :]
        rb[1, f, SUB - 1:SUB, :] = rb[1, f, SUB - 1:SUB, :] + side_w * g1_ref[f:f + 1, :]
    stores = [pltpu.make_async_copy(buf, hbm, sem.at[s]) for s, (hbm, buf) in enumerate(wins)]
    for c in stores:
        c.start()
    for c in stores:
        c.wait()


def fix_edges(out, g0, g1, gl, gr, low_w, side_w):
    nf, rows, lanes = out.shape
    vspec = pl.BlockSpec(memory_space=pltpu.VMEM)
    anyspec = pl.BlockSpec(memory_space=pl.ANY)
    return pl.pallas_call(
        functools.partial(fix_kernel, low_w, side_w),
        out_shape=jax.ShapeDtypeStruct(out.shape, jnp.float32),
        in_specs=[anyspec, vspec, vspec, vspec, vspec],
        out_specs=anyspec,
        scratch_shapes=[
            pltpu.VMEM((2, nf, SUB, lanes), jnp.float32),
            pltpu.VMEM((2, nf, rows - 2 * SUB, LANE), jnp.float32),
            pltpu.SemaphoreType.DMA((4,)),
        ],
        input_output_aliases={0: 0},
    )(out, g0, g1, gl, gr)


def shards(
    fields, react_rate, mix_matrix, activation, inlet_ids, inlet_weights, outlet_ids, outlet_weights
):
    nf, rows, lanes = fields.shape
    n_grp = lax.axis_size("grp")
    n_blk = lax.axis_size("blk")
    g = lax.axis_index("grp")
    b = lax.axis_index("blk")
    exit_grp = n_grp - 2
    turb_grp = n_grp - 1
    flags = jnp.stack([g == exit_grp, g == turb_grp]).astype(jnp.float32)

    last_row = fields[:, -1, :]
    first_row = fields[:, 0, :]
    payload = jnp.concatenate([last_row, first_row[4:5]], axis=0)
    planes = payload[None]
    spans = []
    span = n_blk // 2
    while span >= 1:
        spans.append(span)
        partner = [(i, i ^ span) for i in range(n_blk)]
        planes = jnp.concatenate([planes, lax.ppermute(planes, "blk", partner)], axis=0)
        span //= 2
    table = jnp.transpose(planes, (0, 2, 1)).reshape(n_blk * lanes, nf + 1)
    at_exit = g == exit_grp
    ids = jnp.where(at_exit, inlet_ids, outlet_ids)
    m = jnp.bitwise_xor(ids // lanes, b)
    slot = jnp.zeros_like(m)
    for r, span in enumerate(spans):
        slot = slot + ((m // span) % 2) * (1 << r)
    ids = slot * lanes + ids % lanes
    wt = jnp.transpose(jnp.where(at_exit, inlet_weights, outlet_weights))
    halo_lo = lax.ppermute(last_row, "grp", [(i, i + 1) for i in range(n_grp - 2)])
    halo_hi = lax.ppermute(first_row, "grp", [(i + 1, i) for i in range(n_grp - 2)])
    lft = lax.ppermute(fields[:, :, lanes - 1], "blk", [(i, (i + 1) % n_blk) for i in range(n_blk)])
    rgt = lax.ppermute(fields[:, :, 0], "blk", [((i + 1) % n_blk, i) for i in range(n_blk)])

    swap, halo_lo, halo_hi, lft, rgt = interpolate(flags, ids, wt, table, (halo_lo, halo_hi, lft, rgt))
    swapped = lax.ppermute(swap, "grp", [(exit_grp, turb_grp), (turb_grp, exit_grp)])

    out, elo, ehi, clo, chi = fused_step(
        fields, react_rate, mix_matrix, activation, flags, halo_lo, halo_hi, swapped, lft, rgt
    )

    g0 = lax.ppermute(ehi, "grp", [(i, i + 1) for i in range(n_grp - 2)])
    g1 = lax.ppermute(elo, "grp", [(i + 1, i) for i in range(n_grp - 2)])
    gl = lax.ppermute(chi, "blk", [(i, (i + 1) % n_blk) for i in range(n_blk)])
    gr = lax.ppermute(clo, "blk", [((i + 1) % n_blk, i) for i in range(n_blk)])
    low_w = 0.5 * (courant + diffusion)
    side_w = 0.5 * diffusion
    return fix_edges(out, g0, g1, gl, gr, low_w, side_w)


def solution(mesh):
    in_specs = (
        P(None, "grp", "blk"),
        P("grp", "blk"),
        P(),
        P(),
        P(None, "blk"),
        P(None, "blk"),
        P(None, "blk"),
        P(None, "blk"),
    )
    out_specs = P(None, "grp", "blk")
    return jax.shard_map(shards, mesh=mesh, in_specs=in_specs, out_specs=out_specs, check_vma=False)
```

```python
import functools

import jax
import jax.numpy as jnp
from jax import lax
from jax.experimental import pallas as pl
from jax.experimental.pallas import tpu as pltpu
from jax.sharding import PartitionSpec as P

courant = 0.5
diffusion = 0.1
source_step = 0.5

SUB = 8
LANE = 128


def tile_t(row):
    n = row.shape[1]
    return jnp.transpose(jnp.broadcast_to(row, (n, n)))


def step_kernel(nf, rows, lanes, mix_s, act_s, flag_s, f_hbm, rate_ref, hlo_ref, hhi_ref, sw_ref,
                lft_ref, rgt_ref, out_hbm, elo_ref, ehi_ref, clo_ref, chi_ref, ext1, ext2, coef, obuf,
                sem):
    n_i = rows // SUB
    n_j = lanes // LANE
    top = SUB + rows
    right = LANE + lanes
    at_exit = flag_s[0] > 0.5
    at_turb = flag_s[1] > 0.5
    at_end = flag_s[0] + flag_s[1] > 0.5

    copy = pltpu.make_async_copy(f_hbm, ext1.at[:, SUB:top, LANE:right], sem.at[0])
    copy.start()
    zeros = jnp.zeros((rows, LANE), jnp.float32)
    for f in range(nf):
        inlet = sw_ref[f:f + 1, :]
        ext1[f, SUB - 1:SUB, LANE:right] = jnp.where(at_turb, inlet, hlo_ref[f:f + 1, :])
        ext2[f, SUB - 1:SUB, LANE:right] = jnp.where(at_turb, inlet, 0.0)
        ext1[f, SUB:top, 0:LANE] = tile_t(lft_ref[f:f + 1, :])
        ext1[f, SUB:top, right:right + LANE] = tile_t(rgt_ref[f:f + 1, :])
        ext2[f, SUB:top, 0:LANE] = zeros
        ext2[f, SUB:top, right:right + LANE] = zeros
    for f in range(nf):
        for g in range(nf):
            coef[f * nf + g] = jnp.full((SUB, LANE), source_step * mix_s[f, g], jnp.float32)
        coef[nf * nf + f] = jnp.full((SUB, LANE), -act_s[f], jnp.float32)
    copy.wait()

    def high_ghost(ext, halo_of):
        for f in range(nf):
            own = ext[f, top - 1:top, LANE:right]
            halo = halo_of(f)
            if f == 4:
                row = jnp.where(at_turb, own, jnp.where(at_exit, sw_ref[nf:nf + 1, :], halo))
            else:
                row = jnp.where(at_end, own, halo)
            ext[f, top:top + 1, LANE:right] = row

    high_ghost(ext1, lambda f: hhi_ref[f:f + 1, :])

    sub_id = lax.broadcasted_iota(jnp.int32, (SUB, LANE), 0)
    lane_id = lax.broadcasted_iota(jnp.int32, (SUB, LANE), 1)
    first_sub = sub_id == 0
    last_sub = sub_id == SUB - 1
    first_lane = lane_id == 0
    last_lane = lane_id == LANE - 1

    def tendency_tiles(src, r0, c0s, rate_ts):
        r = pl.multiple_of(r0 + SUB, SUB)
        r_up = pl.multiple_of(r0, SUB)
        r_dn = pl.multiple_of(r0 + 2 * SUB, SUB)
        cs = [pl.multiple_of(c0 + LANE, LANE) for c0 in c0s]
        reacts = []
        for c, rate_t in zip(cs, rate_ts):
            v4 = src[4, pl.ds(r, SUB), pl.ds(c, LANE)]
            heat = 1.0 + (jnp.maximum(v4, 0.0) + jnp.log1p(jnp.exp(-jnp.abs(v4))))
            inv_heat = 1.0 / heat
            reacts.append([
                rate_t * src[f, pl.ds(r, SUB), pl.ds(c, LANE)] * jnp.exp(coef[nf * nf + f] * inv_heat)
                for f in range(nf)
            ])
        tends = [[] for _ in cs]
        for f in range(nf):
            accs = [None] * len(cs)
            for g in range(nf):
                m = coef[f * nf + g]
                for h in range(len(cs)):
                    term = m * reacts[h][g]
                    accs[h] = term if accs[h] is None else accs[h] + term
            for h, c in enumerate(cs):
                c_w = pl.multiple_of(c - LANE, LANE)
                c_e = pl.multiple_of(c + LANE, LANE)
                v = src[f, pl.ds(r, SUB), pl.ds(c, LANE)]
                up = src[f, pl.ds(r_up, SUB), pl.ds(c, LANE)]
                down = src[f, pl.ds(r_dn, SUB), pl.ds(c, LANE)]
                west = src[f, pl.ds(r, SUB), pl.ds(c_w, LANE)]
                east = src[f, pl.ds(r, SUB), pl.ds(c_e, LANE)]
                backward = jnp.where(first_sub, pltpu.roll(up, 1, 0), pltpu.roll(v, 1, 0))
                forward = jnp.where(last_sub, pltpu.roll(down, SUB - 1, 0), pltpu.roll(v, SUB - 1, 0))
                left = jnp.where(first_lane, pltpu.roll(west, 1, 1), pltpu.roll(v, 1, 1))
                rgt = jnp.where(last_lane, pltpu.roll(east, LANE - 1, 1), pltpu.roll(v, LANE - 1, 1))
                flow = (courant + diffusion) * backward + diffusion * (forward + left + rgt)
                flow = flow - (courant + 4.0 * diffusion) * v
                tends[h].append((v, flow + accs[h]))
        return tends

    pair = 2 if n_j % 2 == 0 else 1
    n_jp = n_j // pair

    def tile_offsets(t):
        i = t // n_jp
        jp = t % n_jp
        r0 = pl.multiple_of(i * SUB, SUB)
        c0s = [pl.multiple_of((jp * pair + h) * LANE, LANE) for h in range(pair)]
        return r0, c0s

    def stage_one(t, carry):
        r0, c0s = tile_offsets(t)
        rate_ts = [rate_ref[pl.ds(r0, SUB), pl.ds(c0, LANE)] for c0 in c0s]
        tends = tendency_tiles(ext1, r0, c0s, rate_ts)
        r = pl.multiple_of(r0 + SUB, SUB)
        for c0, tend in zip(c0s, tends):
            c = pl.multiple_of(c0 + LANE, LANE)
            for f in range(nf):
                v, tf = tend[f]
                ext2[f, pl.ds(r, SUB), pl.ds(c, LANE)] = v + tf
        return carry

    lax.fori_loop(0, n_i * n_jp, stage_one, 0)

    high_ghost(ext2, lambda f: jnp.zeros((1, lanes), jnp.float32))

    def stage_two(i, carry):
        for jp in range(n_jp):
            r0, c0s = tile_offsets(i * n_jp + jp)
            rate_ts = [rate_ref[pl.ds(r0, SUB), pl.ds(c0, LANE)] for c0 in c0s]
            tends = tendency_tiles(ext2, r0, c0s, rate_ts)
            r = pl.multiple_of(r0 + SUB, SUB)
            for c0, tend in zip(c0s, tends):
                c = pl.multiple_of(c0 + LANE, LANE)
                for f in range(nf):
                    v, tf = tend[f]
                    base = ext1[f, pl.ds(r, SUB), pl.ds(c, LANE)]
                    obuf[f, pl.ds(r0, SUB), pl.ds(c0, LANE)] = 0.5 * (base + v + tf)
        r0 = pl.multiple_of(i * SUB, SUB)
        pltpu.make_async_copy(
            obuf.at[:, pl.ds(r0, SUB), :], out_hbm.at[:, pl.ds(r0, SUB), :], sem.at[1]
        ).start()
        return carry

    lax.fori_loop(0, n_i, stage_two, 0)

    for f in range(nf):
        elo_ref[f:f + 1, :] = ext2[f, SUB:SUB + 1, LANE:right]
        ehi_ref[f:f + 1, :] = ext2[f, top - 1:top, LANE:right]
        west = jnp.transpose(ext2[f, SUB:top, LANE:2 * LANE])
        east = jnp.transpose(ext2[f, SUB:top, right - LANE:right])
        clo_ref[f:f + 1, :] = west[0:1, :]
        chi_ref[f:f + 1, :] = east[LANE - 1:LANE, :]
    pltpu.make_async_copy(obuf, out_hbm, sem.at[1]).wait()


def fused_step(fields, rate, mix, act, flags, halo_lo, halo_hi, swapped, lft, rgt):
    nf, rows, lanes = fields.shape
    vmem = pltpu.VMEM
    smem = pl.BlockSpec(memory_space=pltpu.SMEM)
    vspec = pl.BlockSpec(memory_space=vmem)
    cells = rows * lanes
    cost = pl.CostEstimate(
        flops=2 * cells * nf * (2 * nf + 24),
        transcendentals=2 * cells * (nf + 3),
        bytes_accessed=4 * cells * (2 * nf + 1),
    )
    return pl.pallas_call(
        functools.partial(step_kernel, nf, rows, lanes),
        out_shape=(
            jax.ShapeDtypeStruct((nf, rows, lanes), jnp.float32),
            jax.ShapeDtypeStruct((nf, lanes), jnp.float32),
            jax.ShapeDtypeStruct((nf, lanes), jnp.float32),
            jax.ShapeDtypeStruct((nf, rows), jnp.float32),
            jax.ShapeDtypeStruct((nf, rows), jnp.float32),
        ),
        in_specs=[smem, smem, smem, pl.BlockSpec(memory_space=pl.ANY)] + [vspec] * 6,
        out_specs=(pl.BlockSpec(memory_space=pl.ANY),) + (vspec,) * 4,
        scratch_shapes=[
            vmem((nf, rows + 2 * SUB, lanes + 2 * LANE), jnp.float32),
            vmem((nf, rows + 2 * SUB, lanes + 2 * LANE), jnp.float32),
            vmem((nf * nf + nf, SUB, LANE), jnp.float32),
            vmem((nf, rows, lanes), jnp.float32),
            pltpu.SemaphoreType.DMA((2,)),
        ],
        compiler_params=pltpu.CompilerParams(vmem_limit_bytes=60 * 1024 * 1024),
        cost_estimate=cost,
    )(mix, act, flags, fields, rate, halo_lo, halo_hi, swapped, lft, rgt)


def interp_kernel(ks, flag_s, ids_s, wt_ref, table_ref, *refs):
    n_pass = (len(refs) - 3) // 2
    ins, o_ref, outs, acc, picked = refs[:n_pass], refs[n_pass], refs[n_pass + 1:-2], refs[-2], refs[-1]
    lanes = o_ref.shape[1]
    width = table_ref.shape[1]
    acc[...] = jnp.zeros(acc.shape, jnp.float32)

    @pl.when(flag_s[0] + flag_s[1] > 0.5)
    def _():
        def group(pg, carry):
            p0 = pl.multiple_of(pg * SUB, SUB)
            for s in range(SUB):
                for k in range(ks):
                    q = ids_s[k, p0 + s]
                    picked[k, pl.ds(p0 + s, 1), :] = table_ref[pl.ds(q, 1), :]
            return carry

        lax.fori_loop(0, lanes // SUB, group, 0)
        total = wt_ref[:, 0:1] * picked[0]
        for k in range(1, ks):
            total = total + wt_ref[:, k:k + 1] * picked[k]
        acc[:, 0:width] = total

    o_ref[...] = jnp.transpose(acc[...])[0:o_ref.shape[0], :]
    for src, dst in zip(ins, outs):
        dst[...] = src[...]


def interpolate(flags, ids, wt, table, passed):
    ks, lanes = ids.shape
    smem = pl.BlockSpec(memory_space=pltpu.SMEM)
    vspec = pl.BlockSpec(memory_space=pltpu.VMEM)
    width = table.shape[1]
    return pl.pallas_call(
        functools.partial(interp_kernel, ks),
        out_shape=(jax.ShapeDtypeStruct((width, lanes), jnp.float32),)
        + tuple(jax.ShapeDtypeStruct(x.shape, x.dtype) for x in passed),
        in_specs=[smem, smem] + [vspec] * (2 + len(passed)),
        out_specs=(vspec,) * (1 + len(passed)),
        scratch_shapes=[
            pltpu.VMEM((lanes, LANE), jnp.float32),
            pltpu.VMEM((ks, lanes, width), jnp.float32),
        ],
    )(flags, ids, wt, table, *passed)


def fix_kernel(low_w, side_w, out_in, g0_ref, g1_ref, gl_ref, gr_ref, out_ref, rb, cb, sem):
    nf, rows, lanes = out_ref.shape
    mid = rows - 2 * SUB
    wins = [
        (out_ref.at[:, pl.ds(0, SUB), :], rb.at[0]),
        (out_ref.at[:, pl.ds(rows - SUB, SUB), :], rb.at[1]),
        (out_ref.at[:, pl.ds(SUB, mid), pl.ds(0, LANE)], cb.at[0]),
        (out_ref.at[:, pl.ds(SUB, mid), pl.ds(lanes - LANE, LANE)], cb.at[1]),
    ]
    loads = [pltpu.make_async_copy(hbm, buf, sem.at[s]) for s, (hbm, buf) in enumerate(wins)]
    for c in loads:
        c.start()
    for c in loads:
        c.wait()
    lane_id = lax.broadcasted_iota(jnp.int32, (rows, LANE), 1)
    row_lane = lax.broadcasted_iota(jnp.int32, (SUB, LANE), 1)
    for f in range(nf):
        west = jnp.where(lane_id == 0, side_w * tile_t(gl_ref[f:f + 1, :]), 0.0)
        east = jnp.where(lane_id == LANE - 1, side_w * tile_t(gr_ref[f:f + 1, :]), 0.0)
        cb[0, f] = cb[0, f] + west[SUB:rows - SUB]
        cb[1, f] = cb[1, f] + east[SUB:rows - SUB]
        for s, lo in ((0, 0), (1, rows - SUB)):
            rb[s, f, :, 0:LANE] = rb[s, f, :, 0:LANE] + west[lo:lo + SUB]
            rb[s, f, :, lanes - LANE:lanes] = rb[s, f, :, lanes - LANE:lanes] + east[lo:lo + SUB]
        rb[0, f, 0:1, :] = rb[0, f, 0:1, :] + low_w * g0_ref[f:f + 1, :]
        rb[1, f, SUB - 1:SUB, :] = rb[1, f, SUB - 1:SUB, :] + side_w * g1_ref[f:f + 1, :]
    stores = [pltpu.make_async_copy(buf, hbm, sem.at[s]) for s, (hbm, buf) in enumerate(wins)]
    for c in stores:
        c.start()
    for c in stores:
        c.wait()


def fix_edges(out, g0, g1, gl, gr, low_w, side_w):
    nf, rows, lanes = out.shape
    vspec = pl.BlockSpec(memory_space=pltpu.VMEM)
    anyspec = pl.BlockSpec(memory_space=pl.ANY)
    return pl.pallas_call(
        functools.partial(fix_kernel, low_w, side_w),
        out_shape=jax.ShapeDtypeStruct(out.shape, jnp.float32),
        in_specs=[anyspec, vspec, vspec, vspec, vspec],
        out_specs=anyspec,
        scratch_shapes=[
            pltpu.VMEM((2, nf, SUB, lanes), jnp.float32),
            pltpu.VMEM((2, nf, rows - 2 * SUB, LANE), jnp.float32),
            pltpu.SemaphoreType.DMA((4,)),
        ],
        input_output_aliases={0: 0},
    )(out, g0, g1, gl, gr)


def shards(
    fields, react_rate, mix_matrix, activation, inlet_ids, inlet_weights, outlet_ids, outlet_weights
):
    nf, rows, lanes = fields.shape
    n_grp = lax.axis_size("grp")
    n_blk = lax.axis_size("blk")
    g = lax.axis_index("grp")
    b = lax.axis_index("blk")
    exit_grp = n_grp - 2
    turb_grp = n_grp - 1
    flags = jnp.stack([g == exit_grp, g == turb_grp]).astype(jnp.float32)

    last_row = fields[:, -1, :]
    first_row = fields[:, 0, :]
    payload = jnp.concatenate([last_row, first_row[4:5]], axis=0)
    planes = payload[None]
    spans = []
    span = n_blk // 2
    while span >= 1:
        spans.append(span)
        partner = [(i, i ^ span) for i in range(n_blk)]
        planes = jnp.concatenate([planes, lax.ppermute(planes, "blk", partner)], axis=0)
        span //= 2
    table = jnp.transpose(planes, (0, 2, 1)).reshape(n_blk * lanes, nf + 1)
    at_exit = g == exit_grp
    ids = jnp.where(at_exit, inlet_ids, outlet_ids)
    m = jnp.bitwise_xor(ids // lanes, b)
    slot = jnp.zeros_like(m)
    for r, span in enumerate(spans):
        slot = slot + ((m // span) % 2) * (1 << r)
    ids = slot * lanes + ids % lanes
    wt = jnp.transpose(jnp.where(at_exit, inlet_weights, outlet_weights))
    halo_lo = lax.ppermute(last_row, "grp", [(i, i + 1) for i in range(n_grp - 2)])
    halo_hi = lax.ppermute(first_row, "grp", [(i + 1, i) for i in range(n_grp - 2)])
    lft = lax.ppermute(fields[:, :, lanes - 1], "blk", [(i, (i + 1) % n_blk) for i in range(n_blk)])
    rgt = lax.ppermute(fields[:, :, 0], "blk", [((i + 1) % n_blk, i) for i in range(n_blk)])

    swap, halo_lo, halo_hi, lft, rgt = interpolate(flags, ids, wt, table, (halo_lo, halo_hi, lft, rgt))
    swapped = lax.ppermute(swap, "grp", [(exit_grp, turb_grp), (turb_grp, exit_grp)])

    out, elo, ehi, clo, chi = fused_step(
        fields, react_rate, mix_matrix, activation, flags, halo_lo, halo_hi, swapped, lft, rgt
    )

    g0 = lax.ppermute(ehi, "grp", [(i, i + 1) for i in range(n_grp - 2)])
    g1 = lax.ppermute(elo, "grp", [(i + 1, i) for i in range(n_grp - 2)])
    gl = lax.ppermute(chi, "blk", [(i, (i + 1) % n_blk) for i in range(n_blk)])
    gr = lax.ppermute(clo, "blk", [((i + 1) % n_blk, i) for i in range(n_blk)])
    low_w = 0.5 * (courant + diffusion)
    side_w = 0.5 * diffusion
    return fix_edges(out, g0, g1, gl, gr, low_w, side_w)


def solution(mesh):
    in_specs = (
        P(None, "grp", "blk"),
        P("grp", "blk"),
        P(),
        P(),
        P(None, "blk"),
        P(None, "blk"),
        P(None, "blk"),
        P(None, "blk"),
    )
    out_specs = P(None, "grp", "blk")
    return jax.shard_map(shards, mesh=mesh, in_specs=in_specs, out_specs=out_specs, check_vma=False)
```

```python
import functools

import jax
import jax.numpy as jnp
from jax import lax
from jax.experimental import pallas as pl
from jax.experimental.pallas import tpu as pltpu
from jax.sharding import PartitionSpec as P

courant = 0.5
diffusion = 0.1
source_step = 0.5

SUB = 8
LANE = 128


def tile_t(row):
    n = row.shape[1]
    return jnp.transpose(jnp.broadcast_to(row, (n, n)))


def step_kernel(nf, rows, lanes, mix_s, act_s, flag_s, f_hbm, rate_ref, hlo_ref, hhi_ref, sw_ref,
                lft_ref, rgt_ref, out_hbm, elo_ref, ehi_ref, clo_ref, chi_ref, ext1, ext2, coef, obuf,
                sem):
    n_i = rows // SUB
    n_j = lanes // LANE
    top = SUB + rows
    right = LANE + lanes
    at_exit = flag_s[0] > 0.5
    at_turb = flag_s[1] > 0.5
    at_end = flag_s[0] + flag_s[1] > 0.5

    copy = pltpu.make_async_copy(f_hbm, ext1.at[:, SUB:top, LANE:right], sem.at[0])
    copy.start()
    zeros = jnp.zeros((rows, LANE), jnp.float32)
    for f in range(nf):
        inlet = sw_ref[f:f + 1, :]
        ext1[f, SUB - 1:SUB, LANE:right] = jnp.where(at_turb, inlet, hlo_ref[f:f + 1, :])
        ext2[f, SUB - 1:SUB, LANE:right] = jnp.where(at_turb, inlet, 0.0)
        ext1[f, SUB:top, 0:LANE] = tile_t(lft_ref[f:f + 1, :])
        ext1[f, SUB:top, right:right + LANE] = tile_t(rgt_ref[f:f + 1, :])
        ext2[f, SUB:top, 0:LANE] = zeros
        ext2[f, SUB:top, right:right + LANE] = zeros
    for f in range(nf):
        for g in range(nf):
            coef[f * nf + g] = jnp.full((SUB, LANE), source_step * mix_s[f, g], jnp.float32)
        coef[nf * nf + f] = jnp.full((SUB, LANE), -act_s[f], jnp.float32)
    copy.wait()

    def high_ghost(ext, halo_of):
        for f in range(nf):
            own = ext[f, top - 1:top, LANE:right]
            halo = halo_of(f)
            if f == 4:
                row = jnp.where(at_turb, own, jnp.where(at_exit, sw_ref[nf:nf + 1, :], halo))
            else:
                row = jnp.where(at_end, own, halo)
            ext[f, top:top + 1, LANE:right] = row

    high_ghost(ext1, lambda f: hhi_ref[f:f + 1, :])

    sub_id = lax.broadcasted_iota(jnp.int32, (SUB, LANE), 0)
    lane_id = lax.broadcasted_iota(jnp.int32, (SUB, LANE), 1)
    first_sub = sub_id == 0
    last_sub = sub_id == SUB - 1
    first_lane = lane_id == 0
    last_lane = lane_id == LANE - 1

    def tendency_tiles(src, r0, c0s, rate_ts):
        r = pl.multiple_of(r0 + SUB, SUB)
        r_up = pl.multiple_of(r0, SUB)
        r_dn = pl.multiple_of(r0 + 2 * SUB, SUB)
        cs = [pl.multiple_of(c0 + LANE, LANE) for c0 in c0s]
        reacts = []
        for c, rate_t in zip(cs, rate_ts):
            v4 = src[4, pl.ds(r, SUB), pl.ds(c, LANE)]
            heat = 1.0 + (jnp.maximum(v4, 0.0) + jnp.log1p(jnp.exp(-jnp.abs(v4))))
            inv_heat = 1.0 / heat
            reacts.append([
                rate_t * src[f, pl.ds(r, SUB), pl.ds(c, LANE)] * jnp.exp(coef[nf * nf + f] * inv_heat)
                for f in range(nf)
            ])
        tends = [[] for _ in cs]
        for f in range(nf):
            accs = [None] * len(cs)
            for g in range(nf):
                m = coef[f * nf + g]
                for h in range(len(cs)):
                    term = m * reacts[h][g]
                    accs[h] = term if accs[h] is None else accs[h] + term
            for h, c in enumerate(cs):
                c_w = pl.multiple_of(c - LANE, LANE)
                c_e = pl.multiple_of(c + LANE, LANE)
                v = src[f, pl.ds(r, SUB), pl.ds(c, LANE)]
                up = src[f, pl.ds(r_up, SUB), pl.ds(c, LANE)]
                down = src[f, pl.ds(r_dn, SUB), pl.ds(c, LANE)]
                west = src[f, pl.ds(r, SUB), pl.ds(c_w, LANE)]
                east = src[f, pl.ds(r, SUB), pl.ds(c_e, LANE)]
                backward = jnp.where(first_sub, pltpu.roll(up, 1, 0), pltpu.roll(v, 1, 0))
                forward = jnp.where(last_sub, pltpu.roll(down, SUB - 1, 0), pltpu.roll(v, SUB - 1, 0))
                left = jnp.where(first_lane, pltpu.roll(west, 1, 1), pltpu.roll(v, 1, 1))
                rgt = jnp.where(last_lane, pltpu.roll(east, LANE - 1, 1), pltpu.roll(v, LANE - 1, 1))
                flow = (courant + diffusion) * backward + diffusion * (forward + left + rgt)
                flow = flow - (courant + 4.0 * diffusion) * v
                tends[h].append((v, flow + accs[h]))
        return tends

    pair = 2 if n_j % 2 == 0 else 1
    n_jp = n_j // pair

    def tile_offsets(t):
        i = t // n_jp
        jp = t % n_jp
        r0 = pl.multiple_of(i * SUB, SUB)
        c0s = [pl.multiple_of((jp * pair + h) * LANE, LANE) for h in range(pair)]
        return r0, c0s

    def stage_one(t, carry):
        r0, c0s = tile_offsets(t)
        rate_ts = [rate_ref[pl.ds(r0, SUB), pl.ds(c0, LANE)] for c0 in c0s]
        tends = tendency_tiles(ext1, r0, c0s, rate_ts)
        r = pl.multiple_of(r0 + SUB, SUB)
        for c0, tend in zip(c0s, tends):
            c = pl.multiple_of(c0 + LANE, LANE)
            for f in range(nf):
                v, tf = tend[f]
                ext2[f, pl.ds(r, SUB), pl.ds(c, LANE)] = v + tf
        return carry

    lax.fori_loop(0, n_i * n_jp, stage_one, 0)

    high_ghost(ext2, lambda f: jnp.zeros((1, lanes), jnp.float32))

    def stage_two(i, carry):
        for jp in range(n_jp):
            r0, c0s = tile_offsets(i * n_jp + jp)
            rate_ts = [rate_ref[pl.ds(r0, SUB), pl.ds(c0, LANE)] for c0 in c0s]
            tends = tendency_tiles(ext2, r0, c0s, rate_ts)
            r = pl.multiple_of(r0 + SUB, SUB)
            for c0, tend in zip(c0s, tends):
                c = pl.multiple_of(c0 + LANE, LANE)
                for f in range(nf):
                    v, tf = tend[f]
                    base = ext1[f, pl.ds(r, SUB), pl.ds(c, LANE)]
                    obuf[f, pl.ds(r0, SUB), pl.ds(c0, LANE)] = 0.5 * (base + v + tf)
        r0 = pl.multiple_of(i * SUB, SUB)
        pltpu.make_async_copy(
            obuf.at[:, pl.ds(r0, SUB), :], out_hbm.at[:, pl.ds(r0, SUB), :], sem.at[1]
        ).start()
        return carry

    lax.fori_loop(0, n_i, stage_two, 0)

    for f in range(nf):
        elo_ref[f:f + 1, :] = ext2[f, SUB:SUB + 1, LANE:right]
        ehi_ref[f:f + 1, :] = ext2[f, top - 1:top, LANE:right]
        west = jnp.transpose(ext2[f, SUB:top, LANE:2 * LANE])
        east = jnp.transpose(ext2[f, SUB:top, right - LANE:right])
        clo_ref[f:f + 1, :] = west[0:1, :]
        chi_ref[f:f + 1, :] = east[LANE - 1:LANE, :]
    pltpu.make_async_copy(obuf, out_hbm, sem.at[1]).wait()


def fused_step(fields, rate, mix, act, flags, halo_lo, halo_hi, swapped, lft, rgt):
    nf, rows, lanes = fields.shape
    vmem = pltpu.VMEM
    smem = pl.BlockSpec(memory_space=pltpu.SMEM)
    vspec = pl.BlockSpec(memory_space=vmem)
    cells = rows * lanes
    cost = pl.CostEstimate(
        flops=2 * cells * nf * (2 * nf + 24),
        transcendentals=2 * cells * (nf + 3),
        bytes_accessed=4 * cells * (2 * nf + 1),
    )
    return pl.pallas_call(
        functools.partial(step_kernel, nf, rows, lanes),
        out_shape=(
            jax.ShapeDtypeStruct((nf, rows, lanes), jnp.float32),
            jax.ShapeDtypeStruct((nf, lanes), jnp.float32),
            jax.ShapeDtypeStruct((nf, lanes), jnp.float32),
            jax.ShapeDtypeStruct((nf, rows), jnp.float32),
            jax.ShapeDtypeStruct((nf, rows), jnp.float32),
        ),
        in_specs=[smem, smem, smem, pl.BlockSpec(memory_space=pl.ANY)] + [vspec] * 6,
        out_specs=(pl.BlockSpec(memory_space=pl.ANY),) + (vspec,) * 4,
        scratch_shapes=[
            vmem((nf, rows + 2 * SUB, lanes + 2 * LANE), jnp.float32),
            vmem((nf, rows + 2 * SUB, lanes + 2 * LANE), jnp.float32),
            vmem((nf * nf + nf, SUB, LANE), jnp.float32),
            vmem((nf, rows, lanes), jnp.float32),
            pltpu.SemaphoreType.DMA((2,)),
        ],
        compiler_params=pltpu.CompilerParams(vmem_limit_bytes=60 * 1024 * 1024),
        cost_estimate=cost,
    )(mix, act, flags, fields, rate, halo_lo, halo_hi, swapped, lft, rgt)


def interp_kernel(ks, width, flag_s, ids_s, wt_ref, table_ref, *refs):
    n_pass = (len(refs) - 3) // 2
    ins, o_ref, outs, acc, picked = refs[:n_pass], refs[n_pass], refs[n_pass + 1:-2], refs[-2], refs[-1]
    lanes = o_ref.shape[1]
    per_row = LANE // width
    acc[...] = jnp.zeros(acc.shape, jnp.float32)

    @pl.when(flag_s[0] + flag_s[1] > 0.5)
    def _():
        def group(pg, carry):
            p0 = pl.multiple_of(pg * SUB, SUB)
            for s in range(SUB):
                for k in range(ks):
                    q = ids_s[k, p0 + s]
                    packed = table_ref[pl.ds(q // per_row, 1), :]
                    shift = (LANE - (q % per_row) * width) % LANE
                    picked[k, pl.ds(p0 + s, 1), :] = pltpu.roll(packed, shift, 1)
            return carry

        lax.fori_loop(0, lanes // SUB, group, 0)
        total = wt_ref[:, 0:1] * picked[0]
        for k in range(1, ks):
            total = total + wt_ref[:, k:k + 1] * picked[k]
        acc[...] = total

    o_ref[...] = jnp.transpose(acc[...])[0:o_ref.shape[0], :]
    for src, dst in zip(ins, outs):
        dst[...] = src[...]


def interpolate(flags, ids, wt, table, width, passed):
    ks, lanes = ids.shape
    smem = pl.BlockSpec(memory_space=pltpu.SMEM)
    vspec = pl.BlockSpec(memory_space=pltpu.VMEM)
    return pl.pallas_call(
        functools.partial(interp_kernel, ks, width),
        out_shape=(jax.ShapeDtypeStruct((width - 1, lanes), jnp.float32),)
        + tuple(jax.ShapeDtypeStruct(x.shape, x.dtype) for x in passed),
        in_specs=[smem, smem] + [vspec] * (2 + len(passed)),
        out_specs=(vspec,) * (1 + len(passed)),
        scratch_shapes=[
            pltpu.VMEM((lanes, LANE), jnp.float32),
            pltpu.VMEM((ks, lanes, LANE), jnp.float32),
        ],
    )(flags, ids, wt, table, *passed)


def fix_kernel(low_w, side_w, out_in, g0_ref, g1_ref, gl_ref, gr_ref, out_ref, rb, cb, sem):
    nf, rows, lanes = out_ref.shape
    mid = rows - 2 * SUB
    wins = [
        (out_ref.at[:, pl.ds(0, SUB), :], rb.at[0]),
        (out_ref.at[:, pl.ds(rows - SUB, SUB), :], rb.at[1]),
        (out_ref.at[:, pl.ds(SUB, mid), pl.ds(0, LANE)], cb.at[0]),
        (out_ref.at[:, pl.ds(SUB, mid), pl.ds(lanes - LANE, LANE)], cb.at[1]),
    ]
    loads = [pltpu.make_async_copy(hbm, buf, sem.at[s]) for s, (hbm, buf) in enumerate(wins)]
    for c in loads:
        c.start()
    for c in loads:
        c.wait()
    lane_id = lax.broadcasted_iota(jnp.int32, (rows, LANE), 1)
    row_lane = lax.broadcasted_iota(jnp.int32, (SUB, LANE), 1)
    for f in range(nf):
        west = jnp.where(lane_id == 0, side_w * tile_t(gl_ref[f:f + 1, :]), 0.0)
        east = jnp.where(lane_id == LANE - 1, side_w * tile_t(gr_ref[f:f + 1, :]), 0.0)
        cb[0, f] = cb[0, f] + west[SUB:rows - SUB]
        cb[1, f] = cb[1, f] + east[SUB:rows - SUB]
        for s, lo in ((0, 0), (1, rows - SUB)):
            rb[s, f, :, 0:LANE] = rb[s, f, :, 0:LANE] + west[lo:lo + SUB]
            rb[s, f, :, lanes - LANE:lanes] = rb[s, f, :, lanes - LANE:lanes] + east[lo:lo + SUB]
        rb[0, f, 0:1, :] = rb[0, f, 0:1, :] + low_w * g0_ref[f:f + 1, :]
        rb[1, f, SUB - 1:SUB, :] = rb[1, f, SUB - 1:SUB, :] + side_w * g1_ref[f:f + 1, :]
    stores = [pltpu.make_async_copy(buf, hbm, sem.at[s]) for s, (hbm, buf) in enumerate(wins)]
    for c in stores:
        c.start()
    for c in stores:
        c.wait()


def fix_edges(out, g0, g1, gl, gr, low_w, side_w):
    nf, rows, lanes = out.shape
    vspec = pl.BlockSpec(memory_space=pltpu.VMEM)
    anyspec = pl.BlockSpec(memory_space=pl.ANY)
    return pl.pallas_call(
        functools.partial(fix_kernel, low_w, side_w),
        out_shape=jax.ShapeDtypeStruct(out.shape, jnp.float32),
        in_specs=[anyspec, vspec, vspec, vspec, vspec],
        out_specs=anyspec,
        scratch_shapes=[
            pltpu.VMEM((2, nf, SUB, lanes), jnp.float32),
            pltpu.VMEM((2, nf, rows - 2 * SUB, LANE), jnp.float32),
            pltpu.SemaphoreType.DMA((4,)),
        ],
        input_output_aliases={0: 0},
    )(out, g0, g1, gl, gr)


def shards(
    fields, react_rate, mix_matrix, activation, inlet_ids, inlet_weights, outlet_ids, outlet_weights
):
    nf, rows, lanes = fields.shape
    n_grp = lax.axis_size("grp")
    n_blk = lax.axis_size("blk")
    g = lax.axis_index("grp")
    b = lax.axis_index("blk")
    exit_grp = n_grp - 2
    turb_grp = n_grp - 1
    flags = jnp.stack([g == exit_grp, g == turb_grp]).astype(jnp.float32)

    last_row = fields[:, -1, :]
    first_row = fields[:, 0, :]
    payload = jnp.concatenate([last_row, first_row[4:5]], axis=0)
    planes = payload[None]
    spans = []
    span = n_blk // 2
    while span >= 1:
        spans.append(span)
        partner = [(i, i ^ span) for i in range(n_blk)]
        planes = jnp.concatenate([planes, lax.ppermute(planes, "blk", partner)], axis=0)
        span //= 2
    width = 16
    table = jnp.pad(jnp.transpose(planes, (0, 2, 1)), ((0, 0), (0, 0), (0, width - nf - 1)))
    table = table.reshape(n_blk * lanes * width // LANE, LANE)
    at_exit = g == exit_grp
    ids = jnp.where(at_exit, inlet_ids, outlet_ids)
    m = jnp.bitwise_xor(ids // lanes, b)
    slot = jnp.zeros_like(m)
    for r, span in enumerate(spans):
        slot = slot + ((m // span) % 2) * (1 << r)
    ids = slot * lanes + ids % lanes
    wt = jnp.transpose(jnp.where(at_exit, inlet_weights, outlet_weights))
    halo_lo = lax.ppermute(last_row, "grp", [(i, i + 1) for i in range(n_grp - 2)])
    halo_hi = lax.ppermute(first_row, "grp", [(i + 1, i) for i in range(n_grp - 2)])
    lft = lax.ppermute(fields[:, :, lanes - 1], "blk", [(i, (i + 1) % n_blk) for i in range(n_blk)])
    rgt = lax.ppermute(fields[:, :, 0], "blk", [((i + 1) % n_blk, i) for i in range(n_blk)])

    swap, halo_lo, halo_hi, lft, rgt = interpolate(
        flags, ids, wt, table, width, (halo_lo, halo_hi, lft, rgt)
    )
    swapped = lax.ppermute(swap, "grp", [(exit_grp, turb_grp), (turb_grp, exit_grp)])

    out, elo, ehi, clo, chi = fused_step(
        fields, react_rate, mix_matrix, activation, flags, halo_lo, halo_hi, swapped, lft, rgt
    )

    g0 = lax.ppermute(ehi, "grp", [(i, i + 1) for i in range(n_grp - 2)])
    g1 = lax.ppermute(elo, "grp", [(i + 1, i) for i in range(n_grp - 2)])
    gl = lax.ppermute(chi, "blk", [(i, (i + 1) % n_blk) for i in range(n_blk)])
    gr = lax.ppermute(clo, "blk", [((i + 1) % n_blk, i) for i in range(n_blk)])
    low_w = 0.5 * (courant + diffusion)
    side_w = 0.5 * diffusion
    return fix_edges(out, g0, g1, gl, gr, low_w, side_w)


def solution(mesh):
    in_specs = (
        P(None, "grp", "blk"),
        P("grp", "blk"),
        P(),
        P(),
        P(None, "blk"),
        P(None, "blk"),
        P(None, "blk"),
        P(None, "blk"),
    )
    out_specs = P(None, "grp", "blk")
    return jax.shard_map(shards, mesh=mesh, in_specs=in_specs, out_specs=out_specs, check_vma=False)
```

```python
import functools

import jax
import jax.numpy as jnp
from jax import lax
from jax.experimental import pallas as pl
from jax.experimental.pallas import tpu as pltpu
from jax.sharding import PartitionSpec as P

courant = 0.5
diffusion = 0.1
source_step = 0.5

SUB = 8
LANE = 128


def tile_t(row):
    n = row.shape[1]
    return jnp.transpose(jnp.broadcast_to(row, (n, n)))


def step_kernel(nf, rows, lanes, mix_s, act_s, flag_s, f_hbm, rate_ref, hlo_ref, hhi_ref, sw_ref,
                lft_ref, rgt_ref, out_hbm, elo_ref, ehi_ref, clo_ref, chi_ref, ext1, ext2, coef, obuf,
                sem):
    n_i = rows // SUB
    n_j = lanes // LANE
    top = SUB + rows
    right = LANE + lanes
    at_exit = flag_s[0] > 0.5
    at_turb = flag_s[1] > 0.5
    at_end = flag_s[0] + flag_s[1] > 0.5

    copy = pltpu.make_async_copy(f_hbm, ext1.at[:, SUB:top, LANE:right], sem.at[0])
    copy.start()
    zeros = jnp.zeros((rows, LANE), jnp.float32)
    for f in range(nf):
        inlet = sw_ref[f:f + 1, :]
        ext1[f, SUB - 1:SUB, LANE:right] = jnp.where(at_turb, inlet, hlo_ref[f:f + 1, :])
        ext2[f, SUB - 1:SUB, LANE:right] = jnp.where(at_turb, inlet, 0.0)
        ext1[f, SUB:top, 0:LANE] = tile_t(lft_ref[f:f + 1, :])
        ext1[f, SUB:top, right:right + LANE] = tile_t(rgt_ref[f:f + 1, :])
        ext2[f, SUB:top, 0:LANE] = zeros
        ext2[f, SUB:top, right:right + LANE] = zeros
    for f in range(nf):
        for g in range(nf):
            coef[f * nf + g] = jnp.full((SUB, LANE), source_step * mix_s[f, g], jnp.float32)
        coef[nf * nf + f] = jnp.full((SUB, LANE), -act_s[f], jnp.float32)
    copy.wait()

    def high_ghost(ext, halo_of):
        for f in range(nf):
            own = ext[f, top - 1:top, LANE:right]
            halo = halo_of(f)
            if f == 4:
                row = jnp.where(at_turb, own, jnp.where(at_exit, sw_ref[nf:nf + 1, :], halo))
            else:
                row = jnp.where(at_end, own, halo)
            ext[f, top:top + 1, LANE:right] = row

    high_ghost(ext1, lambda f: hhi_ref[f:f + 1, :])

    sub_id = lax.broadcasted_iota(jnp.int32, (SUB, LANE), 0)
    lane_id = lax.broadcasted_iota(jnp.int32, (SUB, LANE), 1)
    first_sub = sub_id == 0
    last_sub = sub_id == SUB - 1
    first_lane = lane_id == 0
    last_lane = lane_id == LANE - 1

    def tendency_tiles(src, r0, c0s, rate_ts):
        r = pl.multiple_of(r0 + SUB, SUB)
        r_up = pl.multiple_of(r0, SUB)
        r_dn = pl.multiple_of(r0 + 2 * SUB, SUB)
        cs = [pl.multiple_of(c0 + LANE, LANE) for c0 in c0s]
        reacts = []
        for c, rate_t in zip(cs, rate_ts):
            v4 = src[4, pl.ds(r, SUB), pl.ds(c, LANE)]
            heat = 1.0 + (jnp.maximum(v4, 0.0) + jnp.log1p(jnp.exp(-jnp.abs(v4))))
            inv_heat = 1.0 / heat
            reacts.append([
                rate_t * src[f, pl.ds(r, SUB), pl.ds(c, LANE)] * jnp.exp(coef[nf * nf + f] * inv_heat)
                for f in range(nf)
            ])
        tends = [[] for _ in cs]
        for f in range(nf):
            accs = [None] * len(cs)
            for g in range(nf):
                m = coef[f * nf + g]
                for h in range(len(cs)):
                    term = m * reacts[h][g]
                    accs[h] = term if accs[h] is None else accs[h] + term
            for h, c in enumerate(cs):
                c_w = pl.multiple_of(c - LANE, LANE)
                c_e = pl.multiple_of(c + LANE, LANE)
                v = src[f, pl.ds(r, SUB), pl.ds(c, LANE)]
                up = src[f, pl.ds(r_up, SUB), pl.ds(c, LANE)]
                down = src[f, pl.ds(r_dn, SUB), pl.ds(c, LANE)]
                west = src[f, pl.ds(r, SUB), pl.ds(c_w, LANE)]
                east = src[f, pl.ds(r, SUB), pl.ds(c_e, LANE)]
                backward = jnp.where(first_sub, pltpu.roll(up, 1, 0), pltpu.roll(v, 1, 0))
                forward = jnp.where(last_sub, pltpu.roll(down, SUB - 1, 0), pltpu.roll(v, SUB - 1, 0))
                left = jnp.where(first_lane, pltpu.roll(west, 1, 1), pltpu.roll(v, 1, 1))
                rgt = jnp.where(last_lane, pltpu.roll(east, LANE - 1, 1), pltpu.roll(v, LANE - 1, 1))
                flow = (courant + diffusion) * backward + diffusion * (forward + left + rgt)
                flow = flow - (courant + 4.0 * diffusion) * v
                tends[h].append((v, flow + accs[h]))
        return tends

    pair = 2 if n_j % 2 == 0 else 1
    n_jp = n_j // pair

    def tile_offsets(t):
        i = t // n_jp
        jp = t % n_jp
        r0 = pl.multiple_of(i * SUB, SUB)
        c0s = [pl.multiple_of((jp * pair + h) * LANE, LANE) for h in range(pair)]
        return r0, c0s

    def stage_one(t, carry):
        r0, c0s = tile_offsets(t)
        rate_ts = [rate_ref[pl.ds(r0, SUB), pl.ds(c0, LANE)] for c0 in c0s]
        tends = tendency_tiles(ext1, r0, c0s, rate_ts)
        r = pl.multiple_of(r0 + SUB, SUB)
        for c0, tend in zip(c0s, tends):
            c = pl.multiple_of(c0 + LANE, LANE)
            for f in range(nf):
                v, tf = tend[f]
                ext2[f, pl.ds(r, SUB), pl.ds(c, LANE)] = v + tf
        return carry

    lax.fori_loop(0, n_i * n_jp, stage_one, 0)

    high_ghost(ext2, lambda f: jnp.zeros((1, lanes), jnp.float32))

    def stage_two(i, carry):
        for jp in range(n_jp):
            r0, c0s = tile_offsets(i * n_jp + jp)
            rate_ts = [rate_ref[pl.ds(r0, SUB), pl.ds(c0, LANE)] for c0 in c0s]
            tends = tendency_tiles(ext2, r0, c0s, rate_ts)
            r = pl.multiple_of(r0 + SUB, SUB)
            for c0, tend in zip(c0s, tends):
                c = pl.multiple_of(c0 + LANE, LANE)
                for f in range(nf):
                    v, tf = tend[f]
                    base = ext1[f, pl.ds(r, SUB), pl.ds(c, LANE)]
                    obuf[f, pl.ds(r0, SUB), pl.ds(c0, LANE)] = 0.5 * (base + v + tf)
        r0 = pl.multiple_of(i * SUB, SUB)
        pltpu.make_async_copy(
            obuf.at[:, pl.ds(r0, SUB), :], out_hbm.at[:, pl.ds(r0, SUB), :], sem.at[1]
        ).start()
        return carry

    lax.fori_loop(0, n_i, stage_two, 0)

    for f in range(nf):
        elo_ref[f:f + 1, :] = ext2[f, SUB:SUB + 1, LANE:right]
        ehi_ref[f:f + 1, :] = ext2[f, top - 1:top, LANE:right]
        west = jnp.transpose(ext2[f, SUB:top, LANE:2 * LANE])
        east = jnp.transpose(ext2[f, SUB:top, right - LANE:right])
        clo_ref[f:f + 1, :] = west[0:1, :]
        chi_ref[f:f + 1, :] = east[LANE - 1:LANE, :]
    pltpu.make_async_copy(obuf, out_hbm, sem.at[1]).wait()


def fused_step(fields, rate, mix, act, flags, halo_lo, halo_hi, swapped, lft, rgt):
    nf, rows, lanes = fields.shape
    vmem = pltpu.VMEM
    smem = pl.BlockSpec(memory_space=pltpu.SMEM)
    vspec = pl.BlockSpec(memory_space=vmem)
    cells = rows * lanes
    cost = pl.CostEstimate(
        flops=2 * cells * nf * (2 * nf + 24),
        transcendentals=2 * cells * (nf + 3),
        bytes_accessed=4 * cells * (2 * nf + 1),
    )
    return pl.pallas_call(
        functools.partial(step_kernel, nf, rows, lanes),
        out_shape=(
            jax.ShapeDtypeStruct((nf, rows, lanes), jnp.float32),
            jax.ShapeDtypeStruct((nf, lanes), jnp.float32),
            jax.ShapeDtypeStruct((nf, lanes), jnp.float32),
            jax.ShapeDtypeStruct((nf, rows), jnp.float32),
            jax.ShapeDtypeStruct((nf, rows), jnp.float32),
        ),
        in_specs=[smem, smem, smem, pl.BlockSpec(memory_space=pl.ANY)] + [vspec] * 6,
        out_specs=(pl.BlockSpec(memory_space=pl.ANY),) + (vspec,) * 4,
        scratch_shapes=[
            vmem((nf, rows + 2 * SUB, lanes + 2 * LANE), jnp.float32),
            vmem((nf, rows + 2 * SUB, lanes + 2 * LANE), jnp.float32),
            vmem((nf * nf + nf, SUB, LANE), jnp.float32),
            vmem((nf, rows, lanes), jnp.float32),
            pltpu.SemaphoreType.DMA((2,)),
        ],
        compiler_params=pltpu.CompilerParams(vmem_limit_bytes=60 * 1024 * 1024),
        cost_estimate=cost,
    )(mix, act, flags, fields, rate, halo_lo, halo_hi, swapped, lft, rgt)


def interp_kernel(ks, flag_s, ids_s, wt_ref, table_ref, *refs):
    n_pass = (len(refs) - 3) // 2
    ins, o_ref, outs, acc, picked = refs[:n_pass], refs[n_pass], refs[n_pass + 1:-2], refs[-2], refs[-1]
    lanes = o_ref.shape[1]
    width = table_ref.shape[1]
    acc[...] = jnp.zeros(acc.shape, jnp.float32)

    @pl.when(flag_s[0] + flag_s[1] > 0.5)
    def _():
        def group(pg, carry):
            p0 = pl.multiple_of(pg * SUB, SUB)
            for s in range(SUB):
                for k in range(ks):
                    q = ids_s[k, p0 + s]
                    picked[k, pl.ds(p0 + s, 1), :] = table_ref[pl.ds(q, 1), :]
            return carry

        lax.fori_loop(0, lanes // SUB, group, 0)
        total = wt_ref[:, 0:1] * picked[0]
        for k in range(1, ks):
            total = total + wt_ref[:, k:k + 1] * picked[k]
        acc[:, 0:width] = total

    o_ref[...] = jnp.transpose(acc[...])[0:o_ref.shape[0], :]
    for src, dst in zip(ins, outs):
        dst[...] = src[...]


def interpolate(flags, ids, wt, table, passed):
    ks, lanes = ids.shape
    smem = pl.BlockSpec(memory_space=pltpu.SMEM)
    vspec = pl.BlockSpec(memory_space=pltpu.VMEM)
    width = table.shape[1]
    return pl.pallas_call(
        functools.partial(interp_kernel, ks),
        out_shape=(jax.ShapeDtypeStruct((width, lanes), jnp.float32),)
        + tuple(jax.ShapeDtypeStruct(x.shape, x.dtype) for x in passed),
        in_specs=[smem, smem] + [vspec] * (2 + len(passed)),
        out_specs=(vspec,) * (1 + len(passed)),
        scratch_shapes=[
            pltpu.VMEM((lanes, LANE), jnp.float32),
            pltpu.VMEM((ks, lanes, width), jnp.float32),
        ],
    )(flags, ids, wt, table, *passed)


def fix_kernel(low_w, side_w, out_in, g0_ref, g1_ref, gl_ref, gr_ref, out_ref, rb, cb, sem):
    nf, rows, lanes = out_ref.shape
    mid = rows - 2 * SUB
    wins = [
        (out_ref.at[:, pl.ds(0, SUB), :], rb.at[0]),
        (out_ref.at[:, pl.ds(rows - SUB, SUB), :], rb.at[1]),
        (out_ref.at[:, pl.ds(SUB, mid), pl.ds(0, LANE)], cb.at[0]),
        (out_ref.at[:, pl.ds(SUB, mid), pl.ds(lanes - LANE, LANE)], cb.at[1]),
    ]
    loads = [pltpu.make_async_copy(hbm, buf, sem.at[s]) for s, (hbm, buf) in enumerate(wins)]
    for c in loads:
        c.start()
    for c in loads:
        c.wait()
    lane_id = lax.broadcasted_iota(jnp.int32, (rows, LANE), 1)
    row_lane = lax.broadcasted_iota(jnp.int32, (SUB, LANE), 1)
    for f in range(nf):
        west = jnp.where(lane_id == 0, side_w * tile_t(gl_ref[f:f + 1, :]), 0.0)
        east = jnp.where(lane_id == LANE - 1, side_w * tile_t(gr_ref[f:f + 1, :]), 0.0)
        cb[0, f] = cb[0, f] + west[SUB:rows - SUB]
        cb[1, f] = cb[1, f] + east[SUB:rows - SUB]
        for s, lo in ((0, 0), (1, rows - SUB)):
            rb[s, f, :, 0:LANE] = rb[s, f, :, 0:LANE] + west[lo:lo + SUB]
            rb[s, f, :, lanes - LANE:lanes] = rb[s, f, :, lanes - LANE:lanes] + east[lo:lo + SUB]
        rb[0, f, 0:1, :] = rb[0, f, 0:1, :] + low_w * g0_ref[f:f + 1, :]
        rb[1, f, SUB - 1:SUB, :] = rb[1, f, SUB - 1:SUB, :] + side_w * g1_ref[f:f + 1, :]
    stores = [pltpu.make_async_copy(buf, hbm, sem.at[s]) for s, (hbm, buf) in enumerate(wins)]
    for c in stores:
        c.start()
    for c in stores:
        c.wait()


def fix_edges(out, g0, g1, gl, gr, low_w, side_w):
    nf, rows, lanes = out.shape
    vspec = pl.BlockSpec(memory_space=pltpu.VMEM)
    anyspec = pl.BlockSpec(memory_space=pl.ANY)
    return pl.pallas_call(
        functools.partial(fix_kernel, low_w, side_w),
        out_shape=jax.ShapeDtypeStruct(out.shape, jnp.float32),
        in_specs=[anyspec, vspec, vspec, vspec, vspec],
        out_specs=anyspec,
        scratch_shapes=[
            pltpu.VMEM((2, nf, SUB, lanes), jnp.float32),
            pltpu.VMEM((2, nf, rows - 2 * SUB, LANE), jnp.float32),
            pltpu.SemaphoreType.DMA((4,)),
        ],
        input_output_aliases={0: 0},
    )(out, g0, g1, gl, gr)


def shards(
    fields, react_rate, mix_matrix, activation, inlet_ids, inlet_weights, outlet_ids, outlet_weights
):
    nf, rows, lanes = fields.shape
    n_grp = lax.axis_size("grp")
    n_blk = lax.axis_size("blk")
    g = lax.axis_index("grp")
    b = lax.axis_index("blk")
    exit_grp = n_grp - 2
    turb_grp = n_grp - 1
    flags = jnp.stack([g == exit_grp, g == turb_grp]).astype(jnp.float32)

    last_row = fields[:, -1, :]
    first_row = fields[:, 0, :]
    payload = jnp.concatenate([last_row, first_row[4:5]], axis=0)
    planes = payload[None]
    spans = []
    span = n_blk // 2
    edges = (last_row, first_row, fields[:, :, lanes - 1], fields[:, :, 0])
    while span >= 1:
        spans.append(span)
        if span == 1:
            edges, planes = lax.optimization_barrier((edges, planes))
        partner = [(i, i ^ span) for i in range(n_blk)]
        planes = jnp.concatenate([planes, lax.ppermute(planes, "blk", partner)], axis=0)
        span //= 2
    table = jnp.transpose(planes, (0, 2, 1)).reshape(n_blk * lanes, nf + 1)
    at_exit = g == exit_grp
    ids = jnp.where(at_exit, inlet_ids, outlet_ids)
    m = jnp.bitwise_xor(ids // lanes, b)
    slot = jnp.zeros_like(m)
    for r, span in enumerate(spans):
        slot = slot + ((m // span) % 2) * (1 << r)
    ids = slot * lanes + ids % lanes
    wt = jnp.transpose(jnp.where(at_exit, inlet_weights, outlet_weights))
    halo_lo = lax.ppermute(edges[0], "grp", [(i, i + 1) for i in range(n_grp - 2)])
    halo_hi = lax.ppermute(edges[1], "grp", [(i + 1, i) for i in range(n_grp - 2)])
    lft = lax.ppermute(edges[2], "blk", [(i, (i + 1) % n_blk) for i in range(n_blk)])
    rgt = lax.ppermute(edges[3], "blk", [((i + 1) % n_blk, i) for i in range(n_blk)])

    swap, halo_lo, halo_hi, lft, rgt = interpolate(flags, ids, wt, table, (halo_lo, halo_hi, lft, rgt))
    swapped = lax.ppermute(swap, "grp", [(exit_grp, turb_grp), (turb_grp, exit_grp)])

    out, elo, ehi, clo, chi = fused_step(
        fields, react_rate, mix_matrix, activation, flags, halo_lo, halo_hi, swapped, lft, rgt
    )

    g0 = lax.ppermute(ehi, "grp", [(i, i + 1) for i in range(n_grp - 2)])
    g1 = lax.ppermute(elo, "grp", [(i + 1, i) for i in range(n_grp - 2)])
    gl = lax.ppermute(chi, "blk", [(i, (i + 1) % n_blk) for i in range(n_blk)])
    gr = lax.ppermute(clo, "blk", [((i + 1) % n_blk, i) for i in range(n_blk)])
    low_w = 0.5 * (courant + diffusion)
    side_w = 0.5 * diffusion
    return fix_edges(out, g0, g1, gl, gr, low_w, side_w)


def solution(mesh):
    in_specs = (
        P(None, "grp", "blk"),
        P("grp", "blk"),
        P(),
        P(),
        P(None, "blk"),
        P(None, "blk"),
        P(None, "blk"),
        P(None, "blk"),
    )
    out_specs = P(None, "grp", "blk")
    return jax.shard_map(shards, mesh=mesh, in_specs=in_specs, out_specs=out_specs, check_vma=False)
```

```python
import functools

import jax
import jax.numpy as jnp
from jax import lax
from jax.experimental import pallas as pl
from jax.experimental.pallas import tpu as pltpu
from jax.sharding import PartitionSpec as P

courant = 0.5
diffusion = 0.1
source_step = 0.5

SUB = 8
LANE = 128


def tile_t(row):
    n = row.shape[1]
    return jnp.transpose(jnp.broadcast_to(row, (n, n)))


def step_kernel(nf, rows, lanes, mix_s, act_s, flag_s, f_hbm, rate_ref, hlo_ref, hhi_ref,
                lft_ref, rgt_ref, out_hbm, elo_ref, ehi_ref, clo_ref, chi_ref, ext1, ext2, coef, obuf,
                sem):
    n_i = rows // SUB
    n_j = lanes // LANE
    top = SUB + rows
    right = LANE + lanes
    at_exit = flag_s[0] > 0.5
    at_turb = flag_s[1] > 0.5
    at_end = flag_s[0] + flag_s[1] > 0.5

    copy = pltpu.make_async_copy(f_hbm, ext1.at[:, SUB:top, LANE:right], sem.at[0])
    copy.start()
    zeros = jnp.zeros((rows, LANE), jnp.float32)
    for f in range(nf):
        low = hlo_ref[f:f + 1, :]
        ext1[f, SUB - 1:SUB, LANE:right] = low
        ext2[f, SUB - 1:SUB, LANE:right] = jnp.where(at_turb, low, 0.0)
        ext1[f, SUB:top, 0:LANE] = tile_t(lft_ref[f:f + 1, :])
        ext1[f, SUB:top, right:right + LANE] = tile_t(rgt_ref[f:f + 1, :])
        ext2[f, SUB:top, 0:LANE] = zeros
        ext2[f, SUB:top, right:right + LANE] = zeros
    for f in range(nf):
        for g in range(nf):
            coef[f * nf + g] = jnp.full((SUB, LANE), source_step * mix_s[f, g], jnp.float32)
        coef[nf * nf + f] = jnp.full((SUB, LANE), -act_s[f], jnp.float32)
    copy.wait()

    def high_ghost(ext, outside):
        for f in range(nf):
            own = ext[f, top - 1:top, LANE:right]
            halo = hhi_ref[f:f + 1, :]
            if f == 4:
                row = jnp.where(at_turb, own, jnp.where(at_exit | outside, halo, 0.0))
            else:
                row = jnp.where(at_end, own, jnp.where(outside, halo, 0.0))
            ext[f, top:top + 1, LANE:right] = row

    high_ghost(ext1, True)

    sub_id = lax.broadcasted_iota(jnp.int32, (SUB, LANE), 0)
    lane_id = lax.broadcasted_iota(jnp.int32, (SUB, LANE), 1)
    first_sub = sub_id == 0
    last_sub = sub_id == SUB - 1
    first_lane = lane_id == 0
    last_lane = lane_id == LANE - 1

    def tendency_tiles(src, r0, c0s, rate_ts):
        r = pl.multiple_of(r0 + SUB, SUB)
        r_up = pl.multiple_of(r0, SUB)
        r_dn = pl.multiple_of(r0 + 2 * SUB, SUB)
        cs = [pl.multiple_of(c0 + LANE, LANE) for c0 in c0s]
        reacts = []
        for c, rate_t in zip(cs, rate_ts):
            v4 = src[4, pl.ds(r, SUB), pl.ds(c, LANE)]
            heat = 1.0 + (jnp.maximum(v4, 0.0) + jnp.log1p(jnp.exp(-jnp.abs(v4))))
            inv_heat = 1.0 / heat
            reacts.append([
                rate_t * src[f, pl.ds(r, SUB), pl.ds(c, LANE)] * jnp.exp(coef[nf * nf + f] * inv_heat)
                for f in range(nf)
            ])
        tends = [[] for _ in cs]
        for f in range(nf):
            accs = [None] * len(cs)
            for g in range(nf):
                m = coef[f * nf + g]
                for h in range(len(cs)):
                    term = m * reacts[h][g]
                    accs[h] = term if accs[h] is None else accs[h] + term
            for h, c in enumerate(cs):
                c_w = pl.multiple_of(c - LANE, LANE)
                c_e = pl.multiple_of(c + LANE, LANE)
                v = src[f, pl.ds(r, SUB), pl.ds(c, LANE)]
                up = src[f, pl.ds(r_up, SUB), pl.ds(c, LANE)]
                down = src[f, pl.ds(r_dn, SUB), pl.ds(c, LANE)]
                west = src[f, pl.ds(r, SUB), pl.ds(c_w, LANE)]
                east = src[f, pl.ds(r, SUB), pl.ds(c_e, LANE)]
                backward = jnp.where(first_sub, pltpu.roll(up, 1, 0), pltpu.roll(v, 1, 0))
                forward = jnp.where(last_sub, pltpu.roll(down, SUB - 1, 0), pltpu.roll(v, SUB - 1, 0))
                left = jnp.where(first_lane, pltpu.roll(west, 1, 1), pltpu.roll(v, 1, 1))
                rgt = jnp.where(last_lane, pltpu.roll(east, LANE - 1, 1), pltpu.roll(v, LANE - 1, 1))
                flow = (courant + diffusion) * backward + diffusion * (forward + left + rgt)
                flow = flow - (courant + 4.0 * diffusion) * v
                tends[h].append((v, flow + accs[h]))
        return tends

    pair = 2 if n_j % 2 == 0 else 1
    n_jp = n_j // pair

    def tile_offsets(t):
        i = t // n_jp
        jp = t % n_jp
        r0 = pl.multiple_of(i * SUB, SUB)
        c0s = [pl.multiple_of((jp * pair + h) * LANE, LANE) for h in range(pair)]
        return r0, c0s

    def stage_one(t, carry):
        r0, c0s = tile_offsets(t)
        rate_ts = [rate_ref[pl.ds(r0, SUB), pl.ds(c0, LANE)] for c0 in c0s]
        tends = tendency_tiles(ext1, r0, c0s, rate_ts)
        r = pl.multiple_of(r0 + SUB, SUB)
        for c0, tend in zip(c0s, tends):
            c = pl.multiple_of(c0 + LANE, LANE)
            for f in range(nf):
                v, tf = tend[f]
                ext2[f, pl.ds(r, SUB), pl.ds(c, LANE)] = v + tf
        return carry

    lax.fori_loop(0, n_i * n_jp, stage_one, 0)

    high_ghost(ext2, False)

    def stage_two(i, carry):
        for jp in range(n_jp):
            r0, c0s = tile_offsets(i * n_jp + jp)
            rate_ts = [rate_ref[pl.ds(r0, SUB), pl.ds(c0, LANE)] for c0 in c0s]
            tends = tendency_tiles(ext2, r0, c0s, rate_ts)
            r = pl.multiple_of(r0 + SUB, SUB)
            for c0, tend in zip(c0s, tends):
                c = pl.multiple_of(c0 + LANE, LANE)
                for f in range(nf):
                    v, tf = tend[f]
                    base = ext1[f, pl.ds(r, SUB), pl.ds(c, LANE)]
                    obuf[f, pl.ds(r0, SUB), pl.ds(c0, LANE)] = 0.5 * (base + v + tf)
        r0 = pl.multiple_of(i * SUB, SUB)
        pltpu.make_async_copy(
            obuf.at[:, pl.ds(r0, SUB), :], out_hbm.at[:, pl.ds(r0, SUB), :], sem.at[1]
        ).start()
        return carry

    lax.fori_loop(0, n_i, stage_two, 0)

    for f in range(nf):
        elo_ref[f:f + 1, :] = ext2[f, SUB:SUB + 1, LANE:right]
        ehi_ref[f:f + 1, :] = ext2[f, top - 1:top, LANE:right]
        west = jnp.transpose(ext2[f, SUB:top, LANE:2 * LANE])
        east = jnp.transpose(ext2[f, SUB:top, right - LANE:right])
        clo_ref[f:f + 1, :] = west[0:1, :]
        chi_ref[f:f + 1, :] = east[LANE - 1:LANE, :]
    pltpu.make_async_copy(obuf, out_hbm, sem.at[1]).wait()


def fused_step(fields, rate, mix, act, flags, halo_lo, halo_hi, lft, rgt):
    nf, rows, lanes = fields.shape
    vmem = pltpu.VMEM
    smem = pl.BlockSpec(memory_space=pltpu.SMEM)
    vspec = pl.BlockSpec(memory_space=vmem)
    cells = rows * lanes
    cost = pl.CostEstimate(
        flops=2 * cells * nf * (2 * nf + 24),
        transcendentals=2 * cells * (nf + 3),
        bytes_accessed=4 * cells * (2 * nf + 1),
    )
    return pl.pallas_call(
        functools.partial(step_kernel, nf, rows, lanes),
        out_shape=(
            jax.ShapeDtypeStruct((nf, rows, lanes), jnp.float32),
            jax.ShapeDtypeStruct((nf, lanes), jnp.float32),
            jax.ShapeDtypeStruct((nf, lanes), jnp.float32),
            jax.ShapeDtypeStruct((nf, rows), jnp.float32),
            jax.ShapeDtypeStruct((nf, rows), jnp.float32),
        ),
        in_specs=[smem, smem, smem, pl.BlockSpec(memory_space=pl.ANY)] + [vspec] * 5,
        out_specs=(pl.BlockSpec(memory_space=pl.ANY),) + (vspec,) * 4,
        scratch_shapes=[
            vmem((nf, rows + 2 * SUB, lanes + 2 * LANE), jnp.float32),
            vmem((nf, rows + 2 * SUB, lanes + 2 * LANE), jnp.float32),
            vmem((nf * nf + nf, SUB, LANE), jnp.float32),
            vmem((nf, rows, lanes), jnp.float32),
            pltpu.SemaphoreType.DMA((2,)),
        ],
        compiler_params=pltpu.CompilerParams(vmem_limit_bytes=60 * 1024 * 1024),
        cost_estimate=cost,
    )(mix, act, flags, fields, rate, halo_lo, halo_hi, lft, rgt)


def interp_kernel(ks, flag_s, ids_s, wt_ref, table_ref, *refs):
    n_in = (len(refs) - 1) // 2
    ins, o_ref, outs, acc, picked = refs[:n_in], refs[n_in], refs[n_in + 1:-2], refs[-2], refs[-1]
    lanes = o_ref.shape[1]
    width = table_ref.shape[1]
    acc[...] = jnp.zeros(acc.shape, jnp.float32)

    @pl.when(flag_s[0] + flag_s[1] > 0.5)
    def _():
        def group(pg, carry):
            p0 = pl.multiple_of(pg * SUB, SUB)
            for s in range(SUB):
                for k in range(ks):
                    q = ids_s[k, p0 + s]
                    picked[k, pl.ds(p0 + s, 1), :] = table_ref[pl.ds(q, 1), :]
            return carry

        lax.fori_loop(0, lanes // SUB, group, 0)
        total = wt_ref[:, 0:1] * picked[0]
        for k in range(1, ks):
            total = total + wt_ref[:, k:k + 1] * picked[k]
        acc[:, 0:width] = total

    picked_t = jnp.transpose(acc[...])
    nf = o_ref.shape[0] // 2
    last_ref, first_ref = ins[0], ins[1]
    o_ref[0:nf, :] = jnp.where(flag_s[0] > 0.5, picked_t[0:nf, :], last_ref[...])
    o_ref[nf:2 * nf, :] = jnp.where(
        flag_s[1] > 0.5, jnp.broadcast_to(picked_t[nf:nf + 1, :], (nf, lanes)), first_ref[...]
    )
    for src, dst in zip(ins[2:], outs):
        dst[...] = src[...]


def interpolate(flags, ids, wt, table, passed):
    ks, lanes = ids.shape
    smem = pl.BlockSpec(memory_space=pltpu.SMEM)
    vspec = pl.BlockSpec(memory_space=pltpu.VMEM)
    width = table.shape[1]
    return pl.pallas_call(
        functools.partial(interp_kernel, ks),
        out_shape=(jax.ShapeDtypeStruct((2 * (width - 1), lanes), jnp.float32),)
        + tuple(jax.ShapeDtypeStruct(x.shape, x.dtype) for x in passed[2:]),
        in_specs=[smem, smem] + [vspec] * (2 + len(passed)),
        out_specs=(vspec,) * (len(passed) - 1),
        scratch_shapes=[
            pltpu.VMEM((lanes, LANE), jnp.float32),
            pltpu.VMEM((ks, lanes, width), jnp.float32),
        ],
    )(flags, ids, wt, table, *passed)


def fix_kernel(low_w, side_w, out_in, g0_ref, g1_ref, gl_ref, gr_ref, out_ref, rb, cb, sem):
    nf, rows, lanes = out_ref.shape
    mid = rows - 2 * SUB
    wins = [
        (out_ref.at[:, pl.ds(0, SUB), :], rb.at[0]),
        (out_ref.at[:, pl.ds(rows - SUB, SUB), :], rb.at[1]),
        (out_ref.at[:, pl.ds(SUB, mid), pl.ds(0, LANE)], cb.at[0]),
        (out_ref.at[:, pl.ds(SUB, mid), pl.ds(lanes - LANE, LANE)], cb.at[1]),
    ]
    loads = [pltpu.make_async_copy(hbm, buf, sem.at[s]) for s, (hbm, buf) in enumerate(wins)]
    for c in loads:
        c.start()
    for c in loads:
        c.wait()
    lane_id = lax.broadcasted_iota(jnp.int32, (rows, LANE), 1)
    row_lane = lax.broadcasted_iota(jnp.int32, (SUB, LANE), 1)
    for f in range(nf):
        west = jnp.where(lane_id == 0, side_w * tile_t(gl_ref[f:f + 1, :]), 0.0)
        east = jnp.where(lane_id == LANE - 1, side_w * tile_t(gr_ref[f:f + 1, :]), 0.0)
        cb[0, f] = cb[0, f] + west[SUB:rows - SUB]
        cb[1, f] = cb[1, f] + east[SUB:rows - SUB]
        for s, lo in ((0, 0), (1, rows - SUB)):
            rb[s, f, :, 0:LANE] = rb[s, f, :, 0:LANE] + west[lo:lo + SUB]
            rb[s, f, :, lanes - LANE:lanes] = rb[s, f, :, lanes - LANE:lanes] + east[lo:lo + SUB]
        rb[0, f, 0:1, :] = rb[0, f, 0:1, :] + low_w * g0_ref[f:f + 1, :]
        rb[1, f, SUB - 1:SUB, :] = rb[1, f, SUB - 1:SUB, :] + side_w * g1_ref[f:f + 1, :]
    stores = [pltpu.make_async_copy(buf, hbm, sem.at[s]) for s, (hbm, buf) in enumerate(wins)]
    for c in stores:
        c.start()
    for c in stores:
        c.wait()


def fix_edges(out, g0, g1, gl, gr, low_w, side_w):
    nf, rows, lanes = out.shape
    vspec = pl.BlockSpec(memory_space=pltpu.VMEM)
    anyspec = pl.BlockSpec(memory_space=pl.ANY)
    return pl.pallas_call(
        functools.partial(fix_kernel, low_w, side_w),
        out_shape=jax.ShapeDtypeStruct(out.shape, jnp.float32),
        in_specs=[anyspec, vspec, vspec, vspec, vspec],
        out_specs=anyspec,
        scratch_shapes=[
            pltpu.VMEM((2, nf, SUB, lanes), jnp.float32),
            pltpu.VMEM((2, nf, rows - 2 * SUB, LANE), jnp.float32),
            pltpu.SemaphoreType.DMA((4,)),
        ],
        input_output_aliases={0: 0},
    )(out, g0, g1, gl, gr)


def shards(
    fields, react_rate, mix_matrix, activation, inlet_ids, inlet_weights, outlet_ids, outlet_weights
):
    nf, rows, lanes = fields.shape
    n_grp = lax.axis_size("grp")
    n_blk = lax.axis_size("blk")
    g = lax.axis_index("grp")
    b = lax.axis_index("blk")
    exit_grp = n_grp - 2
    turb_grp = n_grp - 1
    flags = jnp.stack([g == exit_grp, g == turb_grp]).astype(jnp.float32)

    last_row = fields[:, -1, :]
    first_row = fields[:, 0, :]
    payload = jnp.concatenate([last_row, first_row[4:5]], axis=0)
    planes = payload[None]
    spans = []
    span = n_blk // 2
    edges = (last_row, first_row, fields[:, :, lanes - 1], fields[:, :, 0])
    while span >= 1:
        spans.append(span)
        if span == 1:
            edges, planes = lax.optimization_barrier((edges, planes))
        partner = [(i, i ^ span) for i in range(n_blk)]
        planes = jnp.concatenate([planes, lax.ppermute(planes, "blk", partner)], axis=0)
        span //= 2
    table = jnp.transpose(planes, (0, 2, 1)).reshape(n_blk * lanes, nf + 1)
    at_exit = g == exit_grp
    ids = jnp.where(at_exit, inlet_ids, outlet_ids)
    m = jnp.bitwise_xor(ids // lanes, b)
    slot = jnp.zeros_like(m)
    for r, span in enumerate(spans):
        slot = slot + ((m // span) % 2) * (1 << r)
    ids = slot * lanes + ids % lanes
    wt = jnp.transpose(jnp.where(at_exit, inlet_weights, outlet_weights))
    lft = lax.ppermute(edges[2], "blk", [(i, (i + 1) % n_blk) for i in range(n_blk)])
    rgt = lax.ppermute(edges[3], "blk", [((i + 1) % n_blk, i) for i in range(n_blk)])

    sends, lft, rgt = interpolate(flags, ids, wt, table, (edges[0], edges[1], lft, rgt))
    halo_lo = lax.ppermute(sends[:nf], "grp", [(i, i + 1) for i in range(n_grp - 1)])
    halo_hi = lax.ppermute(sends[nf:], "grp", [(i + 1, i) for i in range(n_grp - 1)])

    out, elo, ehi, clo, chi = fused_step(
        fields, react_rate, mix_matrix, activation, flags, halo_lo, halo_hi, lft, rgt
    )

    g0 = lax.ppermute(ehi, "grp", [(i, i + 1) for i in range(n_grp - 2)])
    g1 = lax.ppermute(elo, "grp", [(i + 1, i) for i in range(n_grp - 2)])
    gl = lax.ppermute(chi, "blk", [(i, (i + 1) % n_blk) for i in range(n_blk)])
    gr = lax.ppermute(clo, "blk", [((i + 1) % n_blk, i) for i in range(n_blk)])
    low_w = 0.5 * (courant + diffusion)
    side_w = 0.5 * diffusion
    return fix_edges(out, g0, g1, gl, gr, low_w, side_w)


def solution(mesh):
    in_specs = (
        P(None, "grp", "blk"),
        P("grp", "blk"),
        P(),
        P(),
        P(None, "blk"),
        P(None, "blk"),
        P(None, "blk"),
        P(None, "blk"),
    )
    out_specs = P(None, "grp", "blk")
    return jax.shard_map(shards, mesh=mesh, in_specs=in_specs, out_specs=out_specs, check_vma=False)
```

```python
import functools

import jax
import jax.numpy as jnp
from jax import lax
from jax.experimental import pallas as pl
from jax.experimental.pallas import tpu as pltpu
from jax.sharding import PartitionSpec as P

courant = 0.5
diffusion = 0.1
source_step = 0.5

SUB = 8
LANE = 128


def tile_t(row):
    n = row.shape[1]
    return jnp.transpose(jnp.broadcast_to(row, (n, n)))


def step_kernel(nf, rows, lanes, mix_s, act_s, flag_s, f_hbm, rate_ref, hlo_ref, hhi_ref,
                lft_ref, rgt_ref, out_hbm, elo_ref, ehi_ref, clo_ref, chi_ref, ext1, ext2, coef, obuf,
                sem):
    n_i = rows // SUB
    n_j = lanes // LANE
    top = SUB + rows
    right = LANE + lanes
    at_exit = flag_s[0] > 0.5
    at_turb = flag_s[1] > 0.5
    at_end = flag_s[0] + flag_s[1] > 0.5

    copy = pltpu.make_async_copy(f_hbm, ext1.at[:, SUB:top, LANE:right], sem.at[0])
    copy.start()
    zeros = jnp.zeros((rows, LANE), jnp.float32)
    for f in range(nf):
        low = hlo_ref[f:f + 1, :]
        ext1[f, SUB - 1:SUB, LANE:right] = low
        ext2[f, SUB - 1:SUB, LANE:right] = jnp.where(at_turb, low, 0.0)
        ext1[f, SUB:top, 0:LANE] = tile_t(lft_ref[f:f + 1, :])
        ext1[f, SUB:top, right:right + LANE] = tile_t(rgt_ref[f:f + 1, :])
        ext2[f, SUB:top, 0:LANE] = zeros
        ext2[f, SUB:top, right:right + LANE] = zeros
    for f in range(nf):
        for g in range(nf):
            coef[f * nf + g] = jnp.full((SUB, LANE), source_step * mix_s[f, g], jnp.float32)
        coef[nf * nf + f] = jnp.full((SUB, LANE), -act_s[f], jnp.float32)
    copy.wait()

    def high_ghost(ext, outside):
        for f in range(nf):
            own = ext[f, top - 1:top, LANE:right]
            halo = hhi_ref[f:f + 1, :]
            if f == 4:
                row = jnp.where(at_turb, own, jnp.where(at_exit | outside, halo, 0.0))
            else:
                row = jnp.where(at_end, own, jnp.where(outside, halo, 0.0))
            ext[f, top:top + 1, LANE:right] = row

    high_ghost(ext1, True)

    sub_id = lax.broadcasted_iota(jnp.int32, (SUB, LANE), 0)
    lane_id = lax.broadcasted_iota(jnp.int32, (SUB, LANE), 1)
    first_sub = sub_id == 0
    last_sub = sub_id == SUB - 1
    first_lane = lane_id == 0
    last_lane = lane_id == LANE - 1

    def tendency_tiles(src, r0, c0s, rate_ts):
        r = pl.multiple_of(r0 + SUB, SUB)
        r_up = pl.multiple_of(r0, SUB)
        r_dn = pl.multiple_of(r0 + 2 * SUB, SUB)
        cs = [pl.multiple_of(c0 + LANE, LANE) for c0 in c0s]
        reacts = []
        for c, rate_t in zip(cs, rate_ts):
            v4 = src[4, pl.ds(r, SUB), pl.ds(c, LANE)]
            heat = 1.0 + (jnp.maximum(v4, 0.0) + jnp.log1p(jnp.exp(-jnp.abs(v4))))
            inv_heat = 1.0 / heat
            reacts.append([
                rate_t * src[f, pl.ds(r, SUB), pl.ds(c, LANE)] * jnp.exp(coef[nf * nf + f] * inv_heat)
                for f in range(nf)
            ])
        tends = [[] for _ in cs]
        for f in range(nf):
            accs = [None] * len(cs)
            for g in range(nf):
                m = coef[f * nf + g]
                for h in range(len(cs)):
                    term = m * reacts[h][g]
                    accs[h] = term if accs[h] is None else accs[h] + term
            for h, c in enumerate(cs):
                c_w = pl.multiple_of(c - LANE, LANE)
                c_e = pl.multiple_of(c + LANE, LANE)
                v = src[f, pl.ds(r, SUB), pl.ds(c, LANE)]
                up = src[f, pl.ds(r_up, SUB), pl.ds(c, LANE)]
                down = src[f, pl.ds(r_dn, SUB), pl.ds(c, LANE)]
                west = src[f, pl.ds(r, SUB), pl.ds(c_w, LANE)]
                east = src[f, pl.ds(r, SUB), pl.ds(c_e, LANE)]
                backward = jnp.where(first_sub, pltpu.roll(up, 1, 0), pltpu.roll(v, 1, 0))
                forward = jnp.where(last_sub, pltpu.roll(down, SUB - 1, 0), pltpu.roll(v, SUB - 1, 0))
                left = jnp.where(first_lane, pltpu.roll(west, 1, 1), pltpu.roll(v, 1, 1))
                rgt = jnp.where(last_lane, pltpu.roll(east, LANE - 1, 1), pltpu.roll(v, LANE - 1, 1))
                flow = (courant + diffusion) * backward + diffusion * (forward + left + rgt)
                flow = flow - (courant + 4.0 * diffusion) * v
                tends[h].append((v, flow + accs[h]))
        return tends

    pair = 2 if n_j % 2 == 0 else 1
    n_jp = n_j // pair

    def tile_offsets(t):
        i = t // n_jp
        jp = t % n_jp
        r0 = pl.multiple_of(i * SUB, SUB)
        c0s = [pl.multiple_of((jp * pair + h) * LANE, LANE) for h in range(pair)]
        return r0, c0s

    def stage_one(t, carry):
        r0, c0s = tile_offsets(t)
        rate_ts = [rate_ref[pl.ds(r0, SUB), pl.ds(c0, LANE)] for c0 in c0s]
        tends = tendency_tiles(ext1, r0, c0s, rate_ts)
        r = pl.multiple_of(r0 + SUB, SUB)
        for c0, tend in zip(c0s, tends):
            c = pl.multiple_of(c0 + LANE, LANE)
            for f in range(nf):
                v, tf = tend[f]
                ext2[f, pl.ds(r, SUB), pl.ds(c, LANE)] = v + tf
        return carry

    lax.fori_loop(0, n_i * n_jp, stage_one, 0)

    high_ghost(ext2, False)

    def stage_two(i, carry):
        for jp in range(n_jp):
            r0, c0s = tile_offsets(i * n_jp + jp)
            rate_ts = [rate_ref[pl.ds(r0, SUB), pl.ds(c0, LANE)] for c0 in c0s]
            tends = tendency_tiles(ext2, r0, c0s, rate_ts)
            r = pl.multiple_of(r0 + SUB, SUB)
            for c0, tend in zip(c0s, tends):
                c = pl.multiple_of(c0 + LANE, LANE)
                for f in range(nf):
                    v, tf = tend[f]
                    base = ext1[f, pl.ds(r, SUB), pl.ds(c, LANE)]
                    obuf[f, pl.ds(r0, SUB), pl.ds(c0, LANE)] = 0.5 * (base + v + tf)
        r0 = pl.multiple_of(i * SUB, SUB)
        pltpu.make_async_copy(
            obuf.at[:, pl.ds(r0, SUB), :], out_hbm.at[:, pl.ds(r0, SUB), :], sem.at[1]
        ).start()
        return carry

    lax.fori_loop(0, n_i, stage_two, 0)

    for f in range(nf):
        elo_ref[f:f + 1, :] = ext2[f, SUB:SUB + 1, LANE:right]
        ehi_ref[f:f + 1, :] = ext2[f, top - 1:top, LANE:right]
        west = jnp.transpose(ext2[f, SUB:top, LANE:2 * LANE])
        east = jnp.transpose(ext2[f, SUB:top, right - LANE:right])
        clo_ref[f:f + 1, :] = west[0:1, :]
        chi_ref[f:f + 1, :] = east[LANE - 1:LANE, :]
    pltpu.make_async_copy(obuf, out_hbm, sem.at[1]).wait()


def fused_step(fields, rate, mix, act, flags, halo_lo, halo_hi, lft, rgt):
    nf, rows, lanes = fields.shape
    vmem = pltpu.VMEM
    smem = pl.BlockSpec(memory_space=pltpu.SMEM)
    vspec = pl.BlockSpec(memory_space=vmem)
    cells = rows * lanes
    cost = pl.CostEstimate(
        flops=2 * cells * nf * (2 * nf + 24),
        transcendentals=2 * cells * (nf + 3),
        bytes_accessed=4 * cells * (2 * nf + 1),
    )
    return pl.pallas_call(
        functools.partial(step_kernel, nf, rows, lanes),
        out_shape=(
            jax.ShapeDtypeStruct((nf, rows, lanes), jnp.float32),
            jax.ShapeDtypeStruct((nf, lanes), jnp.float32),
            jax.ShapeDtypeStruct((nf, lanes), jnp.float32),
            jax.ShapeDtypeStruct((nf, rows), jnp.float32),
            jax.ShapeDtypeStruct((nf, rows), jnp.float32),
        ),
        in_specs=[smem, smem, smem, pl.BlockSpec(memory_space=pl.ANY)] + [vspec] * 5,
        out_specs=(pl.BlockSpec(memory_space=pl.ANY),) + (vspec,) * 4,
        scratch_shapes=[
            vmem((nf, rows + 2 * SUB, lanes + 2 * LANE), jnp.float32),
            vmem((nf, rows + 2 * SUB, lanes + 2 * LANE), jnp.float32),
            vmem((nf * nf + nf, SUB, LANE), jnp.float32),
            vmem((nf, rows, lanes), jnp.float32),
            pltpu.SemaphoreType.DMA((2,)),
        ],
        compiler_params=pltpu.CompilerParams(vmem_limit_bytes=60 * 1024 * 1024),
        cost_estimate=cost,
    )(mix, act, flags, fields, rate, halo_lo, halo_hi, lft, rgt)


def interp_kernel(ks, flag_s, ids_s, wt_ref, table_ref, *refs):
    n_in = (len(refs) - 2) // 2
    ins, outs, acc, picked = refs[:n_in], refs[n_in:2 * n_in], refs[-2], refs[-1]
    up_ref, down_ref = outs[0], outs[1]
    lanes = outs[0].shape[1]
    width = table_ref.shape[1]
    acc[...] = jnp.zeros(acc.shape, jnp.float32)

    @pl.when(flag_s[0] + flag_s[1] > 0.5)
    def _():
        def group(pg, carry):
            p0 = pl.multiple_of(pg * SUB, SUB)
            for s in range(SUB):
                for k in range(ks):
                    q = ids_s[k, p0 + s]
                    picked[k, pl.ds(p0 + s, 1), :] = table_ref[pl.ds(q, 1), :]
            return carry

        lax.fori_loop(0, lanes // SUB, group, 0)
        total = wt_ref[:, 0:1] * picked[0]
        for k in range(1, ks):
            total = total + wt_ref[:, k:k + 1] * picked[k]
        acc[:, 0:width] = total

    picked_t = jnp.transpose(acc[...])
    nf = up_ref.shape[0]
    last_ref, first_ref = ins[0], ins[1]
    up_ref[...] = jnp.where(flag_s[0] > 0.5, picked_t[0:nf, :], last_ref[...])
    down_ref[...] = jnp.where(
        flag_s[1] > 0.5, jnp.broadcast_to(picked_t[nf:nf + 1, :], (nf, lanes)), first_ref[...]
    )
    for src, dst in zip(ins[2:], outs[2:]):
        dst[...] = src[...]


def interpolate(flags, ids, wt, table, passed):
    ks, lanes = ids.shape
    smem = pl.BlockSpec(memory_space=pltpu.SMEM)
    vspec = pl.BlockSpec(memory_space=pltpu.VMEM)
    width = table.shape[1]
    return pl.pallas_call(
        functools.partial(interp_kernel, ks),
        out_shape=tuple(jax.ShapeDtypeStruct(x.shape, x.dtype) for x in passed),
        in_specs=[smem, smem] + [vspec] * (2 + len(passed)),
        out_specs=(vspec,) * len(passed),
        scratch_shapes=[
            pltpu.VMEM((lanes, LANE), jnp.float32),
            pltpu.VMEM((ks, lanes, width), jnp.float32),
        ],
    )(flags, ids, wt, table, *passed)


def fix_kernel(low_w, side_w, out_in, g0_ref, g1_ref, gl_ref, gr_ref, out_ref, rb, cb, sem):
    nf, rows, lanes = out_ref.shape
    mid = rows - 2 * SUB
    wins = [
        (out_ref.at[:, pl.ds(0, SUB), :], rb.at[0]),
        (out_ref.at[:, pl.ds(rows - SUB, SUB), :], rb.at[1]),
        (out_ref.at[:, pl.ds(SUB, mid), pl.ds(0, LANE)], cb.at[0]),
        (out_ref.at[:, pl.ds(SUB, mid), pl.ds(lanes - LANE, LANE)], cb.at[1]),
    ]
    loads = [pltpu.make_async_copy(hbm, buf, sem.at[s]) for s, (hbm, buf) in enumerate(wins)]
    for c in loads:
        c.start()
    for c in loads:
        c.wait()
    lane_id = lax.broadcasted_iota(jnp.int32, (rows, LANE), 1)
    row_lane = lax.broadcasted_iota(jnp.int32, (SUB, LANE), 1)
    for f in range(nf):
        west = jnp.where(lane_id == 0, side_w * tile_t(gl_ref[f:f + 1, :]), 0.0)
        east = jnp.where(lane_id == LANE - 1, side_w * tile_t(gr_ref[f:f + 1, :]), 0.0)
        cb[0, f] = cb[0, f] + west[SUB:rows - SUB]
        cb[1, f] = cb[1, f] + east[SUB:rows - SUB]
        for s, lo in ((0, 0), (1, rows - SUB)):
            rb[s, f, :, 0:LANE] = rb[s, f, :, 0:LANE] + west[lo:lo + SUB]
            rb[s, f, :, lanes - LANE:lanes] = rb[s, f, :, lanes - LANE:lanes] + east[lo:lo + SUB]
        rb[0, f, 0:1, :] = rb[0, f, 0:1, :] + low_w * g0_ref[f:f + 1, :]
        rb[1, f, SUB - 1:SUB, :] = rb[1, f, SUB - 1:SUB, :] + side_w * g1_ref[f:f + 1, :]
    stores = [pltpu.make_async_copy(buf, hbm, sem.at[s]) for s, (hbm, buf) in enumerate(wins)]
    for c in stores:
        c.start()
    for c in stores:
        c.wait()


def fix_edges(out, g0, g1, gl, gr, low_w, side_w):
    nf, rows, lanes = out.shape
    vspec = pl.BlockSpec(memory_space=pltpu.VMEM)
    anyspec = pl.BlockSpec(memory_space=pl.ANY)
    return pl.pallas_call(
        functools.partial(fix_kernel, low_w, side_w),
        out_shape=jax.ShapeDtypeStruct(out.shape, jnp.float32),
        in_specs=[anyspec, vspec, vspec, vspec, vspec],
        out_specs=anyspec,
        scratch_shapes=[
            pltpu.VMEM((2, nf, SUB, lanes), jnp.float32),
            pltpu.VMEM((2, nf, rows - 2 * SUB, LANE), jnp.float32),
            pltpu.SemaphoreType.DMA((4,)),
        ],
        input_output_aliases={0: 0},
    )(out, g0, g1, gl, gr)


def shards(
    fields, react_rate, mix_matrix, activation, inlet_ids, inlet_weights, outlet_ids, outlet_weights
):
    nf, rows, lanes = fields.shape
    n_grp = lax.axis_size("grp")
    n_blk = lax.axis_size("blk")
    g = lax.axis_index("grp")
    b = lax.axis_index("blk")
    exit_grp = n_grp - 2
    turb_grp = n_grp - 1
    flags = jnp.stack([g == exit_grp, g == turb_grp]).astype(jnp.float32)

    last_row = fields[:, -1, :]
    first_row = fields[:, 0, :]
    payload = jnp.concatenate([last_row, first_row[4:5]], axis=0)
    planes = payload[None]
    spans = []
    span = n_blk // 2
    edges = (last_row, first_row, fields[:, :, lanes - 1], fields[:, :, 0])
    while span >= 1:
        spans.append(span)
        if span == 1:
            edges, planes = lax.optimization_barrier((edges, planes))
        partner = [(i, i ^ span) for i in range(n_blk)]
        planes = jnp.concatenate([planes, lax.ppermute(planes, "blk", partner)], axis=0)
        span //= 2
    table = jnp.transpose(planes, (0, 2, 1)).reshape(n_blk * lanes, nf + 1)
    at_exit = g == exit_grp
    ids = jnp.where(at_exit, inlet_ids, outlet_ids)
    m = jnp.bitwise_xor(ids // lanes, b)
    slot = jnp.zeros_like(m)
    for r, span in enumerate(spans):
        slot = slot + ((m // span) % 2) * (1 << r)
    ids = slot * lanes + ids % lanes
    wt = jnp.transpose(jnp.where(at_exit, inlet_weights, outlet_weights))
    lft = lax.ppermute(edges[2], "blk", [(i, (i + 1) % n_blk) for i in range(n_blk)])
    rgt = lax.ppermute(edges[3], "blk", [((i + 1) % n_blk, i) for i in range(n_blk)])

    up, down, lft, rgt = interpolate(flags, ids, wt, table, (edges[0], edges[1], lft, rgt))
    halo_lo = lax.ppermute(up, "grp", [(i, i + 1) for i in range(n_grp - 1)])
    halo_hi = lax.ppermute(down, "grp", [(i + 1, i) for i in range(n_grp - 1)])

    out, elo, ehi, clo, chi = fused_step(
        fields, react_rate, mix_matrix, activation, flags, halo_lo, halo_hi, lft, rgt
    )

    g0 = lax.ppermute(ehi, "grp", [(i, i + 1) for i in range(n_grp - 2)])
    g1 = lax.ppermute(elo, "grp", [(i + 1, i) for i in range(n_grp - 2)])
    gl = lax.ppermute(chi, "blk", [(i, (i + 1) % n_blk) for i in range(n_blk)])
    gr = lax.ppermute(clo, "blk", [((i + 1) % n_blk, i) for i in range(n_blk)])
    low_w = 0.5 * (courant + diffusion)
    side_w = 0.5 * diffusion
    return fix_edges(out, g0, g1, gl, gr, low_w, side_w)


def solution(mesh):
    in_specs = (
        P(None, "grp", "blk"),
        P("grp", "blk"),
        P(),
        P(),
        P(None, "blk"),
        P(None, "blk"),
        P(None, "blk"),
        P(None, "blk"),
    )
    out_specs = P(None, "grp", "blk")
    return jax.shard_map(shards, mesh=mesh, in_specs=in_specs, out_specs=out_specs, check_vma=False)
```

```python
import functools

import jax
import jax.numpy as jnp
from jax import lax
from jax.experimental import pallas as pl
from jax.experimental.pallas import tpu as pltpu
from jax.sharding import PartitionSpec as P

courant = 0.5
diffusion = 0.1
source_step = 0.5

SUB = 8
LANE = 128


def tile_t(row):
    n = row.shape[1]
    return jnp.transpose(jnp.broadcast_to(row, (n, n)))


def step_kernel(nf, rows, lanes, mix_s, act_s, flag_s, f_hbm, rate_ref, hlo_ref, hhi_ref,
                lft_ref, rgt_ref, out_hbm, elo_ref, ehi_ref, clo_ref, chi_ref, ext1, ext2, coef, obuf,
                sem):
    n_i = rows // SUB
    n_j = lanes // LANE
    top = SUB + rows
    right = LANE + lanes
    at_exit = flag_s[0] > 0.5
    at_turb = flag_s[1] > 0.5
    at_end = flag_s[0] + flag_s[1] > 0.5

    copy = pltpu.make_async_copy(f_hbm, ext1.at[:, SUB:top, LANE:right], sem.at[0])
    copy.start()
    zeros = jnp.zeros((rows, LANE), jnp.float32)
    for f in range(nf):
        low = hlo_ref[f:f + 1, :]
        ext1[f, SUB - 1:SUB, LANE:right] = low
        ext2[f, SUB - 1:SUB, LANE:right] = jnp.where(at_turb, low, 0.0)
        ext1[f, SUB:top, 0:LANE] = tile_t(lft_ref[f:f + 1, :])
        ext1[f, SUB:top, right:right + LANE] = tile_t(rgt_ref[f:f + 1, :])
        ext2[f, SUB:top, 0:LANE] = zeros
        ext2[f, SUB:top, right:right + LANE] = zeros
    for f in range(nf):
        for g in range(nf):
            coef[f * nf + g] = jnp.full((SUB, LANE), source_step * mix_s[f, g], jnp.float32)
        coef[nf * nf + f] = jnp.full((SUB, LANE), -act_s[f], jnp.float32)
    copy.wait()

    def high_ghost(ext, outside):
        for f in range(nf):
            own = ext[f, top - 1:top, LANE:right]
            halo = hhi_ref[f:f + 1, :]
            if f == 4:
                row = jnp.where(at_turb, own, jnp.where(at_exit | outside, halo, 0.0))
            else:
                row = jnp.where(at_end, own, jnp.where(outside, halo, 0.0))
            ext[f, top:top + 1, LANE:right] = row

    high_ghost(ext1, True)

    sub_id = lax.broadcasted_iota(jnp.int32, (SUB, LANE), 0)
    lane_id = lax.broadcasted_iota(jnp.int32, (SUB, LANE), 1)
    first_sub = sub_id == 0
    last_sub = sub_id == SUB - 1
    first_lane = lane_id == 0
    last_lane = lane_id == LANE - 1

    def tendency_tiles(src, r0, c0s, rate_ts):
        r = pl.multiple_of(r0 + SUB, SUB)
        r_up = pl.multiple_of(r0, SUB)
        r_dn = pl.multiple_of(r0 + 2 * SUB, SUB)
        cs = [pl.multiple_of(c0 + LANE, LANE) for c0 in c0s]
        reacts = []
        for c, rate_t in zip(cs, rate_ts):
            v4 = src[4, pl.ds(r, SUB), pl.ds(c, LANE)]
            heat = 1.0 + (jnp.maximum(v4, 0.0) + jnp.log1p(jnp.exp(-jnp.abs(v4))))
            inv_heat = 1.0 / heat
            reacts.append([
                rate_t * src[f, pl.ds(r, SUB), pl.ds(c, LANE)] * jnp.exp(coef[nf * nf + f] * inv_heat)
                for f in range(nf)
            ])
        tends = [[] for _ in cs]
        for f in range(nf):
            accs = [None] * len(cs)
            for g in range(nf):
                m = coef[f * nf + g]
                for h in range(len(cs)):
                    term = m * reacts[h][g]
                    accs[h] = term if accs[h] is None else accs[h] + term
            for h, c in enumerate(cs):
                c_w = pl.multiple_of(c - LANE, LANE)
                c_e = pl.multiple_of(c + LANE, LANE)
                v = src[f, pl.ds(r, SUB), pl.ds(c, LANE)]
                up = src[f, pl.ds(r_up, SUB), pl.ds(c, LANE)]
                down = src[f, pl.ds(r_dn, SUB), pl.ds(c, LANE)]
                west = src[f, pl.ds(r, SUB), pl.ds(c_w, LANE)]
                east = src[f, pl.ds(r, SUB), pl.ds(c_e, LANE)]
                backward = jnp.where(first_sub, pltpu.roll(up, 1, 0), pltpu.roll(v, 1, 0))
                forward = jnp.where(last_sub, pltpu.roll(down, SUB - 1, 0), pltpu.roll(v, SUB - 1, 0))
                left = jnp.where(first_lane, pltpu.roll(west, 1, 1), pltpu.roll(v, 1, 1))
                rgt = jnp.where(last_lane, pltpu.roll(east, LANE - 1, 1), pltpu.roll(v, LANE - 1, 1))
                flow = (courant + diffusion) * backward + diffusion * (forward + left + rgt)
                flow = flow - (courant + 4.0 * diffusion) * v
                tends[h].append((v, flow + accs[h]))
        return tends

    pair = 2 if n_j % 2 == 0 else 1
    n_jp = n_j // pair

    def tile_offsets(t):
        i = t // n_jp
        jp = t % n_jp
        r0 = pl.multiple_of(i * SUB, SUB)
        c0s = [pl.multiple_of((jp * pair + h) * LANE, LANE) for h in range(pair)]
        return r0, c0s

    def stage_one(t, carry):
        r0, c0s = tile_offsets(t)
        rate_ts = [rate_ref[pl.ds(r0, SUB), pl.ds(c0, LANE)] for c0 in c0s]
        tends = tendency_tiles(ext1, r0, c0s, rate_ts)
        r = pl.multiple_of(r0 + SUB, SUB)
        for c0, tend in zip(c0s, tends):
            c = pl.multiple_of(c0 + LANE, LANE)
            for f in range(nf):
                v, tf = tend[f]
                ext2[f, pl.ds(r, SUB), pl.ds(c, LANE)] = v + tf
        return carry

    lax.fori_loop(0, n_i * n_jp, stage_one, 0)

    high_ghost(ext2, False)

    def stage_two(i, carry):
        for jp in range(n_jp):
            r0, c0s = tile_offsets(i * n_jp + jp)
            rate_ts = [rate_ref[pl.ds(r0, SUB), pl.ds(c0, LANE)] for c0 in c0s]
            tends = tendency_tiles(ext2, r0, c0s, rate_ts)
            r = pl.multiple_of(r0 + SUB, SUB)
            for c0, tend in zip(c0s, tends):
                c = pl.multiple_of(c0 + LANE, LANE)
                for f in range(nf):
                    v, tf = tend[f]
                    base = ext1[f, pl.ds(r, SUB), pl.ds(c, LANE)]
                    obuf[f, pl.ds(r0, SUB), pl.ds(c0, LANE)] = 0.5 * (base + v + tf)
        r0 = pl.multiple_of(i * SUB, SUB)
        pltpu.make_async_copy(
            obuf.at[:, pl.ds(r0, SUB), :], out_hbm.at[:, pl.ds(r0, SUB), :], sem.at[1]
        ).start()
        return carry

    lax.fori_loop(0, n_i, stage_two, 0)

    for f in range(nf):
        elo_ref[f:f + 1, :] = ext2[f, SUB:SUB + 1, LANE:right]
        ehi_ref[f:f + 1, :] = ext2[f, top - 1:top, LANE:right]
        west = jnp.transpose(ext2[f, SUB:top, LANE:2 * LANE])
        east = jnp.transpose(ext2[f, SUB:top, right - LANE:right])
        clo_ref[f:f + 1, :] = west[0:1, :]
        chi_ref[f:f + 1, :] = east[LANE - 1:LANE, :]
    pltpu.make_async_copy(obuf, out_hbm, sem.at[1]).wait()


def fused_step(fields, rate, mix, act, flags, halo_lo, halo_hi, lft, rgt):
    nf, rows, lanes = fields.shape
    vmem = pltpu.VMEM
    smem = pl.BlockSpec(memory_space=pltpu.SMEM)
    vspec = pl.BlockSpec(memory_space=vmem)
    cells = rows * lanes
    cost = pl.CostEstimate(
        flops=2 * cells * nf * (2 * nf + 24),
        transcendentals=2 * cells * (nf + 3),
        bytes_accessed=4 * cells * (2 * nf + 1),
    )
    return pl.pallas_call(
        functools.partial(step_kernel, nf, rows, lanes),
        out_shape=(
            jax.ShapeDtypeStruct((nf, rows, lanes), jnp.float32),
            jax.ShapeDtypeStruct((nf, lanes), jnp.float32),
            jax.ShapeDtypeStruct((nf, lanes), jnp.float32),
            jax.ShapeDtypeStruct((nf, rows), jnp.float32),
            jax.ShapeDtypeStruct((nf, rows), jnp.float32),
        ),
        in_specs=[smem, smem, smem, pl.BlockSpec(memory_space=pl.ANY)] + [vspec] * 5,
        out_specs=(pl.BlockSpec(memory_space=pl.ANY),) + (vspec,) * 4,
        scratch_shapes=[
            vmem((nf, rows + 2 * SUB, lanes + 2 * LANE), jnp.float32),
            vmem((nf, rows + 2 * SUB, lanes + 2 * LANE), jnp.float32),
            vmem((nf * nf + nf, SUB, LANE), jnp.float32),
            vmem((nf, rows, lanes), jnp.float32),
            pltpu.SemaphoreType.DMA((2,)),
        ],
        compiler_params=pltpu.CompilerParams(vmem_limit_bytes=60 * 1024 * 1024),
        cost_estimate=cost,
    )(mix, act, flags, fields, rate, halo_lo, halo_hi, lft, rgt)


def interp_kernel(ks, flag_s, ids_s, wt_ref, planes_ref, *refs):
    n_in = (len(refs) - 3) // 2
    ins, outs, acc, picked, table_ref = refs[:n_in], refs[n_in:2 * n_in], refs[-3], refs[-2], refs[-1]
    up_ref, down_ref = outs[0], outs[1]
    lanes = outs[0].shape[1]
    width = table_ref.shape[1]
    acc[...] = jnp.zeros(acc.shape, jnp.float32)

    @pl.when(flag_s[0] + flag_s[1] > 0.5)
    def _():
        for m in range(planes_ref.shape[0]):
            table_ref[m * lanes:(m + 1) * lanes, :] = jnp.transpose(planes_ref[m])

        def group(pg, carry):
            p0 = pl.multiple_of(pg * SUB, SUB)
            for s in range(SUB):
                for k in range(ks):
                    q = ids_s[k, p0 + s]
                    picked[k, pl.ds(p0 + s, 1), :] = table_ref[pl.ds(q, 1), :]
            return carry

        lax.fori_loop(0, lanes // SUB, group, 0)
        total = wt_ref[:, 0:1] * picked[0]
        for k in range(1, ks):
            total = total + wt_ref[:, k:k + 1] * picked[k]
        acc[:, 0:width] = total

    picked_t = jnp.transpose(acc[...])
    nf = up_ref.shape[0]
    last_ref, first_ref = ins[0], ins[1]
    up_ref[...] = jnp.where(flag_s[0] > 0.5, picked_t[0:nf, :], last_ref[...])
    down_ref[...] = jnp.where(
        flag_s[1] > 0.5, jnp.broadcast_to(picked_t[nf:nf + 1, :], (nf, lanes)), first_ref[...]
    )
    for src, dst in zip(ins[2:], outs[2:]):
        dst[...] = src[...]


def interpolate(flags, ids, wt, planes, passed):
    ks, lanes = ids.shape
    smem = pl.BlockSpec(memory_space=pltpu.SMEM)
    vspec = pl.BlockSpec(memory_space=pltpu.VMEM)
    n_planes, width, _ = planes.shape
    return pl.pallas_call(
        functools.partial(interp_kernel, ks),
        out_shape=tuple(jax.ShapeDtypeStruct(x.shape, x.dtype) for x in passed),
        in_specs=[smem, smem] + [vspec] * (2 + len(passed)),
        out_specs=(vspec,) * len(passed),
        scratch_shapes=[
            pltpu.VMEM((lanes, LANE), jnp.float32),
            pltpu.VMEM((ks, lanes, width), jnp.float32),
            pltpu.VMEM((n_planes * lanes, width), jnp.float32),
        ],
    )(flags, ids, wt, planes, *passed)


def fix_kernel(low_w, side_w, out_in, g0_ref, g1_ref, gl_ref, gr_ref, out_ref, rb, cb, sem):
    nf, rows, lanes = out_ref.shape
    mid = rows - 2 * SUB
    wins = [
        (out_ref.at[:, pl.ds(0, SUB), :], rb.at[0]),
        (out_ref.at[:, pl.ds(rows - SUB, SUB), :], rb.at[1]),
        (out_ref.at[:, pl.ds(SUB, mid), pl.ds(0, LANE)], cb.at[0]),
        (out_ref.at[:, pl.ds(SUB, mid), pl.ds(lanes - LANE, LANE)], cb.at[1]),
    ]
    loads = [pltpu.make_async_copy(hbm, buf, sem.at[s]) for s, (hbm, buf) in enumerate(wins)]
    for c in loads:
        c.start()
    for c in loads:
        c.wait()
    lane_id = lax.broadcasted_iota(jnp.int32, (rows, LANE), 1)
    row_lane = lax.broadcasted_iota(jnp.int32, (SUB, LANE), 1)
    for f in range(nf):
        west = jnp.where(lane_id == 0, side_w * tile_t(gl_ref[f:f + 1, :]), 0.0)
        east = jnp.where(lane_id == LANE - 1, side_w * tile_t(gr_ref[f:f + 1, :]), 0.0)
        cb[0, f] = cb[0, f] + west[SUB:rows - SUB]
        cb[1, f] = cb[1, f] + east[SUB:rows - SUB]
        for s, lo in ((0, 0), (1, rows - SUB)):
            rb[s, f, :, 0:LANE] = rb[s, f, :, 0:LANE] + west[lo:lo + SUB]
            rb[s, f, :, lanes - LANE:lanes] = rb[s, f, :, lanes - LANE:lanes] + east[lo:lo + SUB]
        rb[0, f, 0:1, :] = rb[0, f, 0:1, :] + low_w * g0_ref[f:f + 1, :]
        rb[1, f, SUB - 1:SUB, :] = rb[1, f, SUB - 1:SUB, :] + side_w * g1_ref[f:f + 1, :]
    stores = [pltpu.make_async_copy(buf, hbm, sem.at[s]) for s, (hbm, buf) in enumerate(wins)]
    for c in stores:
        c.start()
    for c in stores:
        c.wait()


def fix_edges(out, g0, g1, gl, gr, low_w, side_w):
    nf, rows, lanes = out.shape
    vspec = pl.BlockSpec(memory_space=pltpu.VMEM)
    anyspec = pl.BlockSpec(memory_space=pl.ANY)
    return pl.pallas_call(
        functools.partial(fix_kernel, low_w, side_w),
        out_shape=jax.ShapeDtypeStruct(out.shape, jnp.float32),
        in_specs=[anyspec, vspec, vspec, vspec, vspec],
        out_specs=anyspec,
        scratch_shapes=[
            pltpu.VMEM((2, nf, SUB, lanes), jnp.float32),
            pltpu.VMEM((2, nf, rows - 2 * SUB, LANE), jnp.float32),
            pltpu.SemaphoreType.DMA((4,)),
        ],
        input_output_aliases={0: 0},
    )(out, g0, g1, gl, gr)


def shards(
    fields, react_rate, mix_matrix, activation, inlet_ids, inlet_weights, outlet_ids, outlet_weights
):
    nf, rows, lanes = fields.shape
    n_grp = lax.axis_size("grp")
    n_blk = lax.axis_size("blk")
    g = lax.axis_index("grp")
    b = lax.axis_index("blk")
    exit_grp = n_grp - 2
    turb_grp = n_grp - 1
    flags = jnp.stack([g == exit_grp, g == turb_grp]).astype(jnp.float32)

    last_row = fields[:, -1, :]
    first_row = fields[:, 0, :]
    payload = jnp.concatenate([last_row, first_row[4:5]], axis=0)
    planes = payload[None]
    spans = []
    span = n_blk // 2
    edges = (last_row, first_row, fields[:, :, lanes - 1], fields[:, :, 0])
    while span >= 1:
        spans.append(span)
        if span == 1:
            edges, planes = lax.optimization_barrier((edges, planes))
        partner = [(i, i ^ span) for i in range(n_blk)]
        planes = jnp.concatenate([planes, lax.ppermute(planes, "blk", partner)], axis=0)
        span //= 2
    at_exit = g == exit_grp
    ids = jnp.where(at_exit, inlet_ids, outlet_ids)
    m = jnp.bitwise_xor(ids // lanes, b)
    slot = jnp.zeros_like(m)
    for r, span in enumerate(spans):
        slot = slot + ((m // span) % 2) * (1 << r)
    ids = slot * lanes + ids % lanes
    wt = jnp.transpose(jnp.where(at_exit, inlet_weights, outlet_weights))
    lft = lax.ppermute(edges[2], "blk", [(i, (i + 1) % n_blk) for i in range(n_blk)])
    rgt = lax.ppermute(edges[3], "blk", [((i + 1) % n_blk, i) for i in range(n_blk)])

    up, down, lft, rgt = interpolate(flags, ids, wt, planes, (edges[0], edges[1], lft, rgt))
    halo_lo = lax.ppermute(up, "grp", [(i, i + 1) for i in range(n_grp - 1)])
    halo_hi = lax.ppermute(down, "grp", [(i + 1, i) for i in range(n_grp - 1)])

    out, elo, ehi, clo, chi = fused_step(
        fields, react_rate, mix_matrix, activation, flags, halo_lo, halo_hi, lft, rgt
    )

    g0 = lax.ppermute(ehi, "grp", [(i, i + 1) for i in range(n_grp - 2)])
    g1 = lax.ppermute(elo, "grp", [(i + 1, i) for i in range(n_grp - 2)])
    gl = lax.ppermute(chi, "blk", [(i, (i + 1) % n_blk) for i in range(n_blk)])
    gr = lax.ppermute(clo, "blk", [((i + 1) % n_blk, i) for i in range(n_blk)])
    low_w = 0.5 * (courant + diffusion)
    side_w = 0.5 * diffusion
    return fix_edges(out, g0, g1, gl, gr, low_w, side_w)


def solution(mesh):
    in_specs = (
        P(None, "grp", "blk"),
        P("grp", "blk"),
        P(),
        P(),
        P(None, "blk"),
        P(None, "blk"),
        P(None, "blk"),
        P(None, "blk"),
    )
    out_specs = P(None, "grp", "blk")
    return jax.shard_map(shards, mesh=mesh, in_specs=in_specs, out_specs=out_specs, check_vma=False)
```

```python
import functools

import jax
import jax.numpy as jnp
from jax import lax
from jax.experimental import pallas as pl
from jax.experimental.pallas import tpu as pltpu
from jax.sharding import PartitionSpec as P

courant = 0.5
diffusion = 0.1
source_step = 0.5

SUB = 8
LANE = 128


def tile_t(row):
    n = row.shape[1]
    return jnp.transpose(jnp.broadcast_to(row, (n, n)))


def step_kernel(nf, rows, lanes, mix_s, act_s, flag_s, f_hbm, rate_ref, hlo_ref, hhi_ref,
                lft_ref, rgt_ref, out_hbm, elo_ref, ehi_ref, clo_ref, chi_ref, ext1, ext2, coef, obuf,
                sem):
    n_i = rows // SUB
    n_j = lanes // LANE
    top = SUB + rows
    right = LANE + lanes
    at_exit = flag_s[0] > 0.5
    at_turb = flag_s[1] > 0.5
    at_end = flag_s[0] + flag_s[1] > 0.5

    copy = pltpu.make_async_copy(f_hbm, ext1.at[:, SUB:top, LANE:right], sem.at[0])
    copy.start()
    zeros = jnp.zeros((rows, LANE), jnp.float32)
    for f in range(nf):
        low = hlo_ref[f:f + 1, :]
        ext1[f, SUB - 1:SUB, LANE:right] = low
        ext2[f, SUB - 1:SUB, LANE:right] = jnp.where(at_turb, low, 0.0)
        ext1[f, SUB:top, 0:LANE] = tile_t(lft_ref[f:f + 1, :])
        ext1[f, SUB:top, right:right + LANE] = tile_t(rgt_ref[f:f + 1, :])
        ext2[f, SUB:top, 0:LANE] = zeros
        ext2[f, SUB:top, right:right + LANE] = zeros
    for f in range(nf):
        for g in range(nf):
            coef[f * nf + g] = jnp.full((SUB, LANE), source_step * mix_s[f, g], jnp.float32)
        coef[nf * nf + f] = jnp.full((SUB, LANE), -act_s[f], jnp.float32)
    copy.wait()

    def high_ghost(ext, outside):
        for f in range(nf):
            own = ext[f, top - 1:top, LANE:right]
            halo = hhi_ref[f:f + 1, :]
            if f == 4:
                row = jnp.where(at_turb, own, jnp.where(at_exit | outside, halo, 0.0))
            else:
                row = jnp.where(at_end, own, jnp.where(outside, halo, 0.0))
            ext[f, top:top + 1, LANE:right] = row

    high_ghost(ext1, True)

    sub_id = lax.broadcasted_iota(jnp.int32, (SUB, LANE), 0)
    lane_id = lax.broadcasted_iota(jnp.int32, (SUB, LANE), 1)
    first_sub = sub_id == 0
    last_sub = sub_id == SUB - 1
    first_lane = lane_id == 0
    last_lane = lane_id == LANE - 1

    def tendency_tiles(src, r0, c0s, rate_ts):
        r = pl.multiple_of(r0 + SUB, SUB)
        r_up = pl.multiple_of(r0, SUB)
        r_dn = pl.multiple_of(r0 + 2 * SUB, SUB)
        cs = [pl.multiple_of(c0 + LANE, LANE) for c0 in c0s]
        reacts = []
        for c, rate_t in zip(cs, rate_ts):
            v4 = src[4, pl.ds(r, SUB), pl.ds(c, LANE)]
            heat = 1.0 + (jnp.maximum(v4, 0.0) + jnp.log1p(jnp.exp(-jnp.abs(v4))))
            inv_heat = 1.0 / heat
            reacts.append([
                rate_t * src[f, pl.ds(r, SUB), pl.ds(c, LANE)] * jnp.exp(coef[nf * nf + f] * inv_heat)
                for f in range(nf)
            ])
        tends = [[] for _ in cs]
        for f in range(nf):
            accs = [None] * len(cs)
            for g in range(nf):
                m = coef[f * nf + g]
                for h in range(len(cs)):
                    term = m * reacts[h][g]
                    accs[h] = term if accs[h] is None else accs[h] + term
            for h, c in enumerate(cs):
                c_w = pl.multiple_of(c - LANE, LANE)
                c_e = pl.multiple_of(c + LANE, LANE)
                v = src[f, pl.ds(r, SUB), pl.ds(c, LANE)]
                up = src[f, pl.ds(r_up, SUB), pl.ds(c, LANE)]
                down = src[f, pl.ds(r_dn, SUB), pl.ds(c, LANE)]
                west = src[f, pl.ds(r, SUB), pl.ds(c_w, LANE)]
                east = src[f, pl.ds(r, SUB), pl.ds(c_e, LANE)]
                backward = jnp.where(first_sub, pltpu.roll(up, 1, 0), pltpu.roll(v, 1, 0))
                forward = jnp.where(last_sub, pltpu.roll(down, SUB - 1, 0), pltpu.roll(v, SUB - 1, 0))
                left = jnp.where(first_lane, pltpu.roll(west, 1, 1), pltpu.roll(v, 1, 1))
                rgt = jnp.where(last_lane, pltpu.roll(east, LANE - 1, 1), pltpu.roll(v, LANE - 1, 1))
                flow = (courant + diffusion) * backward + diffusion * (forward + left + rgt)
                flow = flow - (courant + 4.0 * diffusion) * v
                tends[h].append((v, flow + accs[h]))
        return tends

    pair = 4 if n_j % 4 == 0 else (2 if n_j % 2 == 0 else 1)
    n_jp = n_j // pair

    def tile_offsets(t):
        i = t // n_jp
        jp = t % n_jp
        r0 = pl.multiple_of(i * SUB, SUB)
        c0s = [pl.multiple_of((jp * pair + h) * LANE, LANE) for h in range(pair)]
        return r0, c0s

    def stage_one(t, carry):
        r0, c0s = tile_offsets(t)
        rate_ts = [rate_ref[pl.ds(r0, SUB), pl.ds(c0, LANE)] for c0 in c0s]
        tends = tendency_tiles(ext1, r0, c0s, rate_ts)
        r = pl.multiple_of(r0 + SUB, SUB)
        for c0, tend in zip(c0s, tends):
            c = pl.multiple_of(c0 + LANE, LANE)
            for f in range(nf):
                v, tf = tend[f]
                ext2[f, pl.ds(r, SUB), pl.ds(c, LANE)] = v + tf
        return carry

    lax.fori_loop(0, n_i * n_jp, stage_one, 0)

    high_ghost(ext2, False)

    def stage_two(i, carry):
        for jp in range(n_jp):
            r0, c0s = tile_offsets(i * n_jp + jp)
            rate_ts = [rate_ref[pl.ds(r0, SUB), pl.ds(c0, LANE)] for c0 in c0s]
            tends = tendency_tiles(ext2, r0, c0s, rate_ts)
            r = pl.multiple_of(r0 + SUB, SUB)
            for c0, tend in zip(c0s, tends):
                c = pl.multiple_of(c0 + LANE, LANE)
                for f in range(nf):
                    v, tf = tend[f]
                    base = ext1[f, pl.ds(r, SUB), pl.ds(c, LANE)]
                    obuf[f, pl.ds(r0, SUB), pl.ds(c0, LANE)] = 0.5 * (base + v + tf)
        r0 = pl.multiple_of(i * SUB, SUB)
        pltpu.make_async_copy(
            obuf.at[:, pl.ds(r0, SUB), :], out_hbm.at[:, pl.ds(r0, SUB), :], sem.at[1]
        ).start()
        return carry

    lax.fori_loop(0, n_i, stage_two, 0)

    for f in range(nf):
        elo_ref[f:f + 1, :] = ext2[f, SUB:SUB + 1, LANE:right]
        ehi_ref[f:f + 1, :] = ext2[f, top - 1:top, LANE:right]
        west = jnp.transpose(ext2[f, SUB:top, LANE:2 * LANE])
        east = jnp.transpose(ext2[f, SUB:top, right - LANE:right])
        clo_ref[f:f + 1, :] = west[0:1, :]
        chi_ref[f:f + 1, :] = east[LANE - 1:LANE, :]
    pltpu.make_async_copy(obuf, out_hbm, sem.at[1]).wait()


def fused_step(fields, rate, mix, act, flags, halo_lo, halo_hi, lft, rgt):
    nf, rows, lanes = fields.shape
    vmem = pltpu.VMEM
    smem = pl.BlockSpec(memory_space=pltpu.SMEM)
    vspec = pl.BlockSpec(memory_space=vmem)
    cells = rows * lanes
    cost = pl.CostEstimate(
        flops=2 * cells * nf * (2 * nf + 24),
        transcendentals=2 * cells * (nf + 3),
        bytes_accessed=4 * cells * (2 * nf + 1),
    )
    return pl.pallas_call(
        functools.partial(step_kernel, nf, rows, lanes),
        out_shape=(
            jax.ShapeDtypeStruct((nf, rows, lanes), jnp.float32),
            jax.ShapeDtypeStruct((nf, lanes), jnp.float32),
            jax.ShapeDtypeStruct((nf, lanes), jnp.float32),
            jax.ShapeDtypeStruct((nf, rows), jnp.float32),
            jax.ShapeDtypeStruct((nf, rows), jnp.float32),
        ),
        in_specs=[smem, smem, smem, pl.BlockSpec(memory_space=pl.ANY)] + [vspec] * 5,
        out_specs=(pl.BlockSpec(memory_space=pl.ANY),) + (vspec,) * 4,
        scratch_shapes=[
            vmem((nf, rows + 2 * SUB, lanes + 2 * LANE), jnp.float32),
            vmem((nf, rows + 2 * SUB, lanes + 2 * LANE), jnp.float32),
            vmem((nf * nf + nf, SUB, LANE), jnp.float32),
            vmem((nf, rows, lanes), jnp.float32),
            pltpu.SemaphoreType.DMA((2,)),
        ],
        compiler_params=pltpu.CompilerParams(vmem_limit_bytes=60 * 1024 * 1024),
        cost_estimate=cost,
    )(mix, act, flags, fields, rate, halo_lo, halo_hi, lft, rgt)


def interp_kernel(ks, flag_s, ids_s, wt_ref, table_ref, *refs):
    n_in = (len(refs) - 2) // 2
    ins, outs, acc, picked = refs[:n_in], refs[n_in:2 * n_in], refs[-2], refs[-1]
    up_ref, down_ref = outs[0], outs[1]
    lanes = outs[0].shape[1]
    width = table_ref.shape[1]
    acc[...] = jnp.zeros(acc.shape, jnp.float32)

    @pl.when(flag_s[0] + flag_s[1] > 0.5)
    def _():
        def group(pg, carry):
            p0 = pl.multiple_of(pg * SUB, SUB)
            for s in range(SUB):
                for k in range(ks):
                    q = ids_s[k, p0 + s]
                    picked[k, pl.ds(p0 + s, 1), :] = table_ref[pl.ds(q, 1), :]
            return carry

        lax.fori_loop(0, lanes // SUB, group, 0)
        total = wt_ref[:, 0:1] * picked[0]
        for k in range(1, ks):
            total = total + wt_ref[:, k:k + 1] * picked[k]
        acc[:, 0:width] = total

    picked_t = jnp.transpose(acc[...])
    nf = up_ref.shape[0]
    last_ref, first_ref = ins[0], ins[1]
    up_ref[...] = jnp.where(flag_s[0] > 0.5, picked_t[0:nf, :], last_ref[...])
    down_ref[...] = jnp.where(
        flag_s[1] > 0.5, jnp.broadcast_to(picked_t[nf:nf + 1, :], (nf, lanes)), first_ref[...]
    )
    for src, dst in zip(ins[2:], outs[2:]):
        dst[...] = src[...]


def interpolate(flags, ids, wt, table, passed):
    ks, lanes = ids.shape
    smem = pl.BlockSpec(memory_space=pltpu.SMEM)
    vspec = pl.BlockSpec(memory_space=pltpu.VMEM)
    width = table.shape[1]
    return pl.pallas_call(
        functools.partial(interp_kernel, ks),
        out_shape=tuple(jax.ShapeDtypeStruct(x.shape, x.dtype) for x in passed),
        in_specs=[smem, smem] + [vspec] * (2 + len(passed)),
        out_specs=(vspec,) * len(passed),
        scratch_shapes=[
            pltpu.VMEM((lanes, LANE), jnp.float32),
            pltpu.VMEM((ks, lanes, width), jnp.float32),
        ],
    )(flags, ids, wt, table, *passed)


def fix_kernel(low_w, side_w, out_in, g0_ref, g1_ref, gl_ref, gr_ref, out_ref, rb, cb, sem):
    nf, rows, lanes = out_ref.shape
    mid = rows - 2 * SUB
    wins = [
        (out_ref.at[:, pl.ds(0, SUB), :], rb.at[0]),
        (out_ref.at[:, pl.ds(rows - SUB, SUB), :], rb.at[1]),
        (out_ref.at[:, pl.ds(SUB, mid), pl.ds(0, LANE)], cb.at[0]),
        (out_ref.at[:, pl.ds(SUB, mid), pl.ds(lanes - LANE, LANE)], cb.at[1]),
    ]
    loads = [pltpu.make_async_copy(hbm, buf, sem.at[s]) for s, (hbm, buf) in enumerate(wins)]
    for c in loads:
        c.start()
    for c in loads:
        c.wait()
    lane_id = lax.broadcasted_iota(jnp.int32, (rows, LANE), 1)
    row_lane = lax.broadcasted_iota(jnp.int32, (SUB, LANE), 1)
    for f in range(nf):
        west = jnp.where(lane_id == 0, side_w * tile_t(gl_ref[f:f + 1, :]), 0.0)
        east = jnp.where(lane_id == LANE - 1, side_w * tile_t(gr_ref[f:f + 1, :]), 0.0)
        cb[0, f] = cb[0, f] + west[SUB:rows - SUB]
        cb[1, f] = cb[1, f] + east[SUB:rows - SUB]
        for s, lo in ((0, 0), (1, rows - SUB)):
            rb[s, f, :, 0:LANE] = rb[s, f, :, 0:LANE] + west[lo:lo + SUB]
            rb[s, f, :, lanes - LANE:lanes] = rb[s, f, :, lanes - LANE:lanes] + east[lo:lo + SUB]
        rb[0, f, 0:1, :] = rb[0, f, 0:1, :] + low_w * g0_ref[f:f + 1, :]
        rb[1, f, SUB - 1:SUB, :] = rb[1, f, SUB - 1:SUB, :] + side_w * g1_ref[f:f + 1, :]
    stores = [pltpu.make_async_copy(buf, hbm, sem.at[s]) for s, (hbm, buf) in enumerate(wins)]
    for c in stores:
        c.start()
    for c in stores:
        c.wait()


def fix_edges(out, g0, g1, gl, gr, low_w, side_w):
    nf, rows, lanes = out.shape
    vspec = pl.BlockSpec(memory_space=pltpu.VMEM)
    anyspec = pl.BlockSpec(memory_space=pl.ANY)
    return pl.pallas_call(
        functools.partial(fix_kernel, low_w, side_w),
        out_shape=jax.ShapeDtypeStruct(out.shape, jnp.float32),
        in_specs=[anyspec, vspec, vspec, vspec, vspec],
        out_specs=anyspec,
        scratch_shapes=[
            pltpu.VMEM((2, nf, SUB, lanes), jnp.float32),
            pltpu.VMEM((2, nf, rows - 2 * SUB, LANE), jnp.float32),
            pltpu.SemaphoreType.DMA((4,)),
        ],
        input_output_aliases={0: 0},
    )(out, g0, g1, gl, gr)


def shards(
    fields, react_rate, mix_matrix, activation, inlet_ids, inlet_weights, outlet_ids, outlet_weights
):
    nf, rows, lanes = fields.shape
    n_grp = lax.axis_size("grp")
    n_blk = lax.axis_size("blk")
    g = lax.axis_index("grp")
    b = lax.axis_index("blk")
    exit_grp = n_grp - 2
    turb_grp = n_grp - 1
    flags = jnp.stack([g == exit_grp, g == turb_grp]).astype(jnp.float32)

    last_row = fields[:, -1, :]
    first_row = fields[:, 0, :]
    payload = jnp.concatenate([last_row, first_row[4:5]], axis=0)
    planes = payload[None]
    spans = []
    span = n_blk // 2
    edges = (last_row, first_row, fields[:, :, lanes - 1], fields[:, :, 0])
    while span >= 1:
        spans.append(span)
        if span == 1:
            edges, planes = lax.optimization_barrier((edges, planes))
        partner = [(i, i ^ span) for i in range(n_blk)]
        planes = jnp.concatenate([planes, lax.ppermute(planes, "blk", partner)], axis=0)
        span //= 2
    table = jnp.transpose(planes, (0, 2, 1)).reshape(n_blk * lanes, nf + 1)
    at_exit = g == exit_grp
    ids = jnp.where(at_exit, inlet_ids, outlet_ids)
    m = jnp.bitwise_xor(ids // lanes, b)
    slot = jnp.zeros_like(m)
    for r, span in enumerate(spans):
        slot = slot + ((m // span) % 2) * (1 << r)
    ids = slot * lanes + ids % lanes
    wt = jnp.transpose(jnp.where(at_exit, inlet_weights, outlet_weights))
    lft = lax.ppermute(edges[2], "blk", [(i, (i + 1) % n_blk) for i in range(n_blk)])
    rgt = lax.ppermute(edges[3], "blk", [((i + 1) % n_blk, i) for i in range(n_blk)])

    up, down, lft, rgt = interpolate(flags, ids, wt, table, (edges[0], edges[1], lft, rgt))
    halo_lo = lax.ppermute(up, "grp", [(i, i + 1) for i in range(n_grp - 1)])
    halo_hi = lax.ppermute(down, "grp", [(i + 1, i) for i in range(n_grp - 1)])

    out, elo, ehi, clo, chi = fused_step(
        fields, react_rate, mix_matrix, activation, flags, halo_lo, halo_hi, lft, rgt
    )

    g0 = lax.ppermute(ehi, "grp", [(i, i + 1) for i in range(n_grp - 2)])
    g1 = lax.ppermute(elo, "grp", [(i + 1, i) for i in range(n_grp - 2)])
    gl = lax.ppermute(chi, "blk", [(i, (i + 1) % n_blk) for i in range(n_blk)])
    gr = lax.ppermute(clo, "blk", [((i + 1) % n_blk, i) for i in range(n_blk)])
    low_w = 0.5 * (courant + diffusion)
    side_w = 0.5 * diffusion
    return fix_edges(out, g0, g1, gl, gr, low_w, side_w)


def solution(mesh):
    in_specs = (
        P(None, "grp", "blk"),
        P("grp", "blk"),
        P(),
        P(),
        P(None, "blk"),
        P(None, "blk"),
        P(None, "blk"),
        P(None, "blk"),
    )
    out_specs = P(None, "grp", "blk")
    return jax.shard_map(shards, mesh=mesh, in_specs=in_specs, out_specs=out_specs, check_vma=False)
```

```python
import functools

import jax
import jax.numpy as jnp
from jax import lax
from jax.experimental import pallas as pl
from jax.experimental.pallas import tpu as pltpu
from jax.sharding import PartitionSpec as P

courant = 0.5
diffusion = 0.1
source_step = 0.5

SUB = 8
LANE = 128


def tile_t(row):
    n = row.shape[1]
    return jnp.transpose(jnp.broadcast_to(row, (n, n)))


def step_kernel(nf, rows, lanes, mix_s, act_s, flag_s, f_hbm, rate_ref, hlo_ref, hhi_ref,
                lft_ref, rgt_ref, out_hbm, elo_ref, ehi_ref, clo_ref, chi_ref, ext1, ext2, coef, obuf,
                sem):
    n_i = rows // SUB
    n_j = lanes // LANE
    top = SUB + rows
    right = LANE + lanes
    at_exit = flag_s[0] > 0.5
    at_turb = flag_s[1] > 0.5
    at_end = flag_s[0] + flag_s[1] > 0.5

    copy = pltpu.make_async_copy(f_hbm, ext1.at[:, SUB:top, LANE:right], sem.at[0])
    copy.start()
    zeros = jnp.zeros((rows, LANE), jnp.float32)
    for f in range(nf):
        low = hlo_ref[f:f + 1, :]
        ext1[f, SUB - 1:SUB, LANE:right] = low
        ext2[f, SUB - 1:SUB, LANE:right] = jnp.where(at_turb, low, 0.0)
        ext1[f, SUB:top, 0:LANE] = tile_t(lft_ref[f:f + 1, :])
        ext1[f, SUB:top, right:right + LANE] = tile_t(rgt_ref[f:f + 1, :])
        ext2[f, SUB:top, 0:LANE] = zeros
        ext2[f, SUB:top, right:right + LANE] = zeros
    for f in range(nf):
        for g in range(nf):
            coef[f * nf + g] = jnp.full((SUB, LANE), source_step * mix_s[f, g], jnp.float32)
        coef[nf * nf + f] = jnp.full((SUB, LANE), -act_s[f], jnp.float32)
    copy.wait()

    def high_ghost(ext, outside):
        for f in range(nf):
            own = ext[f, top - 1:top, LANE:right]
            halo = hhi_ref[f:f + 1, :]
            if f == 4:
                row = jnp.where(at_turb, own, jnp.where(at_exit | outside, halo, 0.0))
            else:
                row = jnp.where(at_end, own, jnp.where(outside, halo, 0.0))
            ext[f, top:top + 1, LANE:right] = row

    high_ghost(ext1, True)

    sub_id = lax.broadcasted_iota(jnp.int32, (SUB, LANE), 0)
    lane_id = lax.broadcasted_iota(jnp.int32, (SUB, LANE), 1)
    first_sub = sub_id == 0
    last_sub = sub_id == SUB - 1
    first_lane = lane_id == 0
    last_lane = lane_id == LANE - 1

    def tendency_tiles(src, r0, c0s, rate_ts):
        r = pl.multiple_of(r0 + SUB, SUB)
        r_up = pl.multiple_of(r0, SUB)
        r_dn = pl.multiple_of(r0 + 2 * SUB, SUB)
        cs = [pl.multiple_of(c0 + LANE, LANE) for c0 in c0s]
        reacts = []
        for c, rate_t in zip(cs, rate_ts):
            v4 = src[4, pl.ds(r, SUB), pl.ds(c, LANE)]
            heat = 1.0 + (jnp.maximum(v4, 0.0) + jnp.log1p(jnp.exp(-jnp.abs(v4))))
            inv_heat = 1.0 / heat
            reacts.append([
                rate_t * src[f, pl.ds(r, SUB), pl.ds(c, LANE)] * jnp.exp(coef[nf * nf + f] * inv_heat)
                for f in range(nf)
            ])
        tends = [[] for _ in cs]
        for f in range(nf):
            accs = [None] * len(cs)
            for g in range(nf):
                m = coef[f * nf + g]
                for h in range(len(cs)):
                    term = m * reacts[h][g]
                    accs[h] = term if accs[h] is None else accs[h] + term
            for h, c in enumerate(cs):
                c_w = pl.multiple_of(c - LANE, LANE)
                c_e = pl.multiple_of(c + LANE, LANE)
                v = src[f, pl.ds(r, SUB), pl.ds(c, LANE)]
                up = src[f, pl.ds(r_up, SUB), pl.ds(c, LANE)]
                down = src[f, pl.ds(r_dn, SUB), pl.ds(c, LANE)]
                west = src[f, pl.ds(r, SUB), pl.ds(c_w, LANE)]
                east = src[f, pl.ds(r, SUB), pl.ds(c_e, LANE)]
                backward = jnp.where(first_sub, pltpu.roll(up, 1, 0), pltpu.roll(v, 1, 0))
                forward = jnp.where(last_sub, pltpu.roll(down, SUB - 1, 0), pltpu.roll(v, SUB - 1, 0))
                left = jnp.where(first_lane, pltpu.roll(west, 1, 1), pltpu.roll(v, 1, 1))
                rgt = jnp.where(last_lane, pltpu.roll(east, LANE - 1, 1), pltpu.roll(v, LANE - 1, 1))
                flow = (courant + diffusion) * backward + diffusion * (forward + left + rgt)
                flow = flow - (courant + 4.0 * diffusion) * v
                tends[h].append((v, flow + accs[h]))
        return tends

    pair = 4 if n_j % 4 == 0 else (2 if n_j % 2 == 0 else 1)
    n_jp = n_j // pair

    def tile_offsets(t):
        i = t // n_jp
        jp = t % n_jp
        r0 = pl.multiple_of(i * SUB, SUB)
        c0s = [pl.multiple_of((jp * pair + h) * LANE, LANE) for h in range(pair)]
        return r0, c0s

    def stage_one(t, carry):
        r0, c0s = tile_offsets(t)
        rate_ts = [rate_ref[pl.ds(r0, SUB), pl.ds(c0, LANE)] for c0 in c0s]
        tends = tendency_tiles(ext1, r0, c0s, rate_ts)
        r = pl.multiple_of(r0 + SUB, SUB)
        for c0, tend in zip(c0s, tends):
            c = pl.multiple_of(c0 + LANE, LANE)
            for f in range(nf):
                v, tf = tend[f]
                ext2[f, pl.ds(r, SUB), pl.ds(c, LANE)] = v + tf
        return carry

    lax.fori_loop(0, n_i * n_jp, stage_one, 0)

    high_ghost(ext2, False)

    def stage_two(i, carry):
        for jp in range(n_jp):
            r0, c0s = tile_offsets(i * n_jp + jp)
            rate_ts = [rate_ref[pl.ds(r0, SUB), pl.ds(c0, LANE)] for c0 in c0s]
            tends = tendency_tiles(ext2, r0, c0s, rate_ts)
            r = pl.multiple_of(r0 + SUB, SUB)
            for c0, tend in zip(c0s, tends):
                c = pl.multiple_of(c0 + LANE, LANE)
                for f in range(nf):
                    v, tf = tend[f]
                    base = ext1[f, pl.ds(r, SUB), pl.ds(c, LANE)]
                    obuf[f, pl.ds(r0, SUB), pl.ds(c0, LANE)] = 0.5 * (base + v + tf)
        r0 = pl.multiple_of(i * SUB, SUB)
        pltpu.make_async_copy(
            obuf.at[:, pl.ds(r0, SUB), :], out_hbm.at[:, pl.ds(r0, SUB), :], sem.at[1]
        ).start()
        return carry

    lax.fori_loop(0, n_i, stage_two, 0)

    for f in range(nf):
        elo_ref[f:f + 1, :] = ext2[f, SUB:SUB + 1, LANE:right]
        ehi_ref[f:f + 1, :] = ext2[f, top - 1:top, LANE:right]
        west = jnp.transpose(ext2[f, SUB:top, LANE:2 * LANE])
        east = jnp.transpose(ext2[f, SUB:top, right - LANE:right])
        clo_ref[f:f + 1, :] = west[0:1, :]
        chi_ref[f:f + 1, :] = east[LANE - 1:LANE, :]
    pltpu.make_async_copy(obuf, out_hbm, sem.at[1]).wait()


def fused_step(fields, rate, mix, act, flags, halo_lo, halo_hi, lft, rgt):
    nf, rows, lanes = fields.shape
    vmem = pltpu.VMEM
    smem = pl.BlockSpec(memory_space=pltpu.SMEM)
    vspec = pl.BlockSpec(memory_space=vmem)
    cells = rows * lanes
    cost = pl.CostEstimate(
        flops=2 * cells * nf * (2 * nf + 24),
        transcendentals=2 * cells * (nf + 3),
        bytes_accessed=4 * cells * (2 * nf + 1),
    )
    return pl.pallas_call(
        functools.partial(step_kernel, nf, rows, lanes),
        out_shape=(
            jax.ShapeDtypeStruct((nf, rows, lanes), jnp.float32),
            jax.ShapeDtypeStruct((nf, lanes), jnp.float32),
            jax.ShapeDtypeStruct((nf, lanes), jnp.float32),
            jax.ShapeDtypeStruct((nf, rows), jnp.float32),
            jax.ShapeDtypeStruct((nf, rows), jnp.float32),
        ),
        in_specs=[smem, smem, smem, pl.BlockSpec(memory_space=pl.ANY)] + [vspec] * 5,
        out_specs=(pl.BlockSpec(memory_space=pl.ANY),) + (vspec,) * 4,
        scratch_shapes=[
            vmem((nf, rows + 2 * SUB, lanes + 2 * LANE), jnp.float32),
            vmem((nf, rows + 2 * SUB, lanes + 2 * LANE), jnp.float32),
            vmem((nf * nf + nf, SUB, LANE), jnp.float32),
            vmem((nf, rows, lanes), jnp.float32),
            pltpu.SemaphoreType.DMA((2,)),
        ],
        compiler_params=pltpu.CompilerParams(vmem_limit_bytes=60 * 1024 * 1024),
        cost_estimate=cost,
    )(mix, act, flags, fields, rate, halo_lo, halo_hi, lft, rgt)


def interp_kernel(ks, flag_s, ids_s, wt_ref, table_ref, *refs):
    n_in = (len(refs) - 2) // 2
    ins, outs, acc, picked = refs[:n_in], refs[n_in:2 * n_in], refs[-2], refs[-1]
    up_ref, down_ref = outs[0], outs[1]
    lanes = outs[0].shape[1]
    width = table_ref.shape[1]
    acc[...] = jnp.zeros(acc.shape, jnp.float32)

    @pl.when(flag_s[0] + flag_s[1] > 0.5)
    def _():
        def group(pg, carry):
            p0 = pl.multiple_of(pg * SUB, SUB)
            for s in range(SUB):
                for k in range(ks):
                    q = ids_s[k, p0 + s]
                    picked[k, pl.ds(p0 + s, 1), :] = table_ref[pl.ds(q, 1), :]
            return carry

        lax.fori_loop(0, lanes // SUB, group, 0)
        total = wt_ref[:, 0:1] * picked[0]
        for k in range(1, ks):
            total = total + wt_ref[:, k:k + 1] * picked[k]
        acc[:, 0:width] = total

    picked_t = jnp.transpose(acc[...])
    nf = up_ref.shape[0]
    last_ref, first_ref = ins[0], ins[1]
    up_ref[...] = jnp.where(flag_s[0] > 0.5, picked_t[0:nf, :], last_ref[...])
    down_ref[...] = jnp.where(
        flag_s[1] > 0.5, jnp.broadcast_to(picked_t[nf:nf + 1, :], (nf, lanes)), first_ref[...]
    )
    for src, dst in zip(ins[2:], outs[2:]):
        dst[...] = src[...]


def interpolate(flags, ids, wt, table, passed):
    ks, lanes = ids.shape
    smem = pl.BlockSpec(memory_space=pltpu.SMEM)
    vspec = pl.BlockSpec(memory_space=pltpu.VMEM)
    width = table.shape[1]
    return pl.pallas_call(
        functools.partial(interp_kernel, ks),
        out_shape=tuple(jax.ShapeDtypeStruct(x.shape, x.dtype) for x in passed),
        in_specs=[smem, smem] + [vspec] * (2 + len(passed)),
        out_specs=(vspec,) * len(passed),
        scratch_shapes=[
            pltpu.VMEM((lanes, LANE), jnp.float32),
            pltpu.VMEM((ks, lanes, width), jnp.float32),
        ],
    )(flags, ids, wt, table, *passed)


def fix_kernel(low_w, side_w, out_in, g0_ref, g1_ref, gl_ref, gr_ref, out_ref, rb, cb, sem):
    nf, rows, lanes = out_ref.shape
    mid = rows - 2 * SUB
    wins = [
        (out_ref.at[:, pl.ds(0, SUB), :], rb.at[0]),
        (out_ref.at[:, pl.ds(rows - SUB, SUB), :], rb.at[1]),
        (out_ref.at[:, pl.ds(SUB, mid), pl.ds(0, LANE)], cb.at[0]),
        (out_ref.at[:, pl.ds(SUB, mid), pl.ds(lanes - LANE, LANE)], cb.at[1]),
    ]
    loads = [pltpu.make_async_copy(hbm, buf, sem.at[s]) for s, (hbm, buf) in enumerate(wins)]
    for c in loads:
        c.start()
    for c in loads:
        c.wait()
    lane_id = lax.broadcasted_iota(jnp.int32, (rows, LANE), 1)
    row_lane = lax.broadcasted_iota(jnp.int32, (SUB, LANE), 1)
    for f in range(nf):
        west = jnp.where(lane_id == 0, side_w * tile_t(gl_ref[f:f + 1, :]), 0.0)
        east = jnp.where(lane_id == LANE - 1, side_w * tile_t(gr_ref[f:f + 1, :]), 0.0)
        cb[0, f] = cb[0, f] + west[SUB:rows - SUB]
        cb[1, f] = cb[1, f] + east[SUB:rows - SUB]
        for s, lo in ((0, 0), (1, rows - SUB)):
            rb[s, f, :, 0:LANE] = rb[s, f, :, 0:LANE] + west[lo:lo + SUB]
            rb[s, f, :, lanes - LANE:lanes] = rb[s, f, :, lanes - LANE:lanes] + east[lo:lo + SUB]
        rb[0, f, 0:1, :] = rb[0, f, 0:1, :] + low_w * g0_ref[f:f + 1, :]
        rb[1, f, SUB - 1:SUB, :] = rb[1, f, SUB - 1:SUB, :] + side_w * g1_ref[f:f + 1, :]
    stores = [pltpu.make_async_copy(buf, hbm, sem.at[s]) for s, (hbm, buf) in enumerate(wins)]
    for c in stores:
        c.start()
    for c in stores:
        c.wait()


def fix_edges(out, g0, g1, gl, gr, low_w, side_w):
    nf, rows, lanes = out.shape
    vspec = pl.BlockSpec(memory_space=pltpu.VMEM)
    anyspec = pl.BlockSpec(memory_space=pl.ANY)
    return pl.pallas_call(
        functools.partial(fix_kernel, low_w, side_w),
        out_shape=jax.ShapeDtypeStruct(out.shape, jnp.float32),
        in_specs=[anyspec, vspec, vspec, vspec, vspec],
        out_specs=anyspec,
        scratch_shapes=[
            pltpu.VMEM((2, nf, SUB, lanes), jnp.float32),
            pltpu.VMEM((2, nf, rows - 2 * SUB, LANE), jnp.float32),
            pltpu.SemaphoreType.DMA((4,)),
        ],
        input_output_aliases={0: 0},
    )(out, g0, g1, gl, gr)


def shards(
    fields, react_rate, mix_matrix, activation, inlet_ids, inlet_weights, outlet_ids, outlet_weights
):
    nf, rows, lanes = fields.shape
    n_grp = lax.axis_size("grp")
    n_blk = lax.axis_size("blk")
    g = lax.axis_index("grp")
    b = lax.axis_index("blk")
    exit_grp = n_grp - 2
    turb_grp = n_grp - 1
    flags = jnp.stack([g == exit_grp, g == turb_grp]).astype(jnp.float32)

    last_row = fields[:, -1, :]
    first_row = fields[:, 0, :]
    payload = jnp.concatenate([last_row, first_row[4:5]], axis=0)
    planes = payload[None]
    spans = []
    span = n_blk // 2
    even = b % 2 == 0
    edges = (last_row, first_row, fields[:, :, lanes - 1], fields[:, :, 0])
    while span >= 1:
        spans.append(span)
        partner = [(i, i ^ span) for i in range(n_blk)]
        if span == 1:
            edges, planes = lax.optimization_barrier((edges, planes))
            side = jnp.where(even, edges[2], edges[3])
            side = jnp.pad(side, ((0, 1), (0, lanes - side.shape[1])))[None]
            got = lax.ppermute(jnp.concatenate([planes, side], axis=0), "blk", partner)
            side_got = got[-1, :nf, :edges[2].shape[1]]
            planes = jnp.concatenate([planes, got[:-1]], axis=0)
        else:
            planes = jnp.concatenate([planes, lax.ppermute(planes, "blk", partner)], axis=0)
        span //= 2
    table = jnp.transpose(planes, (0, 2, 1)).reshape(n_blk * lanes, nf + 1)
    at_exit = g == exit_grp
    ids = jnp.where(at_exit, inlet_ids, outlet_ids)
    m = jnp.bitwise_xor(ids // lanes, b)
    slot = jnp.zeros_like(m)
    for r, span in enumerate(spans):
        slot = slot + ((m // span) % 2) * (1 << r)
    ids = slot * lanes + ids % lanes
    wt = jnp.transpose(jnp.where(at_exit, inlet_weights, outlet_weights))
    other = lax.ppermute(
        jnp.where(even, edges[3], edges[2]),
        "blk",
        [(i, (i + 1) % n_blk if i % 2 else (i - 1) % n_blk) for i in range(n_blk)],
    )
    lft = jnp.where(even, other, side_got)
    rgt = jnp.where(even, side_got, other)

    up, down, lft, rgt = interpolate(flags, ids, wt, table, (edges[0], edges[1], lft, rgt))
    halo_lo = lax.ppermute(up, "grp", [(i, i + 1) for i in range(n_grp - 1)])
    halo_hi = lax.ppermute(down, "grp", [(i + 1, i) for i in range(n_grp - 1)])

    out, elo, ehi, clo, chi = fused_step(
        fields, react_rate, mix_matrix, activation, flags, halo_lo, halo_hi, lft, rgt
    )

    g0 = lax.ppermute(ehi, "grp", [(i, i + 1) for i in range(n_grp - 2)])
    g1 = lax.ppermute(elo, "grp", [(i + 1, i) for i in range(n_grp - 2)])
    gl = lax.ppermute(chi, "blk", [(i, (i + 1) % n_blk) for i in range(n_blk)])
    gr = lax.ppermute(clo, "blk", [((i + 1) % n_blk, i) for i in range(n_blk)])
    low_w = 0.5 * (courant + diffusion)
    side_w = 0.5 * diffusion
    return fix_edges(out, g0, g1, gl, gr, low_w, side_w)


def solution(mesh):
    in_specs = (
        P(None, "grp", "blk"),
        P("grp", "blk"),
        P(),
        P(),
        P(None, "blk"),
        P(None, "blk"),
        P(None, "blk"),
        P(None, "blk"),
    )
    out_specs = P(None, "grp", "blk")
    return jax.shard_map(shards, mesh=mesh, in_specs=in_specs, out_specs=out_specs, check_vma=False)
```

```python
import functools

import jax
import jax.numpy as jnp
from jax import lax
from jax.experimental import pallas as pl
from jax.experimental.pallas import tpu as pltpu
from jax.sharding import PartitionSpec as P

courant = 0.5
diffusion = 0.1
source_step = 0.5

SUB = 8
LANE = 128


def tile_t(row):
    n = row.shape[1]
    return jnp.transpose(jnp.broadcast_to(row, (n, n)))


def step_kernel(nf, rows, lanes, mix_s, act_s, flag_s, f_hbm, rate_ref, hlo_ref, hhi_ref,
                lft_ref, rgt_ref, out_hbm, elo_ref, ehi_ref, clo_ref, chi_ref, ext1, ext2, coef, obuf,
                sem):
    n_i = rows // SUB
    n_j = lanes // LANE
    top = SUB + rows
    right = LANE + lanes
    at_exit = flag_s[0] > 0.5
    at_turb = flag_s[1] > 0.5
    at_end = flag_s[0] + flag_s[1] > 0.5

    copy = pltpu.make_async_copy(f_hbm, ext1.at[:, SUB:top, LANE:right], sem.at[0])
    copy.start()
    zeros = jnp.zeros((rows, LANE), jnp.float32)
    for f in range(nf):
        low = hlo_ref[f:f + 1, :]
        ext1[f, SUB - 1:SUB, LANE:right] = low
        ext2[f, SUB - 1:SUB, LANE:right] = jnp.where(at_turb, low, 0.0)
        ext1[f, SUB:top, 0:LANE] = tile_t(lft_ref[f:f + 1, :])
        ext1[f, SUB:top, right:right + LANE] = tile_t(rgt_ref[f:f + 1, :])
        ext2[f, SUB:top, 0:LANE] = zeros
        ext2[f, SUB:top, right:right + LANE] = zeros
    for f in range(nf):
        for g in range(nf):
            coef[f * nf + g] = jnp.full((SUB, LANE), source_step * mix_s[f, g], jnp.float32)
        coef[nf * nf + f] = jnp.full((SUB, LANE), -act_s[f], jnp.float32)
    copy.wait()

    def high_ghost(ext, outside):
        for f in range(nf):
            own = ext[f, top - 1:top, LANE:right]
            halo = hhi_ref[f:f + 1, :]
            if f == 4:
                row = jnp.where(at_turb, own, jnp.where(at_exit | outside, halo, 0.0))
            else:
                row = jnp.where(at_end, own, jnp.where(outside, halo, 0.0))
            ext[f, top:top + 1, LANE:right] = row

    high_ghost(ext1, True)

    sub_id = lax.broadcasted_iota(jnp.int32, (SUB, LANE), 0)
    lane_id = lax.broadcasted_iota(jnp.int32, (SUB, LANE), 1)
    first_sub = sub_id == 0
    last_sub = sub_id == SUB - 1
    first_lane = lane_id == 0
    last_lane = lane_id == LANE - 1

    def tendency_tiles(src, r0, c0s, rate_ts):
        r = pl.multiple_of(r0 + SUB, SUB)
        r_up = pl.multiple_of(r0, SUB)
        r_dn = pl.multiple_of(r0 + 2 * SUB, SUB)
        cs = [pl.multiple_of(c0 + LANE, LANE) for c0 in c0s]
        reacts = []
        for c, rate_t in zip(cs, rate_ts):
            v4 = src[4, pl.ds(r, SUB), pl.ds(c, LANE)]
            heat = 1.0 + (jnp.maximum(v4, 0.0) + jnp.log1p(jnp.exp(-jnp.abs(v4))))
            inv_heat = 1.0 / heat
            reacts.append([
                rate_t * src[f, pl.ds(r, SUB), pl.ds(c, LANE)] * jnp.exp(coef[nf * nf + f] * inv_heat)
                for f in range(nf)
            ])
        tends = [[] for _ in cs]
        for f in range(nf):
            accs = [None] * len(cs)
            for g in range(nf):
                m = coef[f * nf + g]
                for h in range(len(cs)):
                    term = m * reacts[h][g]
                    accs[h] = term if accs[h] is None else accs[h] + term
            for h, c in enumerate(cs):
                c_w = pl.multiple_of(c - LANE, LANE)
                c_e = pl.multiple_of(c + LANE, LANE)
                v = src[f, pl.ds(r, SUB), pl.ds(c, LANE)]
                up = src[f, pl.ds(r_up, SUB), pl.ds(c, LANE)]
                down = src[f, pl.ds(r_dn, SUB), pl.ds(c, LANE)]
                west = src[f, pl.ds(r, SUB), pl.ds(c_w, LANE)]
                east = src[f, pl.ds(r, SUB), pl.ds(c_e, LANE)]
                backward = jnp.where(first_sub, pltpu.roll(up, 1, 0), pltpu.roll(v, 1, 0))
                forward = jnp.where(last_sub, pltpu.roll(down, SUB - 1, 0), pltpu.roll(v, SUB - 1, 0))
                left = jnp.where(first_lane, pltpu.roll(west, 1, 1), pltpu.roll(v, 1, 1))
                rgt = jnp.where(last_lane, pltpu.roll(east, LANE - 1, 1), pltpu.roll(v, LANE - 1, 1))
                flow = (courant + diffusion) * backward + diffusion * (forward + left + rgt)
                flow = flow - (courant + 4.0 * diffusion) * v
                tends[h].append((v, flow + accs[h]))
        return tends

    pair = 4 if n_j % 4 == 0 else (2 if n_j % 2 == 0 else 1)
    n_jp = n_j // pair

    def tile_offsets(t):
        i = t // n_jp
        jp = t % n_jp
        r0 = pl.multiple_of(i * SUB, SUB)
        c0s = [pl.multiple_of((jp * pair + h) * LANE, LANE) for h in range(pair)]
        return r0, c0s

    def stage_one(t, carry):
        r0, c0s = tile_offsets(t)
        rate_ts = [rate_ref[pl.ds(r0, SUB), pl.ds(c0, LANE)] for c0 in c0s]
        tends = tendency_tiles(ext1, r0, c0s, rate_ts)
        r = pl.multiple_of(r0 + SUB, SUB)
        for c0, tend in zip(c0s, tends):
            c = pl.multiple_of(c0 + LANE, LANE)
            for f in range(nf):
                v, tf = tend[f]
                ext2[f, pl.ds(r, SUB), pl.ds(c, LANE)] = v + tf
        return carry

    lax.fori_loop(0, n_i * n_jp, stage_one, 0)

    high_ghost(ext2, False)

    def stage_two(i, carry):
        for jp in range(n_jp):
            r0, c0s = tile_offsets(i * n_jp + jp)
            rate_ts = [rate_ref[pl.ds(r0, SUB), pl.ds(c0, LANE)] for c0 in c0s]
            tends = tendency_tiles(ext2, r0, c0s, rate_ts)
            r = pl.multiple_of(r0 + SUB, SUB)
            for c0, tend in zip(c0s, tends):
                c = pl.multiple_of(c0 + LANE, LANE)
                for f in range(nf):
                    v, tf = tend[f]
                    base = ext1[f, pl.ds(r, SUB), pl.ds(c, LANE)]
                    obuf[f, pl.ds(r0, SUB), pl.ds(c0, LANE)] = 0.5 * (base + v + tf)
        r0 = pl.multiple_of(i * SUB, SUB)
        pltpu.make_async_copy(
            obuf.at[:, pl.ds(r0, SUB), :], out_hbm.at[:, pl.ds(r0, SUB), :], sem.at[1]
        ).start()
        return carry

    lax.fori_loop(0, n_i, stage_two, 0)

    for f in range(nf):
        elo_ref[f:f + 1, :] = ext2[f, SUB:SUB + 1, LANE:right]
        ehi_ref[f:f + 1, :] = ext2[f, top - 1:top, LANE:right]
        west = jnp.transpose(ext2[f, SUB:top, LANE:2 * LANE])
        east = jnp.transpose(ext2[f, SUB:top, right - LANE:right])
        clo_ref[f:f + 1, :] = west[0:1, :]
        chi_ref[f:f + 1, :] = east[LANE - 1:LANE, :]
    pltpu.make_async_copy(obuf, out_hbm, sem.at[1]).wait()


def fused_step(fields, rate, mix, act, flags, halo_lo, halo_hi, lft, rgt):
    nf, rows, lanes = fields.shape
    vmem = pltpu.VMEM
    smem = pl.BlockSpec(memory_space=pltpu.SMEM)
    vspec = pl.BlockSpec(memory_space=vmem)
    cells = rows * lanes
    cost = pl.CostEstimate(
        flops=2 * cells * nf * (2 * nf + 24),
        transcendentals=2 * cells * (nf + 3),
        bytes_accessed=4 * cells * (2 * nf + 1),
    )
    return pl.pallas_call(
        functools.partial(step_kernel, nf, rows, lanes),
        out_shape=(
            jax.ShapeDtypeStruct((nf, rows, lanes), jnp.float32),
            jax.ShapeDtypeStruct((nf, lanes), jnp.float32),
            jax.ShapeDtypeStruct((nf, lanes), jnp.float32),
            jax.ShapeDtypeStruct((nf, rows), jnp.float32),
            jax.ShapeDtypeStruct((nf, rows), jnp.float32),
        ),
        in_specs=[smem, smem, smem, pl.BlockSpec(memory_space=pl.ANY)] + [vspec] * 5,
        out_specs=(pl.BlockSpec(memory_space=pl.ANY),) + (vspec,) * 4,
        scratch_shapes=[
            vmem((nf, rows + 2 * SUB, lanes + 2 * LANE), jnp.float32),
            vmem((nf, rows + 2 * SUB, lanes + 2 * LANE), jnp.float32),
            vmem((nf * nf + nf, SUB, LANE), jnp.float32),
            vmem((nf, rows, lanes), jnp.float32),
            pltpu.SemaphoreType.DMA((2,)),
        ],
        compiler_params=pltpu.CompilerParams(vmem_limit_bytes=60 * 1024 * 1024),
        cost_estimate=cost,
    )(mix, act, flags, fields, rate, halo_lo, halo_hi, lft, rgt)


def interp_kernel(ks, flag_s, ids_s, wt_ref, table_ref, *refs):
    n_in = (len(refs) - 2) // 2
    ins, outs, acc, picked = refs[:n_in], refs[n_in:2 * n_in], refs[-2], refs[-1]
    up_ref, down_ref = outs[0], outs[1]
    lanes = outs[0].shape[1]
    width = table_ref.shape[1]
    acc[...] = jnp.zeros(acc.shape, jnp.float32)

    @pl.when(flag_s[0] + flag_s[1] > 0.5)
    def _():
        def group(pg, carry):
            p0 = pl.multiple_of(pg * SUB, SUB)
            for s in range(SUB):
                for k in range(ks):
                    q = ids_s[k, p0 + s]
                    picked[k, pl.ds(p0 + s, 1), :] = table_ref[pl.ds(q, 1), :]
            return carry

        lax.fori_loop(0, lanes // SUB, group, 0)
        total = wt_ref[:, 0:1] * picked[0]
        for k in range(1, ks):
            total = total + wt_ref[:, k:k + 1] * picked[k]
        acc[:, 0:width] = total

    picked_t = jnp.transpose(acc[...])
    nf = up_ref.shape[0]
    last_ref, first_ref = ins[0], ins[1]
    up_ref[...] = jnp.where(flag_s[0] > 0.5, picked_t[0:nf, :], last_ref[...])
    down_ref[...] = jnp.where(
        flag_s[1] > 0.5, jnp.broadcast_to(picked_t[nf:nf + 1, :], (nf, lanes)), first_ref[...]
    )
    for src, dst in zip(ins[2:], outs[2:]):
        dst[...] = src[...]


def interpolate(flags, ids, wt, table, passed):
    ks, lanes = ids.shape
    smem = pl.BlockSpec(memory_space=pltpu.SMEM)
    vspec = pl.BlockSpec(memory_space=pltpu.VMEM)
    width = table.shape[1]
    return pl.pallas_call(
        functools.partial(interp_kernel, ks),
        out_shape=tuple(jax.ShapeDtypeStruct(x.shape, x.dtype) for x in passed),
        in_specs=[smem, smem] + [vspec] * (2 + len(passed)),
        out_specs=(vspec,) * len(passed),
        scratch_shapes=[
            pltpu.VMEM((lanes, LANE), jnp.float32),
            pltpu.VMEM((ks, lanes, width), jnp.float32),
        ],
    )(flags, ids, wt, table, *passed)


def fix_kernel(low_w, side_w, out_in, g0_ref, g1_ref, gl_ref, gr_ref, out_ref, rb, cb, sem):
    nf, rows, lanes = out_ref.shape
    mid = rows - 2 * SUB
    wins = [
        (out_ref.at[:, pl.ds(0, SUB), :], rb.at[0]),
        (out_ref.at[:, pl.ds(rows - SUB, SUB), :], rb.at[1]),
        (out_ref.at[:, pl.ds(SUB, mid), pl.ds(0, LANE)], cb.at[0]),
        (out_ref.at[:, pl.ds(SUB, mid), pl.ds(lanes - LANE, LANE)], cb.at[1]),
    ]
    loads = [pltpu.make_async_copy(hbm, buf, sem.at[s]) for s, (hbm, buf) in enumerate(wins)]
    for c in loads:
        c.start()
    for c in loads:
        c.wait()
    lane_id = lax.broadcasted_iota(jnp.int32, (rows, LANE), 1)
    row_lane = lax.broadcasted_iota(jnp.int32, (SUB, LANE), 1)
    for f in range(nf):
        west = jnp.where(lane_id == 0, side_w * tile_t(gl_ref[f:f + 1, :]), 0.0)
        east = jnp.where(lane_id == LANE - 1, side_w * tile_t(gr_ref[f:f + 1, :]), 0.0)
        cb[0, f] = cb[0, f] + west[SUB:rows - SUB]
        cb[1, f] = cb[1, f] + east[SUB:rows - SUB]
        for s, lo in ((0, 0), (1, rows - SUB)):
            rb[s, f, :, 0:LANE] = rb[s, f, :, 0:LANE] + west[lo:lo + SUB]
            rb[s, f, :, lanes - LANE:lanes] = rb[s, f, :, lanes - LANE:lanes] + east[lo:lo + SUB]
        rb[0, f, 0:1, :] = rb[0, f, 0:1, :] + low_w * g0_ref[f:f + 1, :]
        rb[1, f, SUB - 1:SUB, :] = rb[1, f, SUB - 1:SUB, :] + side_w * g1_ref[f:f + 1, :]
    stores = [pltpu.make_async_copy(buf, hbm, sem.at[s]) for s, (hbm, buf) in enumerate(wins)]
    for c in stores:
        c.start()
    for c in stores:
        c.wait()


def fix_edges(out, g0, g1, gl, gr, low_w, side_w):
    nf, rows, lanes = out.shape
    vspec = pl.BlockSpec(memory_space=pltpu.VMEM)
    anyspec = pl.BlockSpec(memory_space=pl.ANY)
    return pl.pallas_call(
        functools.partial(fix_kernel, low_w, side_w),
        out_shape=jax.ShapeDtypeStruct(out.shape, jnp.float32),
        in_specs=[anyspec, vspec, vspec, vspec, vspec],
        out_specs=anyspec,
        scratch_shapes=[
            pltpu.VMEM((2, nf, SUB, lanes), jnp.float32),
            pltpu.VMEM((2, nf, rows - 2 * SUB, LANE), jnp.float32),
            pltpu.SemaphoreType.DMA((4,)),
        ],
        input_output_aliases={0: 0},
    )(out, g0, g1, gl, gr)


def shards(
    fields, react_rate, mix_matrix, activation, inlet_ids, inlet_weights, outlet_ids, outlet_weights
):
    nf, rows, lanes = fields.shape
    n_grp = lax.axis_size("grp")
    n_blk = lax.axis_size("blk")
    g = lax.axis_index("grp")
    b = lax.axis_index("blk")
    exit_grp = n_grp - 2
    turb_grp = n_grp - 1
    flags = jnp.stack([g == exit_grp, g == turb_grp]).astype(jnp.float32)

    last_row = fields[:, -1, :]
    first_row = fields[:, 0, :]
    payload = jnp.concatenate([last_row, first_row[4:5]], axis=0)
    planes = payload[None]
    spans = []
    span = n_blk // 2
    even = b % 2 == 0
    edges = (last_row, first_row, fields[:, :, lanes - 1], fields[:, :, 0])
    while span >= 1:
        spans.append(span)
        partner = [(i, i ^ span) for i in range(n_blk)]
        if span == 1:
            edges, planes = lax.optimization_barrier((edges, planes))
            side = jnp.where(even, edges[2], edges[3])
            side = jnp.pad(side, ((0, 1), (0, lanes - side.shape[1])))[None]
            got = lax.ppermute(jnp.concatenate([planes, side], axis=0), "blk", partner)
            side_got = got[-1, :nf, :edges[2].shape[1]]
            planes = jnp.concatenate([planes, got[:-1]], axis=0)
        else:
            planes = jnp.concatenate([planes, lax.ppermute(planes, "blk", partner)], axis=0)
        span //= 2
    table = jnp.transpose(planes, (0, 2, 1)).reshape(n_blk * lanes, nf + 1)
    at_exit = g == exit_grp
    ids = jnp.where(at_exit, inlet_ids, outlet_ids)
    m = jnp.bitwise_xor(ids // lanes, b)
    slot = jnp.zeros_like(m)
    for r, span in enumerate(spans):
        slot = slot + ((m // span) % 2) * (1 << r)
    ids = slot * lanes + ids % lanes
    wt = jnp.transpose(jnp.where(at_exit, inlet_weights, outlet_weights))
    other = lax.ppermute(
        jnp.where(even, edges[3], edges[2]),
        "blk",
        [(i, (i + 1) % n_blk if i % 2 else (i - 1) % n_blk) for i in range(n_blk)],
    )
    lft = jnp.where(even, other, side_got)
    rgt = jnp.where(even, side_got, other)

    up, down, lft, rgt = interpolate(flags, ids, wt, table, (edges[0], edges[1], lft, rgt))
    halo_lo = lax.ppermute(up, "grp", [(i, i + 1) for i in range(n_grp - 1)])
    halo_hi = lax.ppermute(down, "grp", [(i + 1, i) for i in range(n_grp - 1)])

    out, elo, ehi, clo, chi = fused_step(
        fields, react_rate, mix_matrix, activation, flags, halo_lo, halo_hi, lft, rgt
    )

    g0 = lax.ppermute(ehi, "grp", [(i, i + 1) for i in range(n_grp - 2)])
    g1 = lax.ppermute(elo, "grp", [(i + 1, i) for i in range(n_grp - 2)])
    near = lax.ppermute(jnp.where(even, chi, clo), "blk", [(i, i ^ 1) for i in range(n_blk)])
    far = lax.ppermute(
        jnp.where(even, clo, chi),
        "blk",
        [(i, (i + 1) % n_blk if i % 2 else (i - 1) % n_blk) for i in range(n_blk)],
    )
    gl = jnp.where(even, far, near)
    gr = jnp.where(even, near, far)
    low_w = 0.5 * (courant + diffusion)
    side_w = 0.5 * diffusion
    return fix_edges(out, g0, g1, gl, gr, low_w, side_w)


def solution(mesh):
    in_specs = (
        P(None, "grp", "blk"),
        P("grp", "blk"),
        P(),
        P(),
        P(None, "blk"),
        P(None, "blk"),
        P(None, "blk"),
        P(None, "blk"),
    )
    out_specs = P(None, "grp", "blk")
    return jax.shard_map(shards, mesh=mesh, in_specs=in_specs, out_specs=out_specs, check_vma=False)
```

```python
import functools

import jax
import jax.numpy as jnp
from jax import lax
from jax.experimental import pallas as pl
from jax.experimental.pallas import tpu as pltpu
from jax.sharding import PartitionSpec as P

courant = 0.5
diffusion = 0.1
source_step = 0.5

SUB = 8
LANE = 128


def tile_t(row):
    n = row.shape[1]
    return jnp.transpose(jnp.broadcast_to(row, (n, n)))


def step_kernel(nf, rows, lanes, mix_s, act_s, flag_s, f_hbm, rate_ref, hlo_ref, hhi_ref,
                lft_ref, rgt_ref, out_hbm, elo_ref, ehi_ref, clo_ref, chi_ref, ext1, ext2, coef, obuf,
                sem):
    n_i = rows // SUB
    n_j = lanes // LANE
    top = SUB + rows
    right = LANE + lanes
    at_exit = flag_s[0] > 0.5
    at_turb = flag_s[1] > 0.5
    at_end = flag_s[0] + flag_s[1] > 0.5

    copy = pltpu.make_async_copy(f_hbm, ext1.at[:, SUB:top, LANE:right], sem.at[0])
    copy.start()
    zeros = jnp.zeros((rows, LANE), jnp.float32)
    for f in range(nf):
        low = hlo_ref[f:f + 1, :]
        ext1[f, SUB - 1:SUB, LANE:right] = low
        ext2[f, SUB - 1:SUB, LANE:right] = jnp.where(at_turb, low, 0.0)
        ext1[f, SUB:top, 0:LANE] = tile_t(lft_ref[f:f + 1, :])
        ext1[f, SUB:top, right:right + LANE] = tile_t(rgt_ref[f:f + 1, :])
        ext2[f, SUB:top, 0:LANE] = zeros
        ext2[f, SUB:top, right:right + LANE] = zeros
    for f in range(nf):
        for g in range(nf):
            coef[f * nf + g] = jnp.full((SUB, LANE), source_step * mix_s[f, g], jnp.float32)
        coef[nf * nf + f] = jnp.full((SUB, LANE), -act_s[f], jnp.float32)
    copy.wait()

    def high_ghost(ext, outside):
        for f in range(nf):
            own = ext[f, top - 1:top, LANE:right]
            halo = hhi_ref[f:f + 1, :]
            if f == 4:
                row = jnp.where(at_turb, own, jnp.where(at_exit | outside, halo, 0.0))
            else:
                row = jnp.where(at_end, own, jnp.where(outside, halo, 0.0))
            ext[f, top:top + 1, LANE:right] = row

    high_ghost(ext1, True)

    sub_id = lax.broadcasted_iota(jnp.int32, (SUB, LANE), 0)
    lane_id = lax.broadcasted_iota(jnp.int32, (SUB, LANE), 1)
    first_sub = sub_id == 0
    last_sub = sub_id == SUB - 1
    first_lane = lane_id == 0
    last_lane = lane_id == LANE - 1

    def tendency_tiles(src, r0, c0s, rate_ts):
        r = pl.multiple_of(r0 + SUB, SUB)
        r_up = pl.multiple_of(r0, SUB)
        r_dn = pl.multiple_of(r0 + 2 * SUB, SUB)
        cs = [pl.multiple_of(c0 + LANE, LANE) for c0 in c0s]
        reacts = []
        for c, rate_t in zip(cs, rate_ts):
            v4 = src[4, pl.ds(r, SUB), pl.ds(c, LANE)]
            heat = 1.0 + (jnp.maximum(v4, 0.0) + jnp.log1p(jnp.exp(-jnp.abs(v4))))
            inv_heat = 1.0 / heat
            reacts.append([
                rate_t * src[f, pl.ds(r, SUB), pl.ds(c, LANE)] * jnp.exp(coef[nf * nf + f] * inv_heat)
                for f in range(nf)
            ])
        tends = [[] for _ in cs]
        for f in range(nf):
            accs = [None] * len(cs)
            for g in range(nf):
                m = coef[f * nf + g]
                for h in range(len(cs)):
                    term = m * reacts[h][g]
                    accs[h] = term if accs[h] is None else accs[h] + term
            for h, c in enumerate(cs):
                c_w = pl.multiple_of(c - LANE, LANE)
                c_e = pl.multiple_of(c + LANE, LANE)
                v = src[f, pl.ds(r, SUB), pl.ds(c, LANE)]
                up = src[f, pl.ds(r_up, SUB), pl.ds(c, LANE)]
                down = src[f, pl.ds(r_dn, SUB), pl.ds(c, LANE)]
                west = src[f, pl.ds(r, SUB), pl.ds(c_w, LANE)]
                east = src[f, pl.ds(r, SUB), pl.ds(c_e, LANE)]
                backward = jnp.where(first_sub, pltpu.roll(up, 1, 0), pltpu.roll(v, 1, 0))
                forward = jnp.where(last_sub, pltpu.roll(down, SUB - 1, 0), pltpu.roll(v, SUB - 1, 0))
                left = jnp.where(first_lane, pltpu.roll(west, 1, 1), pltpu.roll(v, 1, 1))
                rgt = jnp.where(last_lane, pltpu.roll(east, LANE - 1, 1), pltpu.roll(v, LANE - 1, 1))
                flow = (courant + diffusion) * backward + diffusion * (forward + left + rgt)
                flow = flow - (courant + 4.0 * diffusion) * v
                tends[h].append((v, flow + accs[h]))
        return tends

    pair = 4 if n_j % 4 == 0 else (2 if n_j % 2 == 0 else 1)
    n_jp = n_j // pair

    def tile_offsets(t):
        i = t // n_jp
        jp = t % n_jp
        r0 = pl.multiple_of(i * SUB, SUB)
        c0s = [pl.multiple_of((jp * pair + h) * LANE, LANE) for h in range(pair)]
        return r0, c0s

    def stage_one(t, carry):
        r0, c0s = tile_offsets(t)
        rate_ts = [rate_ref[pl.ds(r0, SUB), pl.ds(c0, LANE)] for c0 in c0s]
        tends = tendency_tiles(ext1, r0, c0s, rate_ts)
        r = pl.multiple_of(r0 + SUB, SUB)
        for c0, tend in zip(c0s, tends):
            c = pl.multiple_of(c0 + LANE, LANE)
            for f in range(nf):
                v, tf = tend[f]
                ext2[f, pl.ds(r, SUB), pl.ds(c, LANE)] = v + tf
        return carry

    lax.fori_loop(0, n_i * n_jp, stage_one, 0)

    high_ghost(ext2, False)

    def stage_two(i, carry):
        for jp in range(n_jp):
            r0, c0s = tile_offsets(i * n_jp + jp)
            rate_ts = [rate_ref[pl.ds(r0, SUB), pl.ds(c0, LANE)] for c0 in c0s]
            tends = tendency_tiles(ext2, r0, c0s, rate_ts)
            r = pl.multiple_of(r0 + SUB, SUB)
            for c0, tend in zip(c0s, tends):
                c = pl.multiple_of(c0 + LANE, LANE)
                for f in range(nf):
                    v, tf = tend[f]
                    base = ext1[f, pl.ds(r, SUB), pl.ds(c, LANE)]
                    obuf[f, pl.ds(r0, SUB), pl.ds(c0, LANE)] = 0.5 * (base + v + tf)
        r0 = pl.multiple_of(i * SUB, SUB)
        pltpu.make_async_copy(
            obuf.at[:, pl.ds(r0, SUB), :], out_hbm.at[:, pl.ds(r0, SUB), :], sem.at[1]
        ).start()
        return carry

    lax.fori_loop(0, n_i, stage_two, 0)

    for f in range(nf):
        elo_ref[f:f + 1, :] = ext2[f, SUB:SUB + 1, LANE:right]
        ehi_ref[f:f + 1, :] = ext2[f, top - 1:top, LANE:right]
        west = jnp.transpose(ext2[f, SUB:top, LANE:2 * LANE])
        east = jnp.transpose(ext2[f, SUB:top, right - LANE:right])
        clo_ref[f:f + 1, :] = west[0:1, :]
        chi_ref[f:f + 1, :] = east[LANE - 1:LANE, :]
    pltpu.make_async_copy(obuf, out_hbm, sem.at[1]).wait()


def fused_step(fields, rate, mix, act, flags, halo_lo, halo_hi, lft, rgt):
    nf, rows, lanes = fields.shape
    vmem = pltpu.VMEM
    smem = pl.BlockSpec(memory_space=pltpu.SMEM)
    vspec = pl.BlockSpec(memory_space=vmem)
    cells = rows * lanes
    cost = pl.CostEstimate(
        flops=2 * cells * nf * (2 * nf + 24),
        transcendentals=2 * cells * (nf + 3),
        bytes_accessed=4 * cells * (2 * nf + 1),
    )
    return pl.pallas_call(
        functools.partial(step_kernel, nf, rows, lanes),
        out_shape=(
            jax.ShapeDtypeStruct((nf, rows, lanes), jnp.float32),
            jax.ShapeDtypeStruct((nf, lanes), jnp.float32),
            jax.ShapeDtypeStruct((nf, lanes), jnp.float32),
            jax.ShapeDtypeStruct((nf, rows), jnp.float32),
            jax.ShapeDtypeStruct((nf, rows), jnp.float32),
        ),
        in_specs=[smem, smem, smem, pl.BlockSpec(memory_space=pl.ANY)] + [vspec] * 5,
        out_specs=(pl.BlockSpec(memory_space=pl.ANY),) + (vspec,) * 4,
        scratch_shapes=[
            vmem((nf, rows + 2 * SUB, lanes + 2 * LANE), jnp.float32),
            vmem((nf, rows + 2 * SUB, lanes + 2 * LANE), jnp.float32),
            vmem((nf * nf + nf, SUB, LANE), jnp.float32),
            vmem((nf, rows, lanes), jnp.float32),
            pltpu.SemaphoreType.DMA((2,)),
        ],
        compiler_params=pltpu.CompilerParams(vmem_limit_bytes=60 * 1024 * 1024),
        cost_estimate=cost,
    )(mix, act, flags, fields, rate, halo_lo, halo_hi, lft, rgt)


def interp_kernel(ks, flag_s, ids_s, wt_ref, table_ref, *refs):
    n_in = (len(refs) - 2) // 2
    ins, outs, acc, picked = refs[:n_in], refs[n_in:2 * n_in], refs[-2], refs[-1]
    up_ref, down_ref = outs[0], outs[1]
    lanes = outs[0].shape[1]
    width = table_ref.shape[1]
    acc[...] = jnp.zeros(acc.shape, jnp.float32)

    @pl.when(flag_s[0] + flag_s[1] > 0.5)
    def _():
        def group(pg, carry):
            p0 = pl.multiple_of(pg * SUB, SUB)
            for s in range(SUB):
                for k in range(ks):
                    q = ids_s[k, p0 + s]
                    picked[k, pl.ds(p0 + s, 1), :] = table_ref[pl.ds(q, 1), :]
            return carry

        lax.fori_loop(0, lanes // SUB, group, 0)
        total = wt_ref[:, 0:1] * picked[0]
        for k in range(1, ks):
            total = total + wt_ref[:, k:k + 1] * picked[k]
        acc[:, 0:width] = total

    picked_t = jnp.transpose(acc[...])
    nf = up_ref.shape[0]
    last_ref, first_ref = ins[0], ins[1]
    up_ref[...] = jnp.where(flag_s[0] > 0.5, picked_t[0:nf, :], last_ref[...])
    down_ref[...] = jnp.where(
        flag_s[1] > 0.5, jnp.broadcast_to(picked_t[nf:nf + 1, :], (nf, lanes)), first_ref[...]
    )
    for src, dst in zip(ins[2:], outs[2:]):
        dst[...] = src[...]


def interpolate(flags, ids, wt, table, passed):
    ks, lanes = ids.shape
    smem = pl.BlockSpec(memory_space=pltpu.SMEM)
    vspec = pl.BlockSpec(memory_space=pltpu.VMEM)
    width = table.shape[1]
    return pl.pallas_call(
        functools.partial(interp_kernel, ks),
        out_shape=tuple(jax.ShapeDtypeStruct(x.shape, x.dtype) for x in passed),
        in_specs=[smem, smem] + [vspec] * (2 + len(passed)),
        out_specs=(vspec,) * len(passed),
        scratch_shapes=[
            pltpu.VMEM((lanes, LANE), jnp.float32),
            pltpu.VMEM((ks, lanes, width), jnp.float32),
        ],
    )(flags, ids, wt, table, *passed)


def fix_kernel(low_w, side_w, out_in, g0_ref, g1_ref, gl_ref, gr_ref, out_ref, rb, cb, sem):
    nf, rows, lanes = out_ref.shape
    mid = rows - 2 * SUB
    wins = [
        (out_ref.at[:, pl.ds(0, SUB), :], rb.at[0]),
        (out_ref.at[:, pl.ds(rows - SUB, SUB), :], rb.at[1]),
        (out_ref.at[:, pl.ds(SUB, mid), pl.ds(0, LANE)], cb.at[0]),
        (out_ref.at[:, pl.ds(SUB, mid), pl.ds(lanes - LANE, LANE)], cb.at[1]),
    ]
    loads = [pltpu.make_async_copy(hbm, buf, sem.at[s]) for s, (hbm, buf) in enumerate(wins)]
    for c in loads:
        c.start()
    for c in loads:
        c.wait()
    lane_id = lax.broadcasted_iota(jnp.int32, (rows, LANE), 1)
    row_lane = lax.broadcasted_iota(jnp.int32, (SUB, LANE), 1)
    for f in range(nf):
        west = jnp.where(lane_id == 0, side_w * tile_t(gl_ref[f:f + 1, :]), 0.0)
        east = jnp.where(lane_id == LANE - 1, side_w * tile_t(gr_ref[f:f + 1, :]), 0.0)
        cb[0, f] = cb[0, f] + west[SUB:rows - SUB]
        cb[1, f] = cb[1, f] + east[SUB:rows - SUB]
        for s, lo in ((0, 0), (1, rows - SUB)):
            rb[s, f, :, 0:LANE] = rb[s, f, :, 0:LANE] + west[lo:lo + SUB]
            rb[s, f, :, lanes - LANE:lanes] = rb[s, f, :, lanes - LANE:lanes] + east[lo:lo + SUB]
        rb[0, f, 0:1, :] = rb[0, f, 0:1, :] + low_w * g0_ref[f:f + 1, :]
        rb[1, f, SUB - 1:SUB, :] = rb[1, f, SUB - 1:SUB, :] + side_w * g1_ref[f:f + 1, :]
    stores = [pltpu.make_async_copy(buf, hbm, sem.at[s]) for s, (hbm, buf) in enumerate(wins)]
    for c in stores:
        c.start()
    for c in stores:
        c.wait()


def fix_edges(out, g0, g1, gl, gr, low_w, side_w):
    nf, rows, lanes = out.shape
    vspec = pl.BlockSpec(memory_space=pltpu.VMEM)
    anyspec = pl.BlockSpec(memory_space=pl.ANY)
    return pl.pallas_call(
        functools.partial(fix_kernel, low_w, side_w),
        out_shape=jax.ShapeDtypeStruct(out.shape, jnp.float32),
        in_specs=[anyspec, vspec, vspec, vspec, vspec],
        out_specs=anyspec,
        scratch_shapes=[
            pltpu.VMEM((2, nf, SUB, lanes), jnp.float32),
            pltpu.VMEM((2, nf, rows - 2 * SUB, LANE), jnp.float32),
            pltpu.SemaphoreType.DMA((4,)),
        ],
        input_output_aliases={0: 0},
    )(out, g0, g1, gl, gr)


def shards(
    fields, react_rate, mix_matrix, activation, inlet_ids, inlet_weights, outlet_ids, outlet_weights
):
    nf, rows, lanes = fields.shape
    n_grp = lax.axis_size("grp")
    n_blk = lax.axis_size("blk")
    g = lax.axis_index("grp")
    b = lax.axis_index("blk")
    exit_grp = n_grp - 2
    turb_grp = n_grp - 1
    flags = jnp.stack([g == exit_grp, g == turb_grp]).astype(jnp.float32)

    last_row = fields[:, -1, :]
    first_row = fields[:, 0, :]
    payload = jnp.concatenate([last_row, first_row[4:5]], axis=0)
    planes = payload[None]
    spans = []
    span = n_blk // 2
    even = b % 2 == 0
    edges = (last_row, first_row, fields[:, :, lanes - 1], fields[:, :, 0])
    while span >= 1:
        spans.append(span)
        partner = [(i, i ^ span) for i in range(n_blk)]
        if span == 1:
            edges, planes = lax.optimization_barrier((edges, planes))
            side = jnp.where(even, edges[2], edges[3])
            side = jnp.pad(side, ((0, 1), (0, lanes - side.shape[1])))[None]
            got = lax.ppermute(jnp.concatenate([planes, side], axis=0), "blk", partner)
            side_got = got[-1, :nf, :edges[2].shape[1]]
            planes = jnp.concatenate([planes, got[:-1]], axis=0)
        else:
            planes = jnp.concatenate([planes, lax.ppermute(planes, "blk", partner)], axis=0)
        span //= 2
    table = jnp.transpose(planes, (0, 2, 1)).reshape(n_blk * lanes, nf + 1)
    at_exit = g == exit_grp
    ids = jnp.where(at_exit, inlet_ids, outlet_ids)
    m = jnp.bitwise_xor(ids // lanes, b)
    slot = jnp.zeros_like(m)
    for r, span in enumerate(spans):
        slot = slot + ((m // span) % 2) * (1 << r)
    ids = slot * lanes + ids % lanes
    wt = jnp.transpose(jnp.where(at_exit, inlet_weights, outlet_weights))
    other = lax.ppermute(
        jnp.where(even, edges[3], edges[2]),
        "blk",
        [(i, (i + 1) % n_blk if i % 2 else (i - 1) % n_blk) for i in range(n_blk)],
    )
    lft = jnp.where(even, other, side_got)
    rgt = jnp.where(even, side_got, other)

    up, down = interpolate(flags, ids, wt, table, (edges[0], edges[1]))
    halo_lo = lax.ppermute(up, "grp", [(i, i + 1) for i in range(n_grp - 1)])
    halo_hi = lax.ppermute(down, "grp", [(i + 1, i) for i in range(n_grp - 1)])

    out, elo, ehi, clo, chi = fused_step(
        fields, react_rate, mix_matrix, activation, flags, halo_lo, halo_hi, lft, rgt
    )

    g0 = lax.ppermute(ehi, "grp", [(i, i + 1) for i in range(n_grp - 2)])
    g1 = lax.ppermute(elo, "grp", [(i + 1, i) for i in range(n_grp - 2)])
    gl = lax.ppermute(chi, "blk", [(i, (i + 1) % n_blk) for i in range(n_blk)])
    gr = lax.ppermute(clo, "blk", [((i + 1) % n_blk, i) for i in range(n_blk)])
    low_w = 0.5 * (courant + diffusion)
    side_w = 0.5 * diffusion
    return fix_edges(out, g0, g1, gl, gr, low_w, side_w)


def solution(mesh):
    in_specs = (
        P(None, "grp", "blk"),
        P("grp", "blk"),
        P(),
        P(),
        P(None, "blk"),
        P(None, "blk"),
        P(None, "blk"),
        P(None, "blk"),
    )
    out_specs = P(None, "grp", "blk")
    return jax.shard_map(shards, mesh=mesh, in_specs=in_specs, out_specs=out_specs, check_vma=False)
```

```python
import functools

import jax
import jax.numpy as jnp
from jax import lax
from jax.experimental import pallas as pl
from jax.experimental.pallas import tpu as pltpu
from jax.sharding import PartitionSpec as P

courant = 0.5
diffusion = 0.1
source_step = 0.5

SUB = 8
LANE = 128


def tile_t(row):
    n = row.shape[1]
    return jnp.transpose(jnp.broadcast_to(row, (n, n)))


def step_kernel(nf, rows, lanes, mix_s, act_s, flag_s, f_hbm, rate_ref, hlo_ref, hhi_ref,
                lft_ref, rgt_ref, out_hbm, elo_ref, ehi_ref, clo_ref, chi_ref, ext1, ext2, coef, obuf,
                sem):
    n_i = rows // SUB
    n_j = lanes // LANE
    top = SUB + rows
    right = LANE + lanes
    at_exit = flag_s[0] > 0.5
    at_turb = flag_s[1] > 0.5
    at_end = flag_s[0] + flag_s[1] > 0.5
    even = flag_s[2] > 0.5

    copy = pltpu.make_async_copy(f_hbm, ext1.at[:, SUB:top, LANE:right], sem.at[0])
    copy.start()
    zeros = jnp.zeros((rows, LANE), jnp.float32)
    for f in range(nf):
        low = hlo_ref[f:f + 1, :]
        ext1[f, SUB - 1:SUB, LANE:right] = low
        ext2[f, SUB - 1:SUB, LANE:right] = jnp.where(at_turb, low, 0.0)
        near, far = lft_ref[f:f + 1, :], rgt_ref[f:f + 1, :]
        ext1[f, SUB:top, 0:LANE] = tile_t(jnp.where(even, far, near))
        ext1[f, SUB:top, right:right + LANE] = tile_t(jnp.where(even, near, far))
        ext2[f, SUB:top, 0:LANE] = zeros
        ext2[f, SUB:top, right:right + LANE] = zeros
    for f in range(nf):
        for g in range(nf):
            coef[f * nf + g] = jnp.full((SUB, LANE), source_step * mix_s[f, g], jnp.float32)
        coef[nf * nf + f] = jnp.full((SUB, LANE), -act_s[f], jnp.float32)
    copy.wait()

    def high_ghost(ext, outside):
        for f in range(nf):
            own = ext[f, top - 1:top, LANE:right]
            halo = hhi_ref[f:f + 1, :]
            if f == 4:
                row = jnp.where(at_turb, own, jnp.where(at_exit | outside, halo, 0.0))
            else:
                row = jnp.where(at_end, own, jnp.where(outside, halo, 0.0))
            ext[f, top:top + 1, LANE:right] = row

    high_ghost(ext1, True)

    sub_id = lax.broadcasted_iota(jnp.int32, (SUB, LANE), 0)
    lane_id = lax.broadcasted_iota(jnp.int32, (SUB, LANE), 1)
    first_sub = sub_id == 0
    last_sub = sub_id == SUB - 1
    first_lane = lane_id == 0
    last_lane = lane_id == LANE - 1

    def tendency_tiles(src, r0, c0s, rate_ts):
        r = pl.multiple_of(r0 + SUB, SUB)
        r_up = pl.multiple_of(r0, SUB)
        r_dn = pl.multiple_of(r0 + 2 * SUB, SUB)
        cs = [pl.multiple_of(c0 + LANE, LANE) for c0 in c0s]
        reacts = []
        for c, rate_t in zip(cs, rate_ts):
            v4 = src[4, pl.ds(r, SUB), pl.ds(c, LANE)]
            heat = 1.0 + (jnp.maximum(v4, 0.0) + jnp.log1p(jnp.exp(-jnp.abs(v4))))
            inv_heat = 1.0 / heat
            reacts.append([
                rate_t * src[f, pl.ds(r, SUB), pl.ds(c, LANE)] * jnp.exp(coef[nf * nf + f] * inv_heat)
                for f in range(nf)
            ])
        tends = [[] for _ in cs]
        for f in range(nf):
            accs = [None] * len(cs)
            for g in range(nf):
                m = coef[f * nf + g]
                for h in range(len(cs)):
                    term = m * reacts[h][g]
                    accs[h] = term if accs[h] is None else accs[h] + term
            for h, c in enumerate(cs):
                c_w = pl.multiple_of(c - LANE, LANE)
                c_e = pl.multiple_of(c + LANE, LANE)
                v = src[f, pl.ds(r, SUB), pl.ds(c, LANE)]
                up = src[f, pl.ds(r_up, SUB), pl.ds(c, LANE)]
                down = src[f, pl.ds(r_dn, SUB), pl.ds(c, LANE)]
                west = src[f, pl.ds(r, SUB), pl.ds(c_w, LANE)]
                east = src[f, pl.ds(r, SUB), pl.ds(c_e, LANE)]
                backward = jnp.where(first_sub, pltpu.roll(up, 1, 0), pltpu.roll(v, 1, 0))
                forward = jnp.where(last_sub, pltpu.roll(down, SUB - 1, 0), pltpu.roll(v, SUB - 1, 0))
                left = jnp.where(first_lane, pltpu.roll(west, 1, 1), pltpu.roll(v, 1, 1))
                rgt = jnp.where(last_lane, pltpu.roll(east, LANE - 1, 1), pltpu.roll(v, LANE - 1, 1))
                flow = (courant + diffusion) * backward + diffusion * (forward + left + rgt)
                flow = flow - (courant + 4.0 * diffusion) * v
                tends[h].append((v, flow + accs[h]))
        return tends

    pair = 4 if n_j % 4 == 0 else (2 if n_j % 2 == 0 else 1)
    n_jp = n_j // pair

    def tile_offsets(t):
        i = t // n_jp
        jp = t % n_jp
        r0 = pl.multiple_of(i * SUB, SUB)
        c0s = [pl.multiple_of((jp * pair + h) * LANE, LANE) for h in range(pair)]
        return r0, c0s

    def stage_one(t, carry):
        r0, c0s = tile_offsets(t)
        rate_ts = [rate_ref[pl.ds(r0, SUB), pl.ds(c0, LANE)] for c0 in c0s]
        tends = tendency_tiles(ext1, r0, c0s, rate_ts)
        r = pl.multiple_of(r0 + SUB, SUB)
        for c0, tend in zip(c0s, tends):
            c = pl.multiple_of(c0 + LANE, LANE)
            for f in range(nf):
                v, tf = tend[f]
                ext2[f, pl.ds(r, SUB), pl.ds(c, LANE)] = v + tf
        return carry

    lax.fori_loop(0, n_i * n_jp, stage_one, 0)

    high_ghost(ext2, False)

    def stage_two(i, carry):
        for jp in range(n_jp):
            r0, c0s = tile_offsets(i * n_jp + jp)
            rate_ts = [rate_ref[pl.ds(r0, SUB), pl.ds(c0, LANE)] for c0 in c0s]
            tends = tendency_tiles(ext2, r0, c0s, rate_ts)
            r = pl.multiple_of(r0 + SUB, SUB)
            for c0, tend in zip(c0s, tends):
                c = pl.multiple_of(c0 + LANE, LANE)
                for f in range(nf):
                    v, tf = tend[f]
                    base = ext1[f, pl.ds(r, SUB), pl.ds(c, LANE)]
                    obuf[f, pl.ds(r0, SUB), pl.ds(c0, LANE)] = 0.5 * (base + v + tf)
        r0 = pl.multiple_of(i * SUB, SUB)
        pltpu.make_async_copy(
            obuf.at[:, pl.ds(r0, SUB), :], out_hbm.at[:, pl.ds(r0, SUB), :], sem.at[1]
        ).start()
        return carry

    lax.fori_loop(0, n_i, stage_two, 0)

    for f in range(nf):
        elo_ref[f:f + 1, :] = ext2[f, SUB:SUB + 1, LANE:right]
        ehi_ref[f:f + 1, :] = ext2[f, top - 1:top, LANE:right]
        west = jnp.transpose(ext2[f, SUB:top, LANE:2 * LANE])
        east = jnp.transpose(ext2[f, SUB:top, right - LANE:right])
        clo_ref[f:f + 1, :] = west[0:1, :]
        chi_ref[f:f + 1, :] = east[LANE - 1:LANE, :]
    pltpu.make_async_copy(obuf, out_hbm, sem.at[1]).wait()


def fused_step(fields, rate, mix, act, flags, halo_lo, halo_hi, lft, rgt):
    nf, rows, lanes = fields.shape
    vmem = pltpu.VMEM
    smem = pl.BlockSpec(memory_space=pltpu.SMEM)
    vspec = pl.BlockSpec(memory_space=vmem)
    cells = rows * lanes
    cost = pl.CostEstimate(
        flops=2 * cells * nf * (2 * nf + 24),
        transcendentals=2 * cells * (nf + 3),
        bytes_accessed=4 * cells * (2 * nf + 1),
    )
    return pl.pallas_call(
        functools.partial(step_kernel, nf, rows, lanes),
        out_shape=(
            jax.ShapeDtypeStruct((nf, rows, lanes), jnp.float32),
            jax.ShapeDtypeStruct((nf, lanes), jnp.float32),
            jax.ShapeDtypeStruct((nf, lanes), jnp.float32),
            jax.ShapeDtypeStruct((nf, rows), jnp.float32),
            jax.ShapeDtypeStruct((nf, rows), jnp.float32),
        ),
        in_specs=[smem, smem, smem, pl.BlockSpec(memory_space=pl.ANY)] + [vspec] * 5,
        out_specs=(pl.BlockSpec(memory_space=pl.ANY),) + (vspec,) * 4,
        scratch_shapes=[
            vmem((nf, rows + 2 * SUB, lanes + 2 * LANE), jnp.float32),
            vmem((nf, rows + 2 * SUB, lanes + 2 * LANE), jnp.float32),
            vmem((nf * nf + nf, SUB, LANE), jnp.float32),
            vmem((nf, rows, lanes), jnp.float32),
            pltpu.SemaphoreType.DMA((2,)),
        ],
        compiler_params=pltpu.CompilerParams(vmem_limit_bytes=60 * 1024 * 1024),
        cost_estimate=cost,
    )(mix, act, flags, fields, rate, halo_lo, halo_hi, lft, rgt)


def interp_kernel(ks, flag_s, ids_s, wt_ref, table_ref, *refs):
    n_in = (len(refs) - 2) // 2
    ins, outs, acc, picked = refs[:n_in], refs[n_in:2 * n_in], refs[-2], refs[-1]
    up_ref, down_ref = outs[0], outs[1]
    lanes = outs[0].shape[1]
    width = table_ref.shape[1]
    acc[...] = jnp.zeros(acc.shape, jnp.float32)

    @pl.when(flag_s[0] + flag_s[1] > 0.5)
    def _():
        def group(pg, carry):
            p0 = pl.multiple_of(pg * SUB, SUB)
            for s in range(SUB):
                for k in range(ks):
                    q = ids_s[k, p0 + s]
                    picked[k, pl.ds(p0 + s, 1), :] = table_ref[pl.ds(q, 1), :]
            return carry

        lax.fori_loop(0, lanes // SUB, group, 0)
        total = wt_ref[:, 0:1] * picked[0]
        for k in range(1, ks):
            total = total + wt_ref[:, k:k + 1] * picked[k]
        acc[:, 0:width] = total

    picked_t = jnp.transpose(acc[...])
    nf = up_ref.shape[0]
    last_ref, first_ref = ins[0], ins[1]
    up_ref[...] = jnp.where(flag_s[0] > 0.5, picked_t[0:nf, :], last_ref[...])
    down_ref[...] = jnp.where(
        flag_s[1] > 0.5, jnp.broadcast_to(picked_t[nf:nf + 1, :], (nf, lanes)), first_ref[...]
    )
    for src, dst in zip(ins[2:], outs[2:]):
        dst[...] = src[...]


def interpolate(flags, ids, wt, table, passed):
    ks, lanes = ids.shape
    smem = pl.BlockSpec(memory_space=pltpu.SMEM)
    vspec = pl.BlockSpec(memory_space=pltpu.VMEM)
    width = table.shape[1]
    return pl.pallas_call(
        functools.partial(interp_kernel, ks),
        out_shape=tuple(jax.ShapeDtypeStruct(x.shape, x.dtype) for x in passed),
        in_specs=[smem, smem] + [vspec] * (2 + len(passed)),
        out_specs=(vspec,) * len(passed),
        scratch_shapes=[
            pltpu.VMEM((lanes, LANE), jnp.float32),
            pltpu.VMEM((ks, lanes, width), jnp.float32),
        ],
    )(flags, ids, wt, table, *passed)


def fix_kernel(low_w, side_w, out_in, g0_ref, g1_ref, gl_ref, gr_ref, out_ref, rb, cb, sem):
    nf, rows, lanes = out_ref.shape
    mid = rows - 2 * SUB
    wins = [
        (out_ref.at[:, pl.ds(0, SUB), :], rb.at[0]),
        (out_ref.at[:, pl.ds(rows - SUB, SUB), :], rb.at[1]),
        (out_ref.at[:, pl.ds(SUB, mid), pl.ds(0, LANE)], cb.at[0]),
        (out_ref.at[:, pl.ds(SUB, mid), pl.ds(lanes - LANE, LANE)], cb.at[1]),
    ]
    loads = [pltpu.make_async_copy(hbm, buf, sem.at[s]) for s, (hbm, buf) in enumerate(wins)]
    for c in loads:
        c.start()
    for c in loads:
        c.wait()
    lane_id = lax.broadcasted_iota(jnp.int32, (rows, LANE), 1)
    row_lane = lax.broadcasted_iota(jnp.int32, (SUB, LANE), 1)
    for f in range(nf):
        west = jnp.where(lane_id == 0, side_w * tile_t(gl_ref[f:f + 1, :]), 0.0)
        east = jnp.where(lane_id == LANE - 1, side_w * tile_t(gr_ref[f:f + 1, :]), 0.0)
        cb[0, f] = cb[0, f] + west[SUB:rows - SUB]
        cb[1, f] = cb[1, f] + east[SUB:rows - SUB]
        for s, lo in ((0, 0), (1, rows - SUB)):
            rb[s, f, :, 0:LANE] = rb[s, f, :, 0:LANE] + west[lo:lo + SUB]
            rb[s, f, :, lanes - LANE:lanes] = rb[s, f, :, lanes - LANE:lanes] + east[lo:lo + SUB]
        rb[0, f, 0:1, :] = rb[0, f, 0:1, :] + low_w * g0_ref[f:f + 1, :]
        rb[1, f, SUB - 1:SUB, :] = rb[1, f, SUB - 1:SUB, :] + side_w * g1_ref[f:f + 1, :]
    stores = [pltpu.make_async_copy(buf, hbm, sem.at[s]) for s, (hbm, buf) in enumerate(wins)]
    for c in stores:
        c.start()
    for c in stores:
        c.wait()


def fix_edges(out, g0, g1, gl, gr, low_w, side_w):
    nf, rows, lanes = out.shape
    vspec = pl.BlockSpec(memory_space=pltpu.VMEM)
    anyspec = pl.BlockSpec(memory_space=pl.ANY)
    return pl.pallas_call(
        functools.partial(fix_kernel, low_w, side_w),
        out_shape=jax.ShapeDtypeStruct(out.shape, jnp.float32),
        in_specs=[anyspec, vspec, vspec, vspec, vspec],
        out_specs=anyspec,
        scratch_shapes=[
            pltpu.VMEM((2, nf, SUB, lanes), jnp.float32),
            pltpu.VMEM((2, nf, rows - 2 * SUB, LANE), jnp.float32),
            pltpu.SemaphoreType.DMA((4,)),
        ],
        input_output_aliases={0: 0},
    )(out, g0, g1, gl, gr)


def shards(
    fields, react_rate, mix_matrix, activation, inlet_ids, inlet_weights, outlet_ids, outlet_weights
):
    nf, rows, lanes = fields.shape
    n_grp = lax.axis_size("grp")
    n_blk = lax.axis_size("blk")
    g = lax.axis_index("grp")
    b = lax.axis_index("blk")
    exit_grp = n_grp - 2
    turb_grp = n_grp - 1
    flags = jnp.stack([g == exit_grp, g == turb_grp, b % 2 == 0]).astype(jnp.float32)

    last_row = fields[:, -1, :]
    first_row = fields[:, 0, :]
    payload = jnp.concatenate([last_row, first_row[4:5]], axis=0)
    planes = payload[None]
    spans = []
    span = n_blk // 2
    even = b % 2 == 0
    edges = (last_row, first_row, fields[:, :, lanes - 1], fields[:, :, 0])
    while span >= 1:
        spans.append(span)
        partner = [(i, i ^ span) for i in range(n_blk)]
        if span == 1:
            edges, planes = lax.optimization_barrier((edges, planes))
            side = jnp.where(even, edges[2], edges[3])
            side = jnp.pad(side, ((0, 1), (0, lanes - side.shape[1])))[None]
            got = lax.ppermute(jnp.concatenate([planes, side], axis=0), "blk", partner)
            side_got = got[-1, :nf, :edges[2].shape[1]]
            planes = jnp.concatenate([planes, got[:-1]], axis=0)
        else:
            planes = jnp.concatenate([planes, lax.ppermute(planes, "blk", partner)], axis=0)
        span //= 2
    table = jnp.transpose(planes, (0, 2, 1)).reshape(n_blk * lanes, nf + 1)
    at_exit = g == exit_grp
    ids = jnp.where(at_exit, inlet_ids, outlet_ids)
    m = jnp.bitwise_xor(ids // lanes, b)
    slot = jnp.zeros_like(m)
    for r, span in enumerate(spans):
        slot = slot + ((m // span) % 2) * (1 << r)
    ids = slot * lanes + ids % lanes
    wt = jnp.transpose(jnp.where(at_exit, inlet_weights, outlet_weights))
    other = lax.ppermute(
        jnp.where(even, edges[3], edges[2]),
        "blk",
        [(i, (i + 1) % n_blk if i % 2 else (i - 1) % n_blk) for i in range(n_blk)],
    )
    lft, rgt = side_got, other

    up, down = interpolate(flags, ids, wt, table, (edges[0], edges[1]))
    halo_lo = lax.ppermute(up, "grp", [(i, i + 1) for i in range(n_grp - 1)])
    halo_hi = lax.ppermute(down, "grp", [(i + 1, i) for i in range(n_grp - 1)])

    out, elo, ehi, clo, chi = fused_step(
        fields, react_rate, mix_matrix, activation, flags, halo_lo, halo_hi, lft, rgt
    )

    g0 = lax.ppermute(ehi, "grp", [(i, i + 1) for i in range(n_grp - 2)])
    g1 = lax.ppermute(elo, "grp", [(i + 1, i) for i in range(n_grp - 2)])
    gl = lax.ppermute(chi, "blk", [(i, (i + 1) % n_blk) for i in range(n_blk)])
    gr = lax.ppermute(clo, "blk", [((i + 1) % n_blk, i) for i in range(n_blk)])
    low_w = 0.5 * (courant + diffusion)
    side_w = 0.5 * diffusion
    return fix_edges(out, g0, g1, gl, gr, low_w, side_w)


def solution(mesh):
    in_specs = (
        P(None, "grp", "blk"),
        P("grp", "blk"),
        P(),
        P(),
        P(None, "blk"),
        P(None, "blk"),
        P(None, "blk"),
        P(None, "blk"),
    )
    out_specs = P(None, "grp", "blk")
    return jax.shard_map(shards, mesh=mesh, in_specs=in_specs, out_specs=out_specs, check_vma=False)
```
